128 devices in a mesh: freq: 4 (over y), rcv: 32 (over x, z, core).
Axes of the slice: x: 4, y: 4, z: 4, core: 2. Of those that a mesh axis runs over, the one named last changes fastest.
Arguments:
- up_time: bfloat16 [128, 256, 20480], P(('freq', 'rcv')), may hold values from -74 to 74
- down_blocks: bfloat16 [8, 160, 11, 2, 128, 128], P('freq', 'rcv'), may hold values from -0.09375 to 0.09375
- block_cols: int32 [8, 160, 11], P('freq', 'rcv'), may hold values from 0 to 159, as said below
- block_counts: int32 [8, 160], P('freq', 'rcv'), may hold values from 1 to 11, as said below
Outputs:
- solution: float32 [2, 8, 128, 20480], P(None, 'freq', None, 'rcv')
- normal_residual: float32 [2, 8, 128, 20480], P(None, 'freq', None, 'rcv')
The draws below stay inside these ranges and needn't reach their ends.
Inputs may be any that keep to these rules, and one draw needn't show every extreme that they name: block_cols[f, r, s] is the column block of slot s of row block r at frequency f; it differs from r by at most 5. Row block r of frequency f stores blocks in its first block_counts[f, r] slots.
All inputs are finite; a program needn't handle non-finite values.
Results may differ from the reference program's by a relative error of at most 0.0062.
Values may be sent and summed in bfloat16 or wider, within the bound.
No kernel may reach another device: no remote copies, remote signals or barrier semaphores. Data moves between devices by JAX's collectives and lax.ppermute only.
A program may use at most 192 MiB of HBM per device.

```python
import math
import jax
import jax.numpy as jnp
from jax import lax

NR = 20480
BLK = 128
REACH = 5
NT = 256
ITERS = 2
SLOTS = 11
NB = 160
NV = 128
NF = 8


def draw_up_time(key, part):
    folded = jax.random.fold_in(key, 37)
    key_traces, key_rough, key_shots = jax.random.split(folded, 3)
    receiver = jnp.arange(NR, dtype=jnp.float32)
    receiver_ramp = jnp.sqrt(1.0 + 2.0 * receiver / NR)[None, None, :]
    roughness = jnp.exp(jax.random.uniform(key_rough, (1, 1, NR), jnp.float32, -1.15, 1.15))
    shot_gain = jnp.exp(jax.random.uniform(key_shots, (NV, 1, 1), jnp.float32, -0.8, 0.8))
    traces = jax.random.normal(key_traces, (NV, NT, NR), jnp.float32)
    traces = jnp.clip(traces, -6.0, 6.0)
    return (traces * receiver_ramp * roughness * shot_gain).astype(jnp.bfloat16)


def draw_block_cols(key, part):
    folded = jax.random.fold_in(key, 23)
    scores = jax.random.randint(folded, (NF, NB, SLOTS), 0, 1 << 20) * SLOTS + jnp.arange(SLOTS, dtype=jnp.int32)
    ranking = jnp.argsort(scores, axis=-1).astype(jnp.int32)
    offsets = ranking - REACH
    row_ids = jnp.arange(NB, dtype=jnp.int32)[None, :, None]
    columns = row_ids + offsets
    columns = jnp.where((columns < 0) | (columns >= NB), row_ids - offsets, columns)
    return columns.astype(jnp.int32)


def draw_block_counts(key, part):
    folded = jax.random.fold_in(key, 11)
    key_one, key_two, key_full, key_single = jax.random.split(folded, 4)
    random_one = jax.random.randint(key_one, (NF, NB), 0, SLOTS)
    random_two = jax.random.randint(key_two, (NF, NB), 0, SLOTS)
    divisor = max(1, (SLOTS - 1) // 2)
    counts = jnp.minimum(SLOTS, 1 + random_one * random_two // divisor)
    full_row = jax.random.randint(key_full, (NF, 1), 0, NB)
    single_row = (full_row + 1 + jax.random.randint(key_single, (NF, 1), 0, NB - 1)) % NB
    row_ids = jnp.arange(NB, dtype=jnp.int32)[None, :]
    counts = jnp.where(row_ids == full_row, SLOTS, counts)
    counts = jnp.where(row_ids == single_row, 1, counts)
    return counts.astype(jnp.int32)


def level_of(own_key, shape, cuts, least, high):
    loudness, own = 1.0, jax.random.fold_in(own_key, 6)
    for position, parts in cuts:
        steps = jnp.exp(jax.random.uniform(jax.random.fold_in(own, position), (parts,), jnp.float32, least / len(cuts), high / len(cuts)))
        loudness = loudness * jnp.repeat(steps, shape[position] // parts).reshape([-1 if axis == position else 1 for axis in range(len(shape))])
    return loudness


def scatter_about(own_key, dims, spread, limit, pieces=(), kind=jnp.bfloat16):
    loudness = level_of(own_key, dims, pieces, -0.22, 0.18) if pieces else 1.0
    drawn = jax.random.normal(own_key, dims, jnp.float32) * spread * loudness
    return jnp.minimum(jnp.maximum(drawn, -limit), limit).astype(kind)


def setup_inputs(seed: int = 0) -> dict:
    splits = jax.random.split(jax.random.key(seed), 5)
    up_time = draw_up_time(jax.random.fold_in(splits[4], 71), 0)
    down_blocks = scatter_about(splits[1], (NF, NB, SLOTS, 2, BLK, BLK), (3 * BLK * SLOTS) ** -0.5, 0.09375, ((0, 4), (1, 32)))
    block_cols = draw_block_cols(jax.random.fold_in(splits[4], 71), 0)
    block_counts = draw_block_counts(jax.random.fold_in(splits[4], 71), 0)
    return {"up_time": up_time, "down_blocks": down_blocks, "block_cols": block_cols, "block_counts": block_counts}


EPSILON = 1e-06

def fourier_table(time_steps, freq_groups, local_freqs):
    shape = (time_steps, freq_groups, local_freqs)
    sample = lax.broadcasted_iota(jnp.int32, shape, 0)
    harmonic = lax.broadcasted_iota(jnp.int32, shape, 1) * local_freqs + lax.broadcasted_iota(jnp.int32, shape, 2) + 1
    phase_angle = 2.0 * math.pi / time_steps * (harmonic * sample % time_steps).astype(jnp.float32)
    scale_factor = 1.0 / math.sqrt(time_steps)
    return jnp.stack([jnp.cos(phase_angle) * scale_factor, -jnp.sin(phase_angle) * scale_factor], axis=1).astype(jnp.bfloat16)

def field_norm(field):
    return jnp.sqrt(jnp.sum(field * field) + EPSILON)

def rounded_field(field):
    return lax.optimization_barrier(field.astype(jnp.bfloat16)).astype(jnp.float32).reshape(2, NV, NB, BLK)

def live_mask(counts):
    return (lax.broadcasted_iota(jnp.int32, (NB, SLOTS), 1) < counts[:, None]).astype(jnp.float32)

def forward(field, blocks, columns, counts):
    rounded = rounded_field(field)
    gathered = rounded[:, :, columns, :] * live_mask(counts)[None, None, :, :, None]
    products = jnp.einsum('cvrsj,rseij->cevri', gathered, blocks.astype(jnp.float32))
    real_part = products[0, 0] - products[1, 1]
    imaginary = products[0, 1] + products[1, 0]
    return field + jnp.stack([real_part, imaginary]).reshape(2, NV, NR)

def adjoint(field, blocks, columns, counts):
    rounded = rounded_field(field)
    products = jnp.einsum('cvri,rseij->cevrsj', rounded, blocks.astype(jnp.float32))
    contributions = jnp.stack([products[0, 0] + products[1, 1], products[1, 0] - products[0, 1]])
    contributions = contributions * live_mask(counts)[None, None, :, :, None]
    summed = jnp.zeros((2, NV, NB, BLK), jnp.float32).at[:, :, columns.reshape(-1), :].add(contributions.reshape(2, NV, NB * SLOTS, BLK))
    return field + summed.reshape(2, NV, NR)

def solve_frequency(inputs):
    right_side, blocks, columns, counts = inputs
    beta_norm = field_norm(right_side)
    left_vector = right_side / beta_norm
    residual_right = adjoint(left_vector, blocks, columns, counts)
    alpha_norm = field_norm(residual_right)
    right_vector = residual_right / alpha_norm
    search_direction = right_vector
    solution = jnp.zeros_like(right_side)
    phibar = beta_norm
    rhobar = alpha_norm
    for iteration in range(ITERS):
        residual_left = forward(right_vector, blocks, columns, counts) - alpha_norm * left_vector
        beta_norm = field_norm(residual_left)
        left_vector = residual_left / beta_norm
        residual_right = adjoint(left_vector, blocks, columns, counts) - beta_norm * right_vector
        alpha_norm = field_norm(residual_right)
        right_vector = residual_right / alpha_norm
        rho_value = jnp.sqrt(rhobar * rhobar + beta_norm * beta_norm)
        cosine = rhobar / rho_value
        sine_value = beta_norm / rho_value
        theta_value = sine_value * alpha_norm
        rhobar = -cosine * alpha_norm
        phi_value = cosine * phibar
        phibar = sine_value * phibar
        solution = solution + phi_value / rho_value * search_direction
        search_direction = right_vector - theta_value / rho_value * search_direction
    return (solution, phibar * alpha_norm * cosine * right_vector)

def reference(up_time, down_blocks, block_cols, block_counts):
    transposed = fourier_table(NT, 1, NF).reshape(NT, 2 * NF).T

    def one_shot(shot_trace):
        return jnp.dot(transposed, shot_trace, preferred_element_type=jnp.float32)
    spectra = lax.map(one_shot, up_time)
    spectra = lax.optimization_barrier(spectra.astype(jnp.bfloat16)).astype(jnp.float32)
    right_side = spectra.reshape(NV, 2, NF, NR).transpose(2, 1, 0, 3)
    solutions, residuals = lax.map(solve_frequency, (right_side, down_blocks, block_cols, block_counts))
    return (solutions.transpose(1, 0, 2, 3), residuals.transpose(1, 0, 2, 3))
```

```python
import math

import jax
import jax.numpy as jnp
from jax import lax
from jax.experimental import pallas as pl
from jax.experimental.pallas import tpu as pltpu
from jax.sharding import PartitionSpec as P

ITERS = 2


EPSILON = 1e-06


def with_halo(cells, sides, width):
    for axis, dim in sides:
        count = lax.axis_size(axis)
        ends = count - 1
        head = lax.slice_in_dim(cells, 0, width, axis=dim)
        tail = lax.slice_in_dim(cells, cells.shape[dim] - width, cells.shape[dim], axis=dim)
        cells = jnp.concatenate(
            [
                lax.ppermute(tail, axis, [(i, (i + 1) % count) for i in range(ends)]),
                cells,
                lax.ppermute(head, axis, [((i + 1) % count, i) for i in range(ends)]),
            ],
            axis=dim,
        )
    return cells


def from_behind(value, axis, steps):
    count = lax.axis_size(axis)
    first, last = (max(0, -steps), min(count, count - steps))
    return lax.ppermute(value, axis, [(source, source + steps) for source in range(first, last)])


def fourier_table(time_steps, freq_groups, local_freqs):
    shape = (time_steps, freq_groups, local_freqs)
    sample = lax.broadcasted_iota(jnp.int32, shape, 0)
    harmonic = (
        lax.broadcasted_iota(jnp.int32, shape, 1) * local_freqs
        + lax.broadcasted_iota(jnp.int32, shape, 2)
        + 1
    )
    phase_angle = 2.0 * math.pi / time_steps * (harmonic * sample % time_steps).astype(jnp.float32)
    scale_factor = 1.0 / math.sqrt(time_steps)
    return jnp.stack(
        [jnp.cos(phase_angle) * scale_factor, -jnp.sin(phase_angle) * scale_factor], axis=1
    ).astype(jnp.bfloat16)


def rcv_sum(partial):
    count = lax.axis_size("rcv")
    spread = jnp.broadcast_to(partial[None], (count,) + partial.shape)
    gathered = lax.all_to_all(spread, "rcv", 0, 0, tiled=False)
    return jnp.sum(gathered, axis=0)


def field_norm(field):
    squares = rcv_sum(jnp.sum(field * field, axis=(0, 2, 3)))
    return jnp.sqrt(squares + EPSILON)[None, :, None, None]


def _forward_kernel(cols_ref, counts_ref, x_ref, a_ref, o_ref):
    freq = pl.program_id(0)
    row = pl.program_id(1)
    rows = pl.num_programs(1)
    slots, _, block, _ = a_ref.shape
    sources = o_ref.shape[1]
    index = freq * rows + row
    count = counts_ref[index]
    o_ref[...] = jnp.zeros(o_ref.shape, o_ref.dtype)
    contract = (((1,), (1,)), ((), ()))
    for slot in range(slots):

        @pl.when(slot < count)
        def _():
            start = pl.multiple_of(cols_ref[index * slots + slot] * block, block)
            picked = x_ref[:, :, pl.ds(start, block)].reshape(2 * sources, block)
            by_real = lax.dot_general(
                picked, a_ref[slot, 0], contract, preferred_element_type=jnp.float32
            )
            by_imag = lax.dot_general(
                picked, a_ref[slot, 1], contract, preferred_element_type=jnp.float32
            )
            o_ref[0] += by_real[:sources] - by_imag[sources:]
            o_ref[1] += by_imag[:sources] + by_real[sources:]


def _adjoint_kernel(cols_ref, counts_ref, u_ref, a_ref, o_ref):
    freq = pl.program_id(0)
    row = pl.program_id(1)
    rows = pl.num_programs(1)
    slots, _, block, _ = a_ref.shape
    sources = u_ref.shape[1]
    index = freq * rows + row
    count = counts_ref[index]

    @pl.when(row == 0)
    def _():
        o_ref[...] = jnp.zeros(o_ref.shape, o_ref.dtype)

    field = u_ref[...].reshape(2 * sources, block)
    for slot in range(slots):

        @pl.when(slot < count)
        def _():
            start = pl.multiple_of(cols_ref[index * slots + slot] * block, block)
            by_real = jnp.dot(field, a_ref[slot, 0], preferred_element_type=jnp.float32)
            by_imag = jnp.dot(field, a_ref[slot, 1], preferred_element_type=jnp.float32)
            o_ref[0, :, pl.ds(start, block)] += by_real[:sources] + by_imag[sources:]
            o_ref[1, :, pl.ds(start, block)] += by_real[sources:] - by_imag[:sources]


def apply_forward(extended, down_blocks, cols, counts):
    local_freqs, local_blocks, slot_count, _, block_size, _ = down_blocks.shape
    _, _, sources, span = extended.shape
    grid_spec = pltpu.PrefetchScalarGridSpec(
        num_scalar_prefetch=2,
        grid=(local_freqs, local_blocks),
        in_specs=[
            pl.BlockSpec((2, None, sources, span), lambda f, r, c, n: (0, f, 0, 0)),
            pl.BlockSpec(
                (None, None, slot_count, 2, block_size, block_size),
                lambda f, r, c, n: (f, r, 0, 0, 0, 0),
            ),
        ],
        out_specs=pl.BlockSpec((2, None, sources, block_size), lambda f, r, c, n: (0, f, 0, r)),
    )
    return pl.pallas_call(
        _forward_kernel,
        grid_spec=grid_spec,
        out_shape=jax.ShapeDtypeStruct(
            (2, local_freqs, sources, local_blocks * block_size), jnp.float32
        ),
        compiler_params=pltpu.CompilerParams(dimension_semantics=("arbitrary", "arbitrary")),
    )(cols, counts, extended, down_blocks)


def apply_adjoint(rounded, down_blocks, cols, counts, span):
    local_freqs, local_blocks, slot_count, _, block_size, _ = down_blocks.shape
    sources = rounded.shape[2]
    grid_spec = pltpu.PrefetchScalarGridSpec(
        num_scalar_prefetch=2,
        grid=(local_freqs, local_blocks),
        in_specs=[
            pl.BlockSpec((2, None, sources, block_size), lambda f, r, c, n: (0, f, 0, r)),
            pl.BlockSpec(
                (None, None, slot_count, 2, block_size, block_size),
                lambda f, r, c, n: (f, r, 0, 0, 0, 0),
            ),
        ],
        out_specs=pl.BlockSpec((2, None, sources, span), lambda f, r, c, n: (0, f, 0, 0)),
    )
    return pl.pallas_call(
        _adjoint_kernel,
        grid_spec=grid_spec,
        out_shape=jax.ShapeDtypeStruct((2, local_freqs, sources, span), jnp.float32),
        compiler_params=pltpu.CompilerParams(dimension_semantics=("arbitrary", "arbitrary")),
    )(cols, counts, rounded, down_blocks)


def body(up_time, down_blocks, block_cols, block_counts):
    freq_groups = lax.axis_size("freq")
    receiver_groups = lax.axis_size("rcv")
    shot_count, time_steps, receivers = up_time.shape
    local_freqs, local_blocks, slot_count, _, block_size, _ = down_blocks.shape
    local_rows = receivers // receiver_groups
    reach_blocks = (slot_count - 1) // 2
    rim_rows = reach_blocks * block_size
    span_blocks = local_blocks + 2 * reach_blocks
    fourier = fourier_table(time_steps, freq_groups, local_freqs)
    spectrum = jnp.einsum(
        "snr,ncgf->cfsgr", up_time, fourier, preferred_element_type=jnp.float32
    ).astype(jnp.bfloat16)
    spectrum = spectrum.reshape(
        2, local_freqs, shot_count, freq_groups * receiver_groups, local_rows
    )
    received = lax.all_to_all(spectrum, ("freq", "rcv"), split_axis=3, concat_axis=2, tiled=True)
    right_side = received.reshape(2, local_freqs, -1, local_rows).astype(jnp.float32)
    position = lax.axis_index("rcv")
    columns = jnp.clip(
        block_cols - position * local_blocks + reach_blocks, 0, span_blocks - 1
    ).reshape(-1)
    counts = jnp.clip(block_counts, 0, slot_count).reshape(-1)

    def adjoint(field):
        rounded = field.astype(jnp.bfloat16)
        spread = apply_adjoint(rounded, down_blocks, columns, counts, span_blocks * block_size)
        lower_rim = spread[..., :rim_rows]
        middle = spread[..., rim_rows : rim_rows + local_rows]
        upper_rim = spread[..., rim_rows + local_rows :]
        from_above = from_behind(lower_rim, "rcv", -1)
        from_below = from_behind(upper_rim, "rcv", 1)
        middle = middle.at[..., :rim_rows].add(from_below)
        middle = middle.at[..., local_rows - rim_rows :].add(from_above)
        return field + middle

    def forward(field):
        extended = with_halo(field.astype(jnp.bfloat16), (("rcv", 3),), rim_rows)
        return field + apply_forward(extended, down_blocks, columns, counts)

    beta_norm = field_norm(right_side)
    left_vector = right_side / beta_norm
    residual_right = adjoint(left_vector)
    alpha_norm = field_norm(residual_right)
    right_vector = residual_right / alpha_norm
    search_direction = right_vector
    solution = jnp.zeros_like(right_side)
    phibar = beta_norm
    rhobar = alpha_norm
    for iteration in range(ITERS):
        residual_left = forward(right_vector) - alpha_norm * left_vector
        beta_norm = field_norm(residual_left)
        left_vector = residual_left / beta_norm
        residual_right = adjoint(left_vector) - beta_norm * right_vector
        alpha_norm = field_norm(residual_right)
        right_vector = residual_right / alpha_norm
        rho_value = jnp.sqrt(rhobar * rhobar + beta_norm * beta_norm)
        cosine = rhobar / rho_value
        sine_value = beta_norm / rho_value
        theta_value = sine_value * alpha_norm
        rhobar = -cosine * alpha_norm
        phi_value = cosine * phibar
        phibar = sine_value * phibar
        solution = solution + phi_value / rho_value * search_direction
        search_direction = right_vector - theta_value / rho_value * search_direction
    return (solution, phibar * alpha_norm * cosine * right_vector)


def solution(mesh):
    return jax.shard_map(
        body,
        mesh=mesh,
        in_specs=(
            P(("freq", "rcv"), None, None),
            P("freq", "rcv", None, None, None, None),
            P("freq", "rcv", None),
            P("freq", "rcv"),
        ),
        out_specs=(P(None, "freq", None, "rcv"), P(None, "freq", None, "rcv")),
        check_vma=False,
    )
```

```python
import math

import jax
import jax.numpy as jnp
from jax import lax
from jax.experimental import pallas as pl
from jax.experimental.pallas import tpu as pltpu
from jax.sharding import PartitionSpec as P

ITERS = 2


EPSILON = 1e-06


def with_halo(cells, sides, width):
    for axis, dim in sides:
        count = lax.axis_size(axis)
        ends = count - 1
        head = lax.slice_in_dim(cells, 0, width, axis=dim)
        tail = lax.slice_in_dim(cells, cells.shape[dim] - width, cells.shape[dim], axis=dim)
        cells = jnp.concatenate(
            [
                lax.ppermute(tail, axis, [(i, (i + 1) % count) for i in range(ends)]),
                cells,
                lax.ppermute(head, axis, [((i + 1) % count, i) for i in range(ends)]),
            ],
            axis=dim,
        )
    return cells


def from_behind(value, axis, steps):
    count = lax.axis_size(axis)
    first, last = (max(0, -steps), min(count, count - steps))
    return lax.ppermute(value, axis, [(source, source + steps) for source in range(first, last)])


def fourier_table(time_steps, freq_groups, local_freqs):
    shape = (time_steps, freq_groups, local_freqs)
    sample = lax.broadcasted_iota(jnp.int32, shape, 0)
    harmonic = (
        lax.broadcasted_iota(jnp.int32, shape, 1) * local_freqs
        + lax.broadcasted_iota(jnp.int32, shape, 2)
        + 1
    )
    phase_angle = 2.0 * math.pi / time_steps * (harmonic * sample % time_steps).astype(jnp.float32)
    scale_factor = 1.0 / math.sqrt(time_steps)
    return jnp.stack(
        [jnp.cos(phase_angle) * scale_factor, -jnp.sin(phase_angle) * scale_factor], axis=1
    ).astype(jnp.bfloat16)


def rcv_sum(partial):
    count = lax.axis_size("rcv")
    spread = jnp.broadcast_to(partial[None], (count,) + partial.shape)
    gathered = lax.all_to_all(spread, "rcv", 0, 0, tiled=False)
    return jnp.sum(gathered, axis=0)


def field_norm(field):
    squares = rcv_sum(jnp.sum(field * field, axis=(0, 2, 3)))
    return jnp.sqrt(squares + EPSILON)[None, :, None, None]


def _forward_kernel(cols_ref, counts_ref, x_ref, a_ref, o_ref, picked_ref):
    freq = pl.program_id(0)
    row = pl.program_id(1)
    rows = pl.num_programs(1)
    _, block, width = a_ref.shape
    slots = width // block
    sources = o_ref.shape[1]
    index = freq * rows + row
    count = counts_ref[index]
    for slot in range(slots):
        start = pl.multiple_of(cols_ref[index * slots + slot] * block, block)
        taken = x_ref[:, :, pl.ds(start, block)]
        picked_ref[:, :, slot * block : (slot + 1) * block] = jnp.where(
            slot < count, taken, jnp.zeros_like(taken)
        )
    picked = picked_ref[...].reshape(2 * sources, width)
    contract = (((1,), (1,)), ((), ()))
    by_real = lax.dot_general(picked, a_ref[0], contract, preferred_element_type=jnp.float32)
    by_imag = lax.dot_general(picked, a_ref[1], contract, preferred_element_type=jnp.float32)
    o_ref[0] = by_real[:sources] - by_imag[sources:]
    o_ref[1] = by_imag[:sources] + by_real[sources:]


def _adjoint_kernel(cols_ref, counts_ref, u_ref, a_ref, o_ref):
    freq = pl.program_id(0)
    row = pl.program_id(1)
    rows = pl.num_programs(1)
    _, block, width = a_ref.shape
    slots = width // block
    sources = u_ref.shape[1]
    index = freq * rows + row
    count = counts_ref[index]

    @pl.when(row == 0)
    def _():
        o_ref[...] = jnp.zeros(o_ref.shape, o_ref.dtype)

    field = u_ref[...].reshape(2 * sources, block)
    by_real = jnp.dot(field, a_ref[0], preferred_element_type=jnp.float32)
    by_imag = jnp.dot(field, a_ref[1], preferred_element_type=jnp.float32)
    real_part = by_real[:sources] + by_imag[sources:]
    imaginary = by_real[sources:] - by_imag[:sources]
    for slot in range(slots):

        @pl.when(slot < count)
        def _():
            start = pl.multiple_of(cols_ref[index * slots + slot] * block, block)
            lanes = slice(slot * block, (slot + 1) * block)
            o_ref[0, :, pl.ds(start, block)] += real_part[:, lanes]
            o_ref[1, :, pl.ds(start, block)] += imaginary[:, lanes]


def apply_forward(extended, stacked, cols, counts):
    local_freqs, local_blocks, _, block_size, width = stacked.shape
    _, _, sources, span = extended.shape
    grid_spec = pltpu.PrefetchScalarGridSpec(
        num_scalar_prefetch=2,
        grid=(local_freqs, local_blocks),
        in_specs=[
            pl.BlockSpec((2, None, sources, span), lambda f, r, c, n: (0, f, 0, 0)),
            pl.BlockSpec((None, None, 2, block_size, width), lambda f, r, c, n: (f, r, 0, 0, 0)),
        ],
        out_specs=pl.BlockSpec((2, None, sources, block_size), lambda f, r, c, n: (0, f, 0, r)),
        scratch_shapes=[pltpu.VMEM((2, sources, width), jnp.bfloat16)],
    )
    return pl.pallas_call(
        _forward_kernel,
        grid_spec=grid_spec,
        out_shape=jax.ShapeDtypeStruct(
            (2, local_freqs, sources, local_blocks * block_size), jnp.float32
        ),
        compiler_params=pltpu.CompilerParams(dimension_semantics=("arbitrary", "arbitrary")),
    )(cols, counts, extended, stacked)


def apply_adjoint(rounded, stacked, cols, counts, span):
    local_freqs, local_blocks, _, block_size, width = stacked.shape
    sources = rounded.shape[2]
    grid_spec = pltpu.PrefetchScalarGridSpec(
        num_scalar_prefetch=2,
        grid=(local_freqs, local_blocks),
        in_specs=[
            pl.BlockSpec((2, None, sources, block_size), lambda f, r, c, n: (0, f, 0, r)),
            pl.BlockSpec((None, None, 2, block_size, width), lambda f, r, c, n: (f, r, 0, 0, 0)),
        ],
        out_specs=pl.BlockSpec((2, None, sources, span), lambda f, r, c, n: (0, f, 0, 0)),
    )
    return pl.pallas_call(
        _adjoint_kernel,
        grid_spec=grid_spec,
        out_shape=jax.ShapeDtypeStruct((2, local_freqs, sources, span), jnp.float32),
        compiler_params=pltpu.CompilerParams(dimension_semantics=("arbitrary", "arbitrary")),
    )(cols, counts, rounded, stacked)


def body(up_time, down_blocks, block_cols, block_counts):
    freq_groups = lax.axis_size("freq")
    receiver_groups = lax.axis_size("rcv")
    shot_count, time_steps, receivers = up_time.shape
    local_freqs, local_blocks, slot_count, _, block_size, _ = down_blocks.shape
    local_rows = receivers // receiver_groups
    reach_blocks = (slot_count - 1) // 2
    rim_rows = reach_blocks * block_size
    span_blocks = local_blocks + 2 * reach_blocks
    fourier = fourier_table(time_steps, freq_groups, local_freqs)
    spectrum = jnp.einsum(
        "snr,ncgf->cfsgr", up_time, fourier, preferred_element_type=jnp.float32
    ).astype(jnp.bfloat16)
    spectrum = spectrum.reshape(
        2, local_freqs, shot_count, freq_groups * receiver_groups, local_rows
    )
    received = lax.all_to_all(spectrum, ("freq", "rcv"), split_axis=3, concat_axis=2, tiled=True)
    right_side = received.reshape(2, local_freqs, -1, local_rows).astype(jnp.float32)
    position = lax.axis_index("rcv")
    columns = jnp.clip(
        block_cols - position * local_blocks + reach_blocks, 0, span_blocks - 1
    ).reshape(-1)
    counts = jnp.clip(block_counts, 0, slot_count).reshape(-1)
    stacked = jnp.transpose(down_blocks, (0, 1, 3, 4, 2, 5)).reshape(
        local_freqs, local_blocks, 2, block_size, slot_count * block_size
    )

    def adjoint(field):
        rounded = field.astype(jnp.bfloat16)
        spread = apply_adjoint(rounded, stacked, columns, counts, span_blocks * block_size)
        lower_rim = spread[..., :rim_rows]
        middle = spread[..., rim_rows : rim_rows + local_rows]
        upper_rim = spread[..., rim_rows + local_rows :]
        from_above = from_behind(lower_rim, "rcv", -1)
        from_below = from_behind(upper_rim, "rcv", 1)
        middle = middle.at[..., :rim_rows].add(from_below)
        middle = middle.at[..., local_rows - rim_rows :].add(from_above)
        return field + middle

    def forward(field):
        extended = with_halo(field.astype(jnp.bfloat16), (("rcv", 3),), rim_rows)
        return field + apply_forward(extended, stacked, columns, counts)

    beta_norm = field_norm(right_side)
    left_vector = right_side / beta_norm
    residual_right = adjoint(left_vector)
    alpha_norm = field_norm(residual_right)
    right_vector = residual_right / alpha_norm
    search_direction = right_vector
    solution = jnp.zeros_like(right_side)
    phibar = beta_norm
    rhobar = alpha_norm
    for iteration in range(ITERS):
        residual_left = forward(right_vector) - alpha_norm * left_vector
        beta_norm = field_norm(residual_left)
        left_vector = residual_left / beta_norm
        residual_right = adjoint(left_vector) - beta_norm * right_vector
        alpha_norm = field_norm(residual_right)
        right_vector = residual_right / alpha_norm
        rho_value = jnp.sqrt(rhobar * rhobar + beta_norm * beta_norm)
        cosine = rhobar / rho_value
        sine_value = beta_norm / rho_value
        theta_value = sine_value * alpha_norm
        rhobar = -cosine * alpha_norm
        phi_value = cosine * phibar
        phibar = sine_value * phibar
        solution = solution + phi_value / rho_value * search_direction
        search_direction = right_vector - theta_value / rho_value * search_direction
    return (solution, phibar * alpha_norm * cosine * right_vector)


def solution(mesh):
    return jax.shard_map(
        body,
        mesh=mesh,
        in_specs=(
            P(("freq", "rcv"), None, None),
            P("freq", "rcv", None, None, None, None),
            P("freq", "rcv", None),
            P("freq", "rcv"),
        ),
        out_specs=(P(None, "freq", None, "rcv"), P(None, "freq", None, "rcv")),
        check_vma=False,
    )
```

```python
import math

import jax
import jax.numpy as jnp
from jax import lax
from jax.experimental import pallas as pl
from jax.experimental.pallas import tpu as pltpu
from jax.sharding import PartitionSpec as P

ITERS = 2


EPSILON = 1e-06


def with_halo(cells, sides, width):
    for axis, dim in sides:
        count = lax.axis_size(axis)
        ends = count - 1
        head = lax.slice_in_dim(cells, 0, width, axis=dim)
        tail = lax.slice_in_dim(cells, cells.shape[dim] - width, cells.shape[dim], axis=dim)
        cells = jnp.concatenate(
            [
                lax.ppermute(tail, axis, [(i, (i + 1) % count) for i in range(ends)]),
                cells,
                lax.ppermute(head, axis, [((i + 1) % count, i) for i in range(ends)]),
            ],
            axis=dim,
        )
    return cells


def from_behind(value, axis, steps):
    count = lax.axis_size(axis)
    first, last = (max(0, -steps), min(count, count - steps))
    return lax.ppermute(value, axis, [(source, source + steps) for source in range(first, last)])


def fourier_table(time_steps, freq_groups, local_freqs):
    shape = (time_steps, freq_groups, local_freqs)
    sample = lax.broadcasted_iota(jnp.int32, shape, 0)
    harmonic = (
        lax.broadcasted_iota(jnp.int32, shape, 1) * local_freqs
        + lax.broadcasted_iota(jnp.int32, shape, 2)
        + 1
    )
    phase_angle = 2.0 * math.pi / time_steps * (harmonic * sample % time_steps).astype(jnp.float32)
    scale_factor = 1.0 / math.sqrt(time_steps)
    return jnp.stack(
        [jnp.cos(phase_angle) * scale_factor, -jnp.sin(phase_angle) * scale_factor], axis=1
    ).astype(jnp.bfloat16)


def rcv_sum(partial):
    count = lax.axis_size("rcv")
    spread = jnp.broadcast_to(partial[None], (count,) + partial.shape)
    gathered = lax.all_to_all(spread, "rcv", 0, 0, tiled=False)
    return jnp.sum(gathered, axis=0)


def field_norm(field):
    squares = rcv_sum(jnp.sum(field * field, axis=(0, 2, 3)))
    return jnp.sqrt(squares + EPSILON)[None, :, None, None]


def _stack_kernel(a_ref, m_ref):
    slots, _, block, _ = a_ref.shape
    for slot in range(slots):
        real_part = a_ref[slot, 0]
        imaginary = a_ref[slot, 1]
        left = slice(2 * slot * block, (2 * slot + 1) * block)
        right = slice((2 * slot + 1) * block, (2 * slot + 2) * block)
        m_ref[:block, left] = real_part
        m_ref[:block, right] = -imaginary
        m_ref[block:, left] = imaginary
        m_ref[block:, right] = real_part


def stack_blocks(down_blocks):
    local_freqs, local_blocks, slot_count, _, block_size, _ = down_blocks.shape
    width = 2 * slot_count * block_size
    return pl.pallas_call(
        _stack_kernel,
        grid=(local_freqs, local_blocks),
        in_specs=[
            pl.BlockSpec(
                (None, None, slot_count, 2, block_size, block_size),
                lambda f, r: (f, r, 0, 0, 0, 0),
            )
        ],
        out_specs=pl.BlockSpec((None, None, 2 * block_size, width), lambda f, r: (f, r, 0, 0)),
        out_shape=jax.ShapeDtypeStruct(
            (local_freqs, local_blocks, 2 * block_size, width), jnp.bfloat16
        ),
    )(down_blocks)


def _forward_kernel(cols_ref, counts_ref, x_ref, m_ref, o_ref, picked_ref):
    freq = pl.program_id(0)
    row = pl.program_id(1)
    rows = pl.num_programs(1)
    depth, width = m_ref.shape
    block = depth // 2
    slots = width // depth
    index = freq * rows + row
    count = counts_ref[index]
    for slot in range(slots):
        start = pl.multiple_of(cols_ref[index * slots + slot] * block, block)
        for part in range(2):
            taken = x_ref[part, :, pl.ds(start, block)]
            lanes = slice((2 * slot + part) * block, (2 * slot + part + 1) * block)
            picked_ref[:, lanes] = jnp.where(slot < count, taken, jnp.zeros_like(taken))
    contract = (((1,), (1,)), ((), ()))
    product = lax.dot_general(
        picked_ref[...], m_ref[...], contract, preferred_element_type=jnp.float32
    )
    o_ref[0] = product[:, :block]
    o_ref[1] = product[:, block:]


def _adjoint_kernel(cols_ref, counts_ref, u_ref, m_ref, o_ref):
    freq = pl.program_id(0)
    row = pl.program_id(1)
    rows = pl.num_programs(1)
    depth, width = m_ref.shape
    block = depth // 2
    slots = width // depth
    index = freq * rows + row
    count = counts_ref[index]

    @pl.when(row == 0)
    def _():
        o_ref[...] = jnp.zeros(o_ref.shape, o_ref.dtype)

    field = jnp.concatenate([u_ref[0], u_ref[1]], axis=1)
    product = jnp.dot(field, m_ref[...], preferred_element_type=jnp.float32)
    for slot in range(slots):

        @pl.when(slot < count)
        def _():
            start = pl.multiple_of(cols_ref[index * slots + slot] * block, block)
            for part in range(2):
                lanes = slice((2 * slot + part) * block, (2 * slot + part + 1) * block)
                o_ref[part, :, pl.ds(start, block)] += product[:, lanes]


def apply_forward(extended, stacked, cols, counts):
    local_freqs, local_blocks, depth, width = stacked.shape
    block_size = depth // 2
    _, _, sources, span = extended.shape
    grid_spec = pltpu.PrefetchScalarGridSpec(
        num_scalar_prefetch=2,
        grid=(local_freqs, local_blocks),
        in_specs=[
            pl.BlockSpec((2, None, sources, span), lambda f, r, c, n: (0, f, 0, 0)),
            pl.BlockSpec((None, None, depth, width), lambda f, r, c, n: (f, r, 0, 0)),
        ],
        out_specs=pl.BlockSpec((2, None, sources, block_size), lambda f, r, c, n: (0, f, 0, r)),
        scratch_shapes=[pltpu.VMEM((sources, width), jnp.bfloat16)],
    )
    return pl.pallas_call(
        _forward_kernel,
        grid_spec=grid_spec,
        out_shape=jax.ShapeDtypeStruct(
            (2, local_freqs, sources, local_blocks * block_size), jnp.float32
        ),
        compiler_params=pltpu.CompilerParams(dimension_semantics=("arbitrary", "arbitrary")),
    )(cols, counts, extended, stacked)


def apply_adjoint(rounded, stacked, cols, counts, span):
    local_freqs, local_blocks, depth, width = stacked.shape
    block_size = depth // 2
    sources = rounded.shape[2]
    grid_spec = pltpu.PrefetchScalarGridSpec(
        num_scalar_prefetch=2,
        grid=(local_freqs, local_blocks),
        in_specs=[
            pl.BlockSpec((2, None, sources, block_size), lambda f, r, c, n: (0, f, 0, r)),
            pl.BlockSpec((None, None, depth, width), lambda f, r, c, n: (f, r, 0, 0)),
        ],
        out_specs=pl.BlockSpec((2, None, sources, span), lambda f, r, c, n: (0, f, 0, 0)),
    )
    return pl.pallas_call(
        _adjoint_kernel,
        grid_spec=grid_spec,
        out_shape=jax.ShapeDtypeStruct((2, local_freqs, sources, span), jnp.float32),
        compiler_params=pltpu.CompilerParams(dimension_semantics=("arbitrary", "arbitrary")),
    )(cols, counts, rounded, stacked)


def body(up_time, down_blocks, block_cols, block_counts):
    freq_groups = lax.axis_size("freq")
    receiver_groups = lax.axis_size("rcv")
    shot_count, time_steps, receivers = up_time.shape
    local_freqs, local_blocks, slot_count, _, block_size, _ = down_blocks.shape
    local_rows = receivers // receiver_groups
    reach_blocks = (slot_count - 1) // 2
    rim_rows = reach_blocks * block_size
    span_blocks = local_blocks + 2 * reach_blocks
    fourier = fourier_table(time_steps, freq_groups, local_freqs)
    spectrum = jnp.einsum(
        "snr,ncgf->cfsgr", up_time, fourier, preferred_element_type=jnp.float32
    ).astype(jnp.bfloat16)
    spectrum = spectrum.reshape(
        2, local_freqs, shot_count, freq_groups * receiver_groups, local_rows
    )
    received = lax.all_to_all(spectrum, ("freq", "rcv"), split_axis=3, concat_axis=2, tiled=True)
    right_side = received.reshape(2, local_freqs, -1, local_rows).astype(jnp.float32)
    position = lax.axis_index("rcv")
    columns = jnp.clip(
        block_cols - position * local_blocks + reach_blocks, 0, span_blocks - 1
    ).reshape(-1)
    counts = jnp.clip(block_counts, 0, slot_count).reshape(-1)
    stacked = stack_blocks(down_blocks)

    def adjoint(field):
        rounded = field.astype(jnp.bfloat16)
        spread = apply_adjoint(rounded, stacked, columns, counts, span_blocks * block_size)
        lower_rim = spread[..., :rim_rows]
        middle = spread[..., rim_rows : rim_rows + local_rows]
        upper_rim = spread[..., rim_rows + local_rows :]
        from_above = from_behind(lower_rim, "rcv", -1)
        from_below = from_behind(upper_rim, "rcv", 1)
        middle = middle.at[..., :rim_rows].add(from_below)
        middle = middle.at[..., local_rows - rim_rows :].add(from_above)
        return field + middle

    def forward(field):
        extended = with_halo(field.astype(jnp.bfloat16), (("rcv", 3),), rim_rows)
        return field + apply_forward(extended, stacked, columns, counts)

    beta_norm = field_norm(right_side)
    left_vector = right_side / beta_norm
    residual_right = adjoint(left_vector)
    alpha_norm = field_norm(residual_right)
    right_vector = residual_right / alpha_norm
    search_direction = right_vector
    solution = jnp.zeros_like(right_side)
    phibar = beta_norm
    rhobar = alpha_norm
    for iteration in range(ITERS):
        residual_left = forward(right_vector) - alpha_norm * left_vector
        beta_norm = field_norm(residual_left)
        left_vector = residual_left / beta_norm
        residual_right = adjoint(left_vector) - beta_norm * right_vector
        alpha_norm = field_norm(residual_right)
        right_vector = residual_right / alpha_norm
        rho_value = jnp.sqrt(rhobar * rhobar + beta_norm * beta_norm)
        cosine = rhobar / rho_value
        sine_value = beta_norm / rho_value
        theta_value = sine_value * alpha_norm
        rhobar = -cosine * alpha_norm
        phi_value = cosine * phibar
        phibar = sine_value * phibar
        solution = solution + phi_value / rho_value * search_direction
        search_direction = right_vector - theta_value / rho_value * search_direction
    return (solution, phibar * alpha_norm * cosine * right_vector)


def solution(mesh):
    return jax.shard_map(
        body,
        mesh=mesh,
        in_specs=(
            P(("freq", "rcv"), None, None),
            P("freq", "rcv", None, None, None, None),
            P("freq", "rcv", None),
            P("freq", "rcv"),
        ),
        out_specs=(P(None, "freq", None, "rcv"), P(None, "freq", None, "rcv")),
        check_vma=False,
    )
```

```python
import math

import jax
import jax.numpy as jnp
from jax import lax
from jax.experimental import pallas as pl
from jax.experimental.pallas import tpu as pltpu
from jax.sharding import PartitionSpec as P

ITERS = 2


EPSILON = 1e-06


def with_halo(cells, sides, width):
    for axis, dim in sides:
        count = lax.axis_size(axis)
        ends = count - 1
        head = lax.slice_in_dim(cells, 0, width, axis=dim)
        tail = lax.slice_in_dim(cells, cells.shape[dim] - width, cells.shape[dim], axis=dim)
        cells = jnp.concatenate(
            [
                lax.ppermute(tail, axis, [(i, (i + 1) % count) for i in range(ends)]),
                cells,
                lax.ppermute(head, axis, [((i + 1) % count, i) for i in range(ends)]),
            ],
            axis=dim,
        )
    return cells


def from_behind(value, axis, steps):
    count = lax.axis_size(axis)
    first, last = (max(0, -steps), min(count, count - steps))
    return lax.ppermute(value, axis, [(source, source + steps) for source in range(first, last)])


def fourier_table(time_steps, freq_groups, local_freqs):
    shape = (time_steps, freq_groups, local_freqs)
    sample = lax.broadcasted_iota(jnp.int32, shape, 0)
    harmonic = (
        lax.broadcasted_iota(jnp.int32, shape, 1) * local_freqs
        + lax.broadcasted_iota(jnp.int32, shape, 2)
        + 1
    )
    phase_angle = 2.0 * math.pi / time_steps * (harmonic * sample % time_steps).astype(jnp.float32)
    scale_factor = 1.0 / math.sqrt(time_steps)
    return jnp.stack(
        [jnp.cos(phase_angle) * scale_factor, -jnp.sin(phase_angle) * scale_factor], axis=1
    ).astype(jnp.bfloat16)


def rcv_sum(partial):
    count = lax.axis_size("rcv")
    spread = jnp.broadcast_to(partial[None], (count,) + partial.shape)
    gathered = lax.all_to_all(spread, "rcv", 0, 0, tiled=False)
    return jnp.sum(gathered, axis=0)


def squares(field):
    return rcv_sum(jnp.sum(field * field, axis=(0, 2, 3)))[None, :, None, None]


def _stack_kernel(a_ref, m_ref):
    slots, _, block, _ = a_ref.shape
    for slot in range(slots):
        real_part = a_ref[slot, 0]
        imaginary = a_ref[slot, 1]
        left = slice(2 * slot * block, (2 * slot + 1) * block)
        right = slice((2 * slot + 1) * block, (2 * slot + 2) * block)
        m_ref[:block, left] = real_part
        m_ref[:block, right] = -imaginary
        m_ref[block:, left] = imaginary
        m_ref[block:, right] = real_part


def stack_blocks(down_blocks):
    local_freqs, local_blocks, slot_count, _, block_size, _ = down_blocks.shape
    width = 2 * slot_count * block_size
    return pl.pallas_call(
        _stack_kernel,
        grid=(local_freqs, local_blocks),
        in_specs=[
            pl.BlockSpec(
                (None, None, slot_count, 2, block_size, block_size),
                lambda f, r: (f, r, 0, 0, 0, 0),
            )
        ],
        out_specs=pl.BlockSpec((None, None, 2 * block_size, width), lambda f, r: (f, r, 0, 0)),
        out_shape=jax.ShapeDtypeStruct(
            (local_freqs, local_blocks, 2 * block_size, width), jnp.bfloat16
        ),
    )(down_blocks)


def _forward_kernel(cols_ref, counts_ref, x_ref, m_ref, o_ref, picked_ref):
    freq = pl.program_id(0)
    row = pl.program_id(1)
    rows = pl.num_programs(1)
    depth, width = m_ref.shape
    block = depth // 2
    slots = width // depth
    index = freq * rows + row
    count = counts_ref[index]
    for slot in range(slots):
        start = pl.multiple_of(cols_ref[index * slots + slot] * block, block)
        for part in range(2):
            taken = x_ref[part, :, pl.ds(start, block)]
            lanes = slice((2 * slot + part) * block, (2 * slot + part + 1) * block)
            picked_ref[:, lanes] = jnp.where(slot < count, taken, jnp.zeros_like(taken))
    contract = (((1,), (1,)), ((), ()))
    product = lax.dot_general(
        picked_ref[...], m_ref[...], contract, preferred_element_type=jnp.float32
    )
    o_ref[0] = product[:, :block]
    o_ref[1] = product[:, block:]


def _adjoint_kernel(cols_ref, counts_ref, u_ref, m_ref, o_ref):
    freq = pl.program_id(0)
    row = pl.program_id(1)
    rows = pl.num_programs(1)
    depth, width = m_ref.shape
    block = depth // 2
    slots = width // depth
    index = freq * rows + row
    count = counts_ref[index]

    @pl.when(row == 0)
    def _():
        o_ref[...] = jnp.zeros(o_ref.shape, o_ref.dtype)

    field = jnp.concatenate([u_ref[0], u_ref[1]], axis=1)
    product = jnp.dot(field, m_ref[...], preferred_element_type=jnp.float32)
    for slot in range(slots):

        @pl.when(slot < count)
        def _():
            start = pl.multiple_of(cols_ref[index * slots + slot] * block, block)
            for part in range(2):
                lanes = slice((2 * slot + part) * block, (2 * slot + part + 1) * block)
                o_ref[part, :, pl.ds(start, block)] += product[:, lanes]


def apply_forward(extended, stacked, cols, counts):
    local_freqs, local_blocks, depth, width = stacked.shape
    block_size = depth // 2
    _, _, sources, span = extended.shape
    grid_spec = pltpu.PrefetchScalarGridSpec(
        num_scalar_prefetch=2,
        grid=(local_freqs, local_blocks),
        in_specs=[
            pl.BlockSpec((2, None, sources, span), lambda f, r, c, n: (0, f, 0, 0)),
            pl.BlockSpec((None, None, depth, width), lambda f, r, c, n: (f, r, 0, 0)),
        ],
        out_specs=pl.BlockSpec((2, None, sources, block_size), lambda f, r, c, n: (0, f, 0, r)),
        scratch_shapes=[pltpu.VMEM((sources, width), jnp.bfloat16)],
    )
    return pl.pallas_call(
        _forward_kernel,
        grid_spec=grid_spec,
        out_shape=jax.ShapeDtypeStruct(
            (2, local_freqs, sources, local_blocks * block_size), jnp.float32
        ),
        compiler_params=pltpu.CompilerParams(dimension_semantics=("arbitrary", "arbitrary")),
        cost_estimate=pl.CostEstimate(
            flops=2 * local_freqs * local_blocks * sources * depth * width,
            transcendentals=0,
            bytes_accessed=stacked.size * 2 + extended.size * 2 + extended.size * 4,
        ),
    )(cols, counts, extended, stacked)


def apply_adjoint(rounded, stacked, cols, counts, span):
    local_freqs, local_blocks, depth, width = stacked.shape
    block_size = depth // 2
    sources = rounded.shape[2]
    grid_spec = pltpu.PrefetchScalarGridSpec(
        num_scalar_prefetch=2,
        grid=(local_freqs, local_blocks),
        in_specs=[
            pl.BlockSpec((2, None, sources, block_size), lambda f, r, c, n: (0, f, 0, r)),
            pl.BlockSpec((None, None, depth, width), lambda f, r, c, n: (f, r, 0, 0)),
        ],
        out_specs=pl.BlockSpec((2, None, sources, span), lambda f, r, c, n: (0, f, 0, 0)),
    )
    return pl.pallas_call(
        _adjoint_kernel,
        grid_spec=grid_spec,
        out_shape=jax.ShapeDtypeStruct((2, local_freqs, sources, span), jnp.float32),
        compiler_params=pltpu.CompilerParams(dimension_semantics=("arbitrary", "arbitrary")),
        cost_estimate=pl.CostEstimate(
            flops=2 * local_freqs * local_blocks * sources * depth * width,
            transcendentals=0,
            bytes_accessed=stacked.size * 2 + rounded.size * 2 + rounded.size * 12,
        ),
    )(cols, counts, rounded, stacked)


def body(up_time, down_blocks, block_cols, block_counts):
    freq_groups = lax.axis_size("freq")
    receiver_groups = lax.axis_size("rcv")
    shot_count, time_steps, receivers = up_time.shape
    local_freqs, local_blocks, slot_count, _, block_size, _ = down_blocks.shape
    local_rows = receivers // receiver_groups
    reach_blocks = (slot_count - 1) // 2
    rim_rows = reach_blocks * block_size
    span_blocks = local_blocks + 2 * reach_blocks
    fourier = fourier_table(time_steps, freq_groups, local_freqs)
    spectrum = jnp.einsum(
        "snr,ncgf->cfsgr", up_time, fourier, preferred_element_type=jnp.float32
    ).astype(jnp.bfloat16)
    spectrum = spectrum.reshape(
        2, local_freqs, shot_count, freq_groups * receiver_groups, local_rows
    )
    received = lax.all_to_all(spectrum, ("freq", "rcv"), split_axis=3, concat_axis=2, tiled=True)
    right_side = received.reshape(2, local_freqs, -1, local_rows).astype(jnp.float32)
    position = lax.axis_index("rcv")
    columns = jnp.clip(
        block_cols - position * local_blocks + reach_blocks, 0, span_blocks - 1
    ).reshape(-1)
    counts = jnp.clip(block_counts, 0, slot_count).reshape(-1)
    stacked = stack_blocks(down_blocks)

    def adjoint(field):
        rounded = field.astype(jnp.bfloat16)
        spread = apply_adjoint(rounded, stacked, columns, counts, span_blocks * block_size)
        lower_rim = spread[..., :rim_rows]
        middle = spread[..., rim_rows : rim_rows + local_rows]
        upper_rim = spread[..., rim_rows + local_rows :]
        from_above = from_behind(lower_rim, "rcv", -1)
        from_below = from_behind(upper_rim, "rcv", 1)
        middle = middle.at[..., :rim_rows].add(from_below)
        middle = middle.at[..., local_rows - rim_rows :].add(from_above)
        return field + middle

    def forward(field):
        extended = with_halo(field.astype(jnp.bfloat16), (("rcv", 3),), rim_rows)
        return field + apply_forward(extended, stacked, columns, counts)

    beta_norm = jnp.sqrt(squares(right_side) + EPSILON)
    lifted = adjoint(right_side)
    alpha_norm = jnp.sqrt(squares(lifted) / (beta_norm * beta_norm) + EPSILON)
    left_vector = right_side / beta_norm
    right_raw = lifted
    right_scale = beta_norm * alpha_norm
    right_vector = right_raw / right_scale
    search_direction = right_vector
    solution = jnp.zeros_like(right_side)
    phibar = beta_norm
    rhobar = alpha_norm
    for iteration in range(ITERS):
        residual_left = forward(right_raw) / right_scale - alpha_norm * left_vector
        beta_norm = jnp.sqrt(squares(residual_left) + EPSILON)
        left_vector = residual_left / beta_norm
        residual_right = adjoint(residual_left) / beta_norm - beta_norm * right_vector
        alpha_norm = jnp.sqrt(squares(residual_right) + EPSILON)
        right_raw = residual_right
        right_scale = alpha_norm
        right_vector = residual_right / alpha_norm
        rho_value = jnp.sqrt(rhobar * rhobar + beta_norm * beta_norm)
        cosine = rhobar / rho_value
        sine_value = beta_norm / rho_value
        theta_value = sine_value * alpha_norm
        rhobar = -cosine * alpha_norm
        phi_value = cosine * phibar
        phibar = sine_value * phibar
        solution = solution + phi_value / rho_value * search_direction
        search_direction = right_vector - theta_value / rho_value * search_direction
    return (solution, phibar * alpha_norm * cosine * right_vector)


def solution(mesh):
    return jax.shard_map(
        body,
        mesh=mesh,
        in_specs=(
            P(("freq", "rcv"), None, None),
            P("freq", "rcv", None, None, None, None),
            P("freq", "rcv", None),
            P("freq", "rcv"),
        ),
        out_specs=(P(None, "freq", None, "rcv"), P(None, "freq", None, "rcv")),
        check_vma=False,
    )
```

```python
import math

import jax
import jax.numpy as jnp
from jax import lax
from jax.experimental import pallas as pl
from jax.experimental.pallas import tpu as pltpu
from jax.sharding import PartitionSpec as P

ITERS = 2


EPSILON = 1e-06


def with_halo(cells, sides, width):
    for axis, dim in sides:
        count = lax.axis_size(axis)
        ends = count - 1
        head = lax.slice_in_dim(cells, 0, width, axis=dim)
        tail = lax.slice_in_dim(cells, cells.shape[dim] - width, cells.shape[dim], axis=dim)
        cells = jnp.concatenate(
            [
                lax.ppermute(tail, axis, [(i, (i + 1) % count) for i in range(ends)]),
                cells,
                lax.ppermute(head, axis, [((i + 1) % count, i) for i in range(ends)]),
            ],
            axis=dim,
        )
    return cells


def from_behind(value, axis, steps):
    count = lax.axis_size(axis)
    first, last = (max(0, -steps), min(count, count - steps))
    return lax.ppermute(value, axis, [(source, source + steps) for source in range(first, last)])


def fourier_table(time_steps, freq_groups, local_freqs):
    shape = (time_steps, freq_groups, local_freqs)
    sample = lax.broadcasted_iota(jnp.int32, shape, 0)
    harmonic = (
        lax.broadcasted_iota(jnp.int32, shape, 1) * local_freqs
        + lax.broadcasted_iota(jnp.int32, shape, 2)
        + 1
    )
    phase_angle = 2.0 * math.pi / time_steps * (harmonic * sample % time_steps).astype(jnp.float32)
    scale_factor = 1.0 / math.sqrt(time_steps)
    return jnp.stack(
        [jnp.cos(phase_angle) * scale_factor, -jnp.sin(phase_angle) * scale_factor], axis=1
    ).astype(jnp.bfloat16)


def rcv_sum(partial):
    count = lax.axis_size("rcv")
    spread = jnp.broadcast_to(partial[None], (count,) + partial.shape)
    gathered = lax.all_to_all(spread, "rcv", 0, 0, tiled=False)
    return jnp.sum(gathered, axis=0)


def squares(field):
    return rcv_sum(jnp.sum(field * field, axis=(0, 2, 3)))[None, :, None, None]


def _stack_kernel(a_ref, m_ref):
    slots, _, block, _ = a_ref.shape
    for slot in range(slots):
        real_part = a_ref[slot, 0]
        imaginary = a_ref[slot, 1]
        left = slice(2 * slot * block, (2 * slot + 1) * block)
        right = slice((2 * slot + 1) * block, (2 * slot + 2) * block)
        m_ref[:block, left] = real_part
        m_ref[:block, right] = -imaginary
        m_ref[block:, left] = imaginary
        m_ref[block:, right] = real_part


def stack_blocks(down_blocks):
    local_freqs, local_blocks, slot_count, _, block_size, _ = down_blocks.shape
    width = 2 * slot_count * block_size
    return pl.pallas_call(
        _stack_kernel,
        grid=(local_freqs, local_blocks),
        in_specs=[
            pl.BlockSpec(
                (None, None, slot_count, 2, block_size, block_size),
                lambda f, r: (f, r, 0, 0, 0, 0),
            )
        ],
        out_specs=pl.BlockSpec((None, None, 2 * block_size, width), lambda f, r: (f, r, 0, 0)),
        out_shape=jax.ShapeDtypeStruct(
            (local_freqs, local_blocks, 2 * block_size, width), jnp.bfloat16
        ),
    )(down_blocks)


def _forward_kernel(cols_ref, counts_ref, x_ref, m_ref, o_ref, picked_ref):
    freq = pl.program_id(0)
    row = pl.program_id(1)
    rows = pl.num_programs(1)
    depth, width = m_ref.shape
    block = depth // 2
    slots = width // depth
    index = freq * rows + row
    count = counts_ref[index]
    for slot in range(slots):
        start = pl.multiple_of(cols_ref[index * slots + slot] * block, block)
        for part in range(2):
            taken = x_ref[part, :, pl.ds(start, block)]
            lanes = slice((2 * slot + part) * block, (2 * slot + part + 1) * block)
            picked_ref[:, lanes] = jnp.where(slot < count, taken, jnp.zeros_like(taken))
    contract = (((1,), (1,)), ((), ()))
    product = lax.dot_general(
        picked_ref[...], m_ref[...], contract, preferred_element_type=jnp.float32
    )
    o_ref[0] = product[:, :block]
    o_ref[1] = product[:, block:]


def _adjoint_kernel(cols_ref, counts_ref, u_ref, m_ref, o_ref):
    freq = pl.program_id(0)
    row = pl.program_id(1)
    rows = pl.num_programs(1)
    depth, width = m_ref.shape
    block = depth // 2
    slots = width // depth
    index = freq * rows + row
    count = counts_ref[index]

    @pl.when(row == 0)
    def _():
        o_ref[...] = jnp.zeros(o_ref.shape, o_ref.dtype)

    field = jnp.concatenate([u_ref[0], u_ref[1]], axis=1)
    product = jnp.dot(field, m_ref[...], preferred_element_type=jnp.float32)
    for slot in range(slots):

        @pl.when(slot < count)
        def _():
            start = pl.multiple_of(cols_ref[index * slots + slot] * block, block)
            for part in range(2):
                lanes = slice((2 * slot + part) * block, (2 * slot + part + 1) * block)
                o_ref[part, :, pl.ds(start, block)] += product[:, lanes]


def _both_kernel(
    cols_ref, counts_ref, coef_ref, x_ref, q_ref, u_ref, m_ref, p_ref, o_ref, picked_ref
):
    freq = pl.program_id(0)
    row = pl.program_id(1)
    rows = pl.num_programs(1)
    depth, width = m_ref.shape
    block = depth // 2
    slots = width // depth
    index = freq * rows + row
    count = counts_ref[index]

    @pl.when(row == 0)
    def _():
        o_ref[...] = jnp.zeros(o_ref.shape, o_ref.dtype)

    for slot in range(slots):
        start = pl.multiple_of(cols_ref[index * slots + slot] * block, block)
        for part in range(2):
            taken = x_ref[part, :, pl.ds(start, block)]
            lanes = slice((2 * slot + part) * block, (2 * slot + part + 1) * block)
            picked_ref[:, lanes] = jnp.where(slot < count, taken, jnp.zeros_like(taken))
    contract = (((1,), (1,)), ((), ()))
    product = lax.dot_general(
        picked_ref[...], m_ref[...], contract, preferred_element_type=jnp.float32
    )
    scale = coef_ref[2 * freq]
    shift = coef_ref[2 * freq + 1]
    for part in range(2):
        lanes = slice(part * block, (part + 1) * block)
        p_ref[part] = (q_ref[part] + product[:, lanes]) / scale - shift * u_ref[part]
    field = jnp.concatenate(
        [p_ref[0].astype(jnp.bfloat16), p_ref[1].astype(jnp.bfloat16)], axis=1
    )
    spread = jnp.dot(field, m_ref[...], preferred_element_type=jnp.float32)
    for slot in range(slots):

        @pl.when(slot < count)
        def _():
            start = pl.multiple_of(cols_ref[index * slots + slot] * block, block)
            for part in range(2):
                lanes = slice((2 * slot + part) * block, (2 * slot + part + 1) * block)
                o_ref[part, :, pl.ds(start, block)] += spread[:, lanes]


def apply_both(extended, raw, left, coefs, stacked, cols, counts):
    local_freqs, local_blocks, depth, width = stacked.shape
    block_size = depth // 2
    _, _, sources, span = extended.shape
    own = pl.BlockSpec((2, None, sources, block_size), lambda f, r, c, n: (0, f, 0, r))
    grid_spec = pltpu.PrefetchScalarGridSpec(
        num_scalar_prefetch=2,
        grid=(local_freqs, local_blocks),
        in_specs=[
            pl.BlockSpec(memory_space=pltpu.SMEM),
            pl.BlockSpec((2, None, sources, span), lambda f, r, c, n: (0, f, 0, 0)),
            own,
            own,
            pl.BlockSpec((None, None, depth, width), lambda f, r, c, n: (f, r, 0, 0)),
        ],
        out_specs=[
            own,
            pl.BlockSpec((2, None, sources, span), lambda f, r, c, n: (0, f, 0, 0)),
        ],
        scratch_shapes=[pltpu.VMEM((sources, width), jnp.bfloat16)],
    )
    return pl.pallas_call(
        _both_kernel,
        grid_spec=grid_spec,
        out_shape=[
            jax.ShapeDtypeStruct(raw.shape, jnp.float32),
            jax.ShapeDtypeStruct((2, local_freqs, sources, span), jnp.float32),
        ],
        compiler_params=pltpu.CompilerParams(dimension_semantics=("arbitrary", "arbitrary")),
        cost_estimate=pl.CostEstimate(
            flops=4 * local_freqs * local_blocks * sources * depth * width,
            transcendentals=0,
            bytes_accessed=stacked.size * 2 + extended.size * 2 + raw.size * 40,
        ),
    )(cols, counts, coefs, extended, raw, left, stacked)


def apply_forward(extended, stacked, cols, counts):
    local_freqs, local_blocks, depth, width = stacked.shape
    block_size = depth // 2
    _, _, sources, span = extended.shape
    grid_spec = pltpu.PrefetchScalarGridSpec(
        num_scalar_prefetch=2,
        grid=(local_freqs, local_blocks),
        in_specs=[
            pl.BlockSpec((2, None, sources, span), lambda f, r, c, n: (0, f, 0, 0)),
            pl.BlockSpec((None, None, depth, width), lambda f, r, c, n: (f, r, 0, 0)),
        ],
        out_specs=pl.BlockSpec((2, None, sources, block_size), lambda f, r, c, n: (0, f, 0, r)),
        scratch_shapes=[pltpu.VMEM((sources, width), jnp.bfloat16)],
    )
    return pl.pallas_call(
        _forward_kernel,
        grid_spec=grid_spec,
        out_shape=jax.ShapeDtypeStruct(
            (2, local_freqs, sources, local_blocks * block_size), jnp.float32
        ),
        compiler_params=pltpu.CompilerParams(dimension_semantics=("arbitrary", "arbitrary")),
        cost_estimate=pl.CostEstimate(
            flops=2 * local_freqs * local_blocks * sources * depth * width,
            transcendentals=0,
            bytes_accessed=stacked.size * 2 + extended.size * 2 + extended.size * 4,
        ),
    )(cols, counts, extended, stacked)


def apply_adjoint(rounded, stacked, cols, counts, span):
    local_freqs, local_blocks, depth, width = stacked.shape
    block_size = depth // 2
    sources = rounded.shape[2]
    grid_spec = pltpu.PrefetchScalarGridSpec(
        num_scalar_prefetch=2,
        grid=(local_freqs, local_blocks),
        in_specs=[
            pl.BlockSpec((2, None, sources, block_size), lambda f, r, c, n: (0, f, 0, r)),
            pl.BlockSpec((None, None, depth, width), lambda f, r, c, n: (f, r, 0, 0)),
        ],
        out_specs=pl.BlockSpec((2, None, sources, span), lambda f, r, c, n: (0, f, 0, 0)),
    )
    return pl.pallas_call(
        _adjoint_kernel,
        grid_spec=grid_spec,
        out_shape=jax.ShapeDtypeStruct((2, local_freqs, sources, span), jnp.float32),
        compiler_params=pltpu.CompilerParams(dimension_semantics=("arbitrary", "arbitrary")),
        cost_estimate=pl.CostEstimate(
            flops=2 * local_freqs * local_blocks * sources * depth * width,
            transcendentals=0,
            bytes_accessed=stacked.size * 2 + rounded.size * 2 + rounded.size * 12,
        ),
    )(cols, counts, rounded, stacked)


def body(up_time, down_blocks, block_cols, block_counts):
    freq_groups = lax.axis_size("freq")
    receiver_groups = lax.axis_size("rcv")
    shot_count, time_steps, receivers = up_time.shape
    local_freqs, local_blocks, slot_count, _, block_size, _ = down_blocks.shape
    local_rows = receivers // receiver_groups
    reach_blocks = (slot_count - 1) // 2
    rim_rows = reach_blocks * block_size
    span_blocks = local_blocks + 2 * reach_blocks
    fourier = fourier_table(time_steps, freq_groups, local_freqs)
    spectrum = jnp.einsum(
        "snr,ncgf->cfsgr", up_time, fourier, preferred_element_type=jnp.float32
    ).astype(jnp.bfloat16)
    spectrum = spectrum.reshape(
        2, local_freqs, shot_count, freq_groups * receiver_groups, local_rows
    )
    received = lax.all_to_all(spectrum, ("freq", "rcv"), split_axis=3, concat_axis=2, tiled=True)
    right_side = received.reshape(2, local_freqs, -1, local_rows).astype(jnp.float32)
    position = lax.axis_index("rcv")
    columns = jnp.clip(
        block_cols - position * local_blocks + reach_blocks, 0, span_blocks - 1
    ).reshape(-1)
    counts = jnp.clip(block_counts, 0, slot_count).reshape(-1)
    stacked = stack_blocks(down_blocks)

    def exchange(spread):
        lower_rim = spread[..., :rim_rows]
        middle = spread[..., rim_rows : rim_rows + local_rows]
        upper_rim = spread[..., rim_rows + local_rows :]
        from_above = from_behind(lower_rim, "rcv", -1)
        from_below = from_behind(upper_rim, "rcv", 1)
        middle = middle.at[..., :rim_rows].add(from_below)
        middle = middle.at[..., local_rows - rim_rows :].add(from_above)
        return middle

    def adjoint(field):
        rounded = field.astype(jnp.bfloat16)
        spread = apply_adjoint(rounded, stacked, columns, counts, span_blocks * block_size)
        return field + exchange(spread)

    def forward_adjoint(raw, scale, left, shift):
        extended = with_halo(raw.astype(jnp.bfloat16), (("rcv", 3),), rim_rows)
        coefs = jnp.stack(
            [jnp.broadcast_to(scale, shift.shape).reshape(-1), shift.reshape(-1)], axis=1
        ).reshape(-1)
        residual, spread = apply_both(extended, raw, left, coefs, stacked, columns, counts)
        return residual, residual + exchange(spread)

    def forward(field):
        extended = with_halo(field.astype(jnp.bfloat16), (("rcv", 3),), rim_rows)
        return field + apply_forward(extended, stacked, columns, counts)

    beta_norm = jnp.sqrt(squares(right_side) + EPSILON)
    lifted = adjoint(right_side)
    alpha_norm = jnp.sqrt(squares(lifted) / (beta_norm * beta_norm) + EPSILON)
    left_vector = right_side / beta_norm
    right_raw = lifted
    right_scale = beta_norm * alpha_norm
    right_vector = right_raw / right_scale
    search_direction = right_vector
    solution = jnp.zeros_like(right_side)
    phibar = beta_norm
    rhobar = alpha_norm
    for iteration in range(ITERS):
        residual_left, lifted = forward_adjoint(right_raw, right_scale, left_vector, alpha_norm)
        beta_norm = jnp.sqrt(squares(residual_left) + EPSILON)
        left_vector = residual_left / beta_norm
        residual_right = lifted / beta_norm - beta_norm * right_vector
        alpha_norm = jnp.sqrt(squares(residual_right) + EPSILON)
        right_raw = residual_right
        right_scale = alpha_norm
        right_vector = residual_right / alpha_norm
        rho_value = jnp.sqrt(rhobar * rhobar + beta_norm * beta_norm)
        cosine = rhobar / rho_value
        sine_value = beta_norm / rho_value
        theta_value = sine_value * alpha_norm
        rhobar = -cosine * alpha_norm
        phi_value = cosine * phibar
        phibar = sine_value * phibar
        solution = solution + phi_value / rho_value * search_direction
        search_direction = right_vector - theta_value / rho_value * search_direction
    return (solution, phibar * alpha_norm * cosine * right_vector)


def solution(mesh):
    return jax.shard_map(
        body,
        mesh=mesh,
        in_specs=(
            P(("freq", "rcv"), None, None),
            P("freq", "rcv", None, None, None, None),
            P("freq", "rcv", None),
            P("freq", "rcv"),
        ),
        out_specs=(P(None, "freq", None, "rcv"), P(None, "freq", None, "rcv")),
        check_vma=False,
    )
```

```python
import math

import jax
import jax.numpy as jnp
from jax import lax
from jax.experimental import pallas as pl
from jax.experimental.pallas import tpu as pltpu
from jax.sharding import PartitionSpec as P

ITERS = 2


EPSILON = 1e-06


def with_halo(cells, sides, width):
    for axis, dim in sides:
        count = lax.axis_size(axis)
        ends = count - 1
        head = lax.slice_in_dim(cells, 0, width, axis=dim)
        tail = lax.slice_in_dim(cells, cells.shape[dim] - width, cells.shape[dim], axis=dim)
        cells = jnp.concatenate(
            [
                lax.ppermute(tail, axis, [(i, (i + 1) % count) for i in range(ends)]),
                cells,
                lax.ppermute(head, axis, [((i + 1) % count, i) for i in range(ends)]),
            ],
            axis=dim,
        )
    return cells


def from_behind(value, axis, steps):
    count = lax.axis_size(axis)
    first, last = (max(0, -steps), min(count, count - steps))
    return lax.ppermute(value, axis, [(source, source + steps) for source in range(first, last)])


def fourier_table(time_steps, freq_groups, local_freqs):
    shape = (time_steps, freq_groups, local_freqs)
    sample = lax.broadcasted_iota(jnp.int32, shape, 0)
    harmonic = (
        lax.broadcasted_iota(jnp.int32, shape, 1) * local_freqs
        + lax.broadcasted_iota(jnp.int32, shape, 2)
        + 1
    )
    phase_angle = 2.0 * math.pi / time_steps * (harmonic * sample % time_steps).astype(jnp.float32)
    scale_factor = 1.0 / math.sqrt(time_steps)
    return jnp.stack(
        [jnp.cos(phase_angle) * scale_factor, -jnp.sin(phase_angle) * scale_factor], axis=1
    ).astype(jnp.bfloat16)


def rcv_sum(partial):
    count = lax.axis_size("rcv")
    spread = jnp.broadcast_to(partial[None], (count,) + partial.shape)
    gathered = lax.all_to_all(spread, "rcv", 0, 0, tiled=False)
    return jnp.sum(gathered, axis=0)


def squares(field):
    return rcv_sum(jnp.sum(field * field, axis=(0, 2, 3)))[None, :, None, None]


def both_squares(first, second):
    partial = jnp.stack(
        [jnp.sum(first * first, axis=(0, 2, 3)), jnp.sum(second * second, axis=(0, 2, 3))]
    )
    total = rcv_sum(partial)
    return total[0][None, :, None, None], total[1][None, :, None, None]


def _stack_kernel(a_ref, m_ref):
    slots, _, block, _ = a_ref.shape
    for slot in range(slots):
        real_part = a_ref[slot, 0]
        imaginary = a_ref[slot, 1]
        left = slice(2 * slot * block, (2 * slot + 1) * block)
        right = slice((2 * slot + 1) * block, (2 * slot + 2) * block)
        m_ref[:block, left] = real_part
        m_ref[:block, right] = -imaginary
        m_ref[block:, left] = imaginary
        m_ref[block:, right] = real_part


def stack_blocks(down_blocks):
    local_freqs, local_blocks, slot_count, _, block_size, _ = down_blocks.shape
    width = 2 * slot_count * block_size
    return pl.pallas_call(
        _stack_kernel,
        grid=(local_freqs, local_blocks),
        in_specs=[
            pl.BlockSpec(
                (None, None, slot_count, 2, block_size, block_size),
                lambda f, r: (f, r, 0, 0, 0, 0),
            )
        ],
        out_specs=pl.BlockSpec((None, None, 2 * block_size, width), lambda f, r: (f, r, 0, 0)),
        out_shape=jax.ShapeDtypeStruct(
            (local_freqs, local_blocks, 2 * block_size, width), jnp.bfloat16
        ),
    )(down_blocks)


def _forward_kernel(cols_ref, counts_ref, x_ref, m_ref, o_ref, picked_ref):
    freq = pl.program_id(0)
    row = pl.program_id(1)
    rows = pl.num_programs(1)
    depth, width = m_ref.shape
    block = depth // 2
    slots = width // depth
    index = freq * rows + row
    count = counts_ref[index]
    for slot in range(slots):
        start = pl.multiple_of(cols_ref[index * slots + slot] * block, block)
        for part in range(2):
            taken = x_ref[part, :, pl.ds(start, block)]
            lanes = slice((2 * slot + part) * block, (2 * slot + part + 1) * block)
            picked_ref[:, lanes] = jnp.where(slot < count, taken, jnp.zeros_like(taken))
    contract = (((1,), (1,)), ((), ()))
    product = lax.dot_general(
        picked_ref[...], m_ref[...], contract, preferred_element_type=jnp.float32
    )
    o_ref[0] = product[:, :block]
    o_ref[1] = product[:, block:]


def _adjoint_kernel(cols_ref, counts_ref, u_ref, m_ref, o_ref):
    freq = pl.program_id(0)
    row = pl.program_id(1)
    rows = pl.num_programs(1)
    depth, width = m_ref.shape
    block = depth // 2
    slots = width // depth
    index = freq * rows + row
    count = counts_ref[index]

    @pl.when(row == 0)
    def _():
        o_ref[...] = jnp.zeros(o_ref.shape, o_ref.dtype)

    field = jnp.concatenate([u_ref[0], u_ref[1]], axis=1)
    product = jnp.dot(field, m_ref[...], preferred_element_type=jnp.float32)
    for slot in range(slots):

        @pl.when(slot < count)
        def _():
            start = pl.multiple_of(cols_ref[index * slots + slot] * block, block)
            for part in range(2):
                lanes = slice((2 * slot + part) * block, (2 * slot + part + 1) * block)
                o_ref[part, :, pl.ds(start, block)] += product[:, lanes]


def _both_kernel(
    cols_ref, counts_ref, coef_ref, x_ref, q_ref, u_ref, m_ref, p_ref, o_ref, picked_ref
):
    freq = pl.program_id(0)
    row = pl.program_id(1)
    rows = pl.num_programs(1)
    depth, width = m_ref.shape
    block = depth // 2
    slots = width // depth
    index = freq * rows + row
    count = counts_ref[index]

    @pl.when(row == 0)
    def _():
        o_ref[...] = jnp.zeros(o_ref.shape, o_ref.dtype)

    for slot in range(slots):
        start = pl.multiple_of(cols_ref[index * slots + slot] * block, block)
        for part in range(2):
            taken = x_ref[part, :, pl.ds(start, block)]
            lanes = slice((2 * slot + part) * block, (2 * slot + part + 1) * block)
            picked_ref[:, lanes] = jnp.where(slot < count, taken, jnp.zeros_like(taken))
    contract = (((1,), (1,)), ((), ()))
    product = lax.dot_general(
        picked_ref[...], m_ref[...], contract, preferred_element_type=jnp.float32
    )
    scale = coef_ref[2 * freq]
    shift = coef_ref[2 * freq + 1]
    for part in range(2):
        lanes = slice(part * block, (part + 1) * block)
        p_ref[part] = (q_ref[part] + product[:, lanes]) / scale - shift * u_ref[part]
    field = jnp.concatenate(
        [p_ref[0].astype(jnp.bfloat16), p_ref[1].astype(jnp.bfloat16)], axis=1
    )
    spread = jnp.dot(field, m_ref[...], preferred_element_type=jnp.float32)
    for slot in range(slots):

        @pl.when(slot < count)
        def _():
            start = pl.multiple_of(cols_ref[index * slots + slot] * block, block)
            for part in range(2):
                lanes = slice((2 * slot + part) * block, (2 * slot + part + 1) * block)
                o_ref[part, :, pl.ds(start, block)] += spread[:, lanes]


def apply_both(extended, raw, left, coefs, stacked, cols, counts):
    local_freqs, local_blocks, depth, width = stacked.shape
    block_size = depth // 2
    _, _, sources, span = extended.shape
    own = pl.BlockSpec((2, None, sources, block_size), lambda f, r, c, n: (0, f, 0, r))
    grid_spec = pltpu.PrefetchScalarGridSpec(
        num_scalar_prefetch=2,
        grid=(local_freqs, local_blocks),
        in_specs=[
            pl.BlockSpec(memory_space=pltpu.SMEM),
            pl.BlockSpec((2, None, sources, span), lambda f, r, c, n: (0, f, 0, 0)),
            own,
            own,
            pl.BlockSpec((None, None, depth, width), lambda f, r, c, n: (f, r, 0, 0)),
        ],
        out_specs=[
            own,
            pl.BlockSpec((2, None, sources, span), lambda f, r, c, n: (0, f, 0, 0)),
        ],
        scratch_shapes=[pltpu.VMEM((sources, width), jnp.bfloat16)],
    )
    return pl.pallas_call(
        _both_kernel,
        grid_spec=grid_spec,
        out_shape=[
            jax.ShapeDtypeStruct(raw.shape, jnp.float32),
            jax.ShapeDtypeStruct((2, local_freqs, sources, span), jnp.float32),
        ],
        compiler_params=pltpu.CompilerParams(dimension_semantics=("arbitrary", "arbitrary")),
        cost_estimate=pl.CostEstimate(
            flops=4 * local_freqs * local_blocks * sources * depth * width,
            transcendentals=0,
            bytes_accessed=stacked.size * 2 + extended.size * 2 + raw.size * 40,
        ),
    )(cols, counts, coefs, extended, raw, left, stacked)


def apply_forward(extended, stacked, cols, counts):
    local_freqs, local_blocks, depth, width = stacked.shape
    block_size = depth // 2
    _, _, sources, span = extended.shape
    grid_spec = pltpu.PrefetchScalarGridSpec(
        num_scalar_prefetch=2,
        grid=(local_freqs, local_blocks),
        in_specs=[
            pl.BlockSpec((2, None, sources, span), lambda f, r, c, n: (0, f, 0, 0)),
            pl.BlockSpec((None, None, depth, width), lambda f, r, c, n: (f, r, 0, 0)),
        ],
        out_specs=pl.BlockSpec((2, None, sources, block_size), lambda f, r, c, n: (0, f, 0, r)),
        scratch_shapes=[pltpu.VMEM((sources, width), jnp.bfloat16)],
    )
    return pl.pallas_call(
        _forward_kernel,
        grid_spec=grid_spec,
        out_shape=jax.ShapeDtypeStruct(
            (2, local_freqs, sources, local_blocks * block_size), jnp.float32
        ),
        compiler_params=pltpu.CompilerParams(dimension_semantics=("arbitrary", "arbitrary")),
        cost_estimate=pl.CostEstimate(
            flops=2 * local_freqs * local_blocks * sources * depth * width,
            transcendentals=0,
            bytes_accessed=stacked.size * 2 + extended.size * 2 + extended.size * 4,
        ),
    )(cols, counts, extended, stacked)


def apply_adjoint(rounded, stacked, cols, counts, span):
    local_freqs, local_blocks, depth, width = stacked.shape
    block_size = depth // 2
    sources = rounded.shape[2]
    grid_spec = pltpu.PrefetchScalarGridSpec(
        num_scalar_prefetch=2,
        grid=(local_freqs, local_blocks),
        in_specs=[
            pl.BlockSpec((2, None, sources, block_size), lambda f, r, c, n: (0, f, 0, r)),
            pl.BlockSpec((None, None, depth, width), lambda f, r, c, n: (f, r, 0, 0)),
        ],
        out_specs=pl.BlockSpec((2, None, sources, span), lambda f, r, c, n: (0, f, 0, 0)),
    )
    return pl.pallas_call(
        _adjoint_kernel,
        grid_spec=grid_spec,
        out_shape=jax.ShapeDtypeStruct((2, local_freqs, sources, span), jnp.float32),
        compiler_params=pltpu.CompilerParams(dimension_semantics=("arbitrary", "arbitrary")),
        cost_estimate=pl.CostEstimate(
            flops=2 * local_freqs * local_blocks * sources * depth * width,
            transcendentals=0,
            bytes_accessed=stacked.size * 2 + rounded.size * 2 + rounded.size * 12,
        ),
    )(cols, counts, rounded, stacked)


def body(up_time, down_blocks, block_cols, block_counts):
    freq_groups = lax.axis_size("freq")
    receiver_groups = lax.axis_size("rcv")
    shot_count, time_steps, receivers = up_time.shape
    local_freqs, local_blocks, slot_count, _, block_size, _ = down_blocks.shape
    local_rows = receivers // receiver_groups
    reach_blocks = (slot_count - 1) // 2
    rim_rows = reach_blocks * block_size
    span_blocks = local_blocks + 2 * reach_blocks
    fourier = fourier_table(time_steps, freq_groups, local_freqs)
    spectrum = jnp.einsum(
        "snr,ncgf->cfsgr", up_time, fourier, preferred_element_type=jnp.float32
    ).astype(jnp.bfloat16)
    spectrum = spectrum.reshape(
        2, local_freqs, shot_count, freq_groups * receiver_groups, local_rows
    )
    received = lax.all_to_all(spectrum, ("freq", "rcv"), split_axis=3, concat_axis=2, tiled=True)
    right_side = received.reshape(2, local_freqs, -1, local_rows).astype(jnp.float32)
    position = lax.axis_index("rcv")
    columns = jnp.clip(
        block_cols - position * local_blocks + reach_blocks, 0, span_blocks - 1
    ).reshape(-1)
    counts = jnp.clip(block_counts, 0, slot_count).reshape(-1)
    stacked = stack_blocks(down_blocks)

    def exchange(spread):
        lower_rim = spread[..., :rim_rows]
        middle = spread[..., rim_rows : rim_rows + local_rows]
        upper_rim = spread[..., rim_rows + local_rows :]
        from_above = from_behind(lower_rim, "rcv", -1)
        from_below = from_behind(upper_rim, "rcv", 1)
        middle = middle.at[..., :rim_rows].add(from_below)
        middle = middle.at[..., local_rows - rim_rows :].add(from_above)
        return middle

    def adjoint(field):
        rounded = field.astype(jnp.bfloat16)
        spread = apply_adjoint(rounded, stacked, columns, counts, span_blocks * block_size)
        return field + exchange(spread)

    def forward_adjoint(raw, scale, left, shift):
        extended = with_halo(raw.astype(jnp.bfloat16), (("rcv", 3),), rim_rows)
        coefs = jnp.stack(
            [jnp.broadcast_to(scale, shift.shape).reshape(-1), shift.reshape(-1)], axis=1
        ).reshape(-1)
        residual, spread = apply_both(extended, raw, left, coefs, stacked, columns, counts)
        return residual, residual + exchange(spread)

    def forward(field):
        extended = with_halo(field.astype(jnp.bfloat16), (("rcv", 3),), rim_rows)
        return field + apply_forward(extended, stacked, columns, counts)

    lifted = adjoint(right_side)
    right_squares, lifted_squares = both_squares(right_side, lifted)
    beta_norm = jnp.sqrt(right_squares + EPSILON)
    alpha_norm = jnp.sqrt(lifted_squares / (beta_norm * beta_norm) + EPSILON)
    left_vector = right_side / beta_norm
    right_raw = lifted
    right_scale = beta_norm * alpha_norm
    right_vector = right_raw / right_scale
    search_direction = right_vector
    solution = jnp.zeros_like(right_side)
    phibar = beta_norm
    rhobar = alpha_norm
    for iteration in range(ITERS):
        last = iteration == ITERS - 1
        residual_left, lifted = forward_adjoint(right_raw, right_scale, left_vector, alpha_norm)
        beta_norm = jnp.sqrt(squares(residual_left) + EPSILON)
        left_vector = residual_left / beta_norm
        residual_right = lifted / beta_norm - beta_norm * right_vector
        rho_value = jnp.sqrt(rhobar * rhobar + beta_norm * beta_norm)
        cosine = rhobar / rho_value
        sine_value = beta_norm / rho_value
        phi_value = cosine * phibar
        phibar = sine_value * phibar
        solution = solution + phi_value / rho_value * search_direction
        if last:
            break
        alpha_norm = jnp.sqrt(squares(residual_right) + EPSILON)
        right_raw = residual_right
        right_scale = alpha_norm
        right_vector = residual_right / alpha_norm
        theta_value = sine_value * alpha_norm
        rhobar = -cosine * alpha_norm
        search_direction = right_vector - theta_value / rho_value * search_direction
    return (solution, phibar * cosine * residual_right)


def solution(mesh):
    return jax.shard_map(
        body,
        mesh=mesh,
        in_specs=(
            P(("freq", "rcv"), None, None),
            P("freq", "rcv", None, None, None, None),
            P("freq", "rcv", None),
            P("freq", "rcv"),
        ),
        out_specs=(P(None, "freq", None, "rcv"), P(None, "freq", None, "rcv")),
        check_vma=False,
    )
```

```python
import math

import jax
import jax.numpy as jnp
from jax import lax
from jax.experimental import pallas as pl
from jax.experimental.pallas import tpu as pltpu
from jax.sharding import PartitionSpec as P

ITERS = 2


EPSILON = 1e-06


def with_halo(cells, sides, width):
    for axis, dim in sides:
        count = lax.axis_size(axis)
        ends = count - 1
        head = lax.slice_in_dim(cells, 0, width, axis=dim)
        tail = lax.slice_in_dim(cells, cells.shape[dim] - width, cells.shape[dim], axis=dim)
        cells = jnp.concatenate(
            [
                lax.ppermute(tail, axis, [(i, (i + 1) % count) for i in range(ends)]),
                cells,
                lax.ppermute(head, axis, [((i + 1) % count, i) for i in range(ends)]),
            ],
            axis=dim,
        )
    return cells


def from_behind(value, axis, steps):
    count = lax.axis_size(axis)
    first, last = (max(0, -steps), min(count, count - steps))
    return lax.ppermute(value, axis, [(source, source + steps) for source in range(first, last)])


def fourier_table(time_steps, freq_groups, local_freqs):
    shape = (time_steps, freq_groups, local_freqs)
    sample = lax.broadcasted_iota(jnp.int32, shape, 0)
    harmonic = (
        lax.broadcasted_iota(jnp.int32, shape, 1) * local_freqs
        + lax.broadcasted_iota(jnp.int32, shape, 2)
        + 1
    )
    phase_angle = 2.0 * math.pi / time_steps * (harmonic * sample % time_steps).astype(jnp.float32)
    scale_factor = 1.0 / math.sqrt(time_steps)
    return jnp.stack(
        [jnp.cos(phase_angle) * scale_factor, -jnp.sin(phase_angle) * scale_factor], axis=1
    ).astype(jnp.bfloat16)


def rcv_sum(partial):
    count = lax.axis_size("rcv")
    spread = jnp.broadcast_to(partial[None], (count,) + partial.shape)
    gathered = lax.all_to_all(spread, "rcv", 0, 0, tiled=False)
    return jnp.sum(gathered, axis=0)


def squares(field):
    return rcv_sum(jnp.sum(field * field, axis=(0, 2, 3)))[None, :, None, None]


def both_squares(first, second):
    partial = jnp.stack(
        [jnp.sum(first * first, axis=(0, 2, 3)), jnp.sum(second * second, axis=(0, 2, 3))]
    )
    total = rcv_sum(partial)
    return total[0][None, :, None, None], total[1][None, :, None, None]


def _stack_kernel(a_ref, m_ref):
    slots, _, block, _ = a_ref.shape
    for slot in range(slots):
        real_part = a_ref[slot, 0]
        imaginary = a_ref[slot, 1]
        left = slice(2 * slot * block, (2 * slot + 1) * block)
        right = slice((2 * slot + 1) * block, (2 * slot + 2) * block)
        m_ref[:block, left] = real_part
        m_ref[:block, right] = -imaginary
        m_ref[block:, left] = imaginary
        m_ref[block:, right] = real_part


def stack_blocks(down_blocks):
    local_freqs, local_blocks, slot_count, _, block_size, _ = down_blocks.shape
    width = 2 * slot_count * block_size
    return pl.pallas_call(
        _stack_kernel,
        grid=(local_freqs, local_blocks),
        in_specs=[
            pl.BlockSpec(
                (None, None, slot_count, 2, block_size, block_size),
                lambda f, r: (f, r, 0, 0, 0, 0),
            )
        ],
        out_specs=pl.BlockSpec((None, None, 2 * block_size, width), lambda f, r: (f, r, 0, 0)),
        out_shape=jax.ShapeDtypeStruct(
            (local_freqs, local_blocks, 2 * block_size, width), jnp.bfloat16
        ),
    )(down_blocks)


def _forward_kernel(cols_ref, counts_ref, x_ref, m_ref, o_ref, picked_ref):
    freq = pl.program_id(0)
    row = pl.program_id(1)
    rows = pl.num_programs(1)
    depth, width = m_ref.shape
    block = depth // 2
    slots = width // depth
    index = freq * rows + row
    count = counts_ref[index]
    for slot in range(slots):
        start = pl.multiple_of(cols_ref[index * slots + slot] * block, block)
        for part in range(2):
            taken = x_ref[part, :, pl.ds(start, block)]
            lanes = slice((2 * slot + part) * block, (2 * slot + part + 1) * block)
            picked_ref[:, lanes] = jnp.where(slot < count, taken, jnp.zeros_like(taken))
    contract = (((1,), (1,)), ((), ()))
    product = lax.dot_general(
        picked_ref[...], m_ref[...], contract, preferred_element_type=jnp.float32
    )
    o_ref[0] = product[:, :block]
    o_ref[1] = product[:, block:]


def _adjoint_kernel(cols_ref, counts_ref, u_ref, m_ref, o_ref):
    freq = pl.program_id(0)
    row = pl.program_id(1)
    rows = pl.num_programs(1)
    depth, width = m_ref.shape
    block = depth // 2
    slots = width // depth
    index = freq * rows + row
    count = counts_ref[index]

    @pl.when(row == 0)
    def _():
        o_ref[...] = jnp.zeros(o_ref.shape, o_ref.dtype)

    field = jnp.concatenate([u_ref[0], u_ref[1]], axis=1)
    for slot in range(slots):

        @pl.when(slot < count)
        def _():
            start = pl.multiple_of(cols_ref[index * slots + slot] * block, block)
            weights = m_ref[:, slot * depth : (slot + 1) * depth]
            product = jnp.dot(field, weights, preferred_element_type=jnp.float32)
            for part in range(2):
                o_ref[part, :, pl.ds(start, block)] += product[:, part * block : (part + 1) * block]


def _both_kernel(
    cols_ref, counts_ref, coef_ref, x_ref, q_ref, u_ref, m_ref, p_ref, o_ref, acc_ref
):
    freq = pl.program_id(0)
    row = pl.program_id(1)
    rows = pl.num_programs(1)
    depth, width = m_ref.shape
    block = depth // 2
    slots = width // depth
    index = freq * rows + row
    count = counts_ref[index]

    @pl.when(row == 0)
    def _():
        o_ref[...] = jnp.zeros(o_ref.shape, o_ref.dtype)

    acc_ref[...] = jnp.zeros(acc_ref.shape, acc_ref.dtype)
    contract = (((1,), (1,)), ((), ()))
    for slot in range(slots):

        @pl.when(slot < count)
        def _():
            start = pl.multiple_of(cols_ref[index * slots + slot] * block, block)
            picked = jnp.concatenate(
                [x_ref[0, :, pl.ds(start, block)], x_ref[1, :, pl.ds(start, block)]], axis=1
            )
            weights = m_ref[:, slot * depth : (slot + 1) * depth]
            acc_ref[...] += lax.dot_general(
                picked, weights, contract, preferred_element_type=jnp.float32
            )

    scale = coef_ref[2 * freq]
    shift = coef_ref[2 * freq + 1]
    for part in range(2):
        lanes = slice(part * block, (part + 1) * block)
        p_ref[part] = (q_ref[part] + acc_ref[:, lanes]) / scale - shift * u_ref[part]
    field = jnp.concatenate(
        [p_ref[0].astype(jnp.bfloat16), p_ref[1].astype(jnp.bfloat16)], axis=1
    )
    for slot in range(slots):

        @pl.when(slot < count)
        def _():
            start = pl.multiple_of(cols_ref[index * slots + slot] * block, block)
            weights = m_ref[:, slot * depth : (slot + 1) * depth]
            product = jnp.dot(field, weights, preferred_element_type=jnp.float32)
            for part in range(2):
                o_ref[part, :, pl.ds(start, block)] += product[:, part * block : (part + 1) * block]


def apply_both(extended, raw, left, coefs, stacked, cols, counts):
    local_freqs, local_blocks, depth, width = stacked.shape
    block_size = depth // 2
    _, _, sources, span = extended.shape
    own = pl.BlockSpec((2, None, sources, block_size), lambda f, r, c, n: (0, f, 0, r))
    grid_spec = pltpu.PrefetchScalarGridSpec(
        num_scalar_prefetch=2,
        grid=(local_freqs, local_blocks),
        in_specs=[
            pl.BlockSpec(memory_space=pltpu.SMEM),
            pl.BlockSpec((2, None, sources, span), lambda f, r, c, n: (0, f, 0, 0)),
            own,
            own,
            pl.BlockSpec((None, None, depth, width), lambda f, r, c, n: (f, r, 0, 0)),
        ],
        out_specs=[
            own,
            pl.BlockSpec((2, None, sources, span), lambda f, r, c, n: (0, f, 0, 0)),
        ],
        scratch_shapes=[pltpu.VMEM((sources, depth), jnp.float32)],
    )
    return pl.pallas_call(
        _both_kernel,
        grid_spec=grid_spec,
        out_shape=[
            jax.ShapeDtypeStruct(raw.shape, jnp.float32),
            jax.ShapeDtypeStruct((2, local_freqs, sources, span), jnp.float32),
        ],
        compiler_params=pltpu.CompilerParams(dimension_semantics=("arbitrary", "arbitrary")),
        cost_estimate=pl.CostEstimate(
            flops=4 * local_freqs * local_blocks * sources * depth * width,
            transcendentals=0,
            bytes_accessed=stacked.size * 2 + extended.size * 2 + raw.size * 40,
        ),
    )(cols, counts, coefs, extended, raw, left, stacked)


def apply_forward(extended, stacked, cols, counts):
    local_freqs, local_blocks, depth, width = stacked.shape
    block_size = depth // 2
    _, _, sources, span = extended.shape
    grid_spec = pltpu.PrefetchScalarGridSpec(
        num_scalar_prefetch=2,
        grid=(local_freqs, local_blocks),
        in_specs=[
            pl.BlockSpec((2, None, sources, span), lambda f, r, c, n: (0, f, 0, 0)),
            pl.BlockSpec((None, None, depth, width), lambda f, r, c, n: (f, r, 0, 0)),
        ],
        out_specs=pl.BlockSpec((2, None, sources, block_size), lambda f, r, c, n: (0, f, 0, r)),
        scratch_shapes=[pltpu.VMEM((sources, width), jnp.bfloat16)],
    )
    return pl.pallas_call(
        _forward_kernel,
        grid_spec=grid_spec,
        out_shape=jax.ShapeDtypeStruct(
            (2, local_freqs, sources, local_blocks * block_size), jnp.float32
        ),
        compiler_params=pltpu.CompilerParams(dimension_semantics=("arbitrary", "arbitrary")),
        cost_estimate=pl.CostEstimate(
            flops=2 * local_freqs * local_blocks * sources * depth * width,
            transcendentals=0,
            bytes_accessed=stacked.size * 2 + extended.size * 2 + extended.size * 4,
        ),
    )(cols, counts, extended, stacked)


def apply_adjoint(rounded, stacked, cols, counts, span):
    local_freqs, local_blocks, depth, width = stacked.shape
    block_size = depth // 2
    sources = rounded.shape[2]
    grid_spec = pltpu.PrefetchScalarGridSpec(
        num_scalar_prefetch=2,
        grid=(local_freqs, local_blocks),
        in_specs=[
            pl.BlockSpec((2, None, sources, block_size), lambda f, r, c, n: (0, f, 0, r)),
            pl.BlockSpec((None, None, depth, width), lambda f, r, c, n: (f, r, 0, 0)),
        ],
        out_specs=pl.BlockSpec((2, None, sources, span), lambda f, r, c, n: (0, f, 0, 0)),
    )
    return pl.pallas_call(
        _adjoint_kernel,
        grid_spec=grid_spec,
        out_shape=jax.ShapeDtypeStruct((2, local_freqs, sources, span), jnp.float32),
        compiler_params=pltpu.CompilerParams(dimension_semantics=("arbitrary", "arbitrary")),
        cost_estimate=pl.CostEstimate(
            flops=2 * local_freqs * local_blocks * sources * depth * width,
            transcendentals=0,
            bytes_accessed=stacked.size * 2 + rounded.size * 2 + rounded.size * 12,
        ),
    )(cols, counts, rounded, stacked)


def body(up_time, down_blocks, block_cols, block_counts):
    freq_groups = lax.axis_size("freq")
    receiver_groups = lax.axis_size("rcv")
    shot_count, time_steps, receivers = up_time.shape
    local_freqs, local_blocks, slot_count, _, block_size, _ = down_blocks.shape
    local_rows = receivers // receiver_groups
    reach_blocks = (slot_count - 1) // 2
    rim_rows = reach_blocks * block_size
    span_blocks = local_blocks + 2 * reach_blocks
    fourier = fourier_table(time_steps, freq_groups, local_freqs)
    spectrum = jnp.einsum(
        "snr,ncgf->cfsgr", up_time, fourier, preferred_element_type=jnp.float32
    ).astype(jnp.bfloat16)
    spectrum = spectrum.reshape(
        2, local_freqs, shot_count, freq_groups * receiver_groups, local_rows
    )
    received = lax.all_to_all(spectrum, ("freq", "rcv"), split_axis=3, concat_axis=2, tiled=True)
    right_side = received.reshape(2, local_freqs, -1, local_rows).astype(jnp.float32)
    position = lax.axis_index("rcv")
    columns = jnp.clip(
        block_cols - position * local_blocks + reach_blocks, 0, span_blocks - 1
    ).reshape(-1)
    counts = jnp.clip(block_counts, 0, slot_count).reshape(-1)
    stacked = stack_blocks(down_blocks)

    def exchange(spread):
        lower_rim = spread[..., :rim_rows]
        middle = spread[..., rim_rows : rim_rows + local_rows]
        upper_rim = spread[..., rim_rows + local_rows :]
        from_above = from_behind(lower_rim, "rcv", -1)
        from_below = from_behind(upper_rim, "rcv", 1)
        middle = middle.at[..., :rim_rows].add(from_below)
        middle = middle.at[..., local_rows - rim_rows :].add(from_above)
        return middle

    def adjoint(field):
        rounded = field.astype(jnp.bfloat16)
        spread = apply_adjoint(rounded, stacked, columns, counts, span_blocks * block_size)
        return field + exchange(spread)

    def forward_adjoint(raw, scale, left, shift):
        extended = with_halo(raw.astype(jnp.bfloat16), (("rcv", 3),), rim_rows)
        coefs = jnp.stack(
            [jnp.broadcast_to(scale, shift.shape).reshape(-1), shift.reshape(-1)], axis=1
        ).reshape(-1)
        residual, spread = apply_both(extended, raw, left, coefs, stacked, columns, counts)
        return residual, residual + exchange(spread)

    def forward(field):
        extended = with_halo(field.astype(jnp.bfloat16), (("rcv", 3),), rim_rows)
        return field + apply_forward(extended, stacked, columns, counts)

    lifted = adjoint(right_side)
    right_squares, lifted_squares = both_squares(right_side, lifted)
    beta_norm = jnp.sqrt(right_squares + EPSILON)
    alpha_norm = jnp.sqrt(lifted_squares / (beta_norm * beta_norm) + EPSILON)
    left_vector = right_side / beta_norm
    right_raw = lifted
    right_scale = beta_norm * alpha_norm
    right_vector = right_raw / right_scale
    search_direction = right_vector
    solution = jnp.zeros_like(right_side)
    phibar = beta_norm
    rhobar = alpha_norm
    for iteration in range(ITERS):
        last = iteration == ITERS - 1
        residual_left, lifted = forward_adjoint(right_raw, right_scale, left_vector, alpha_norm)
        beta_norm = jnp.sqrt(squares(residual_left) + EPSILON)
        left_vector = residual_left / beta_norm
        residual_right = lifted / beta_norm - beta_norm * right_vector
        rho_value = jnp.sqrt(rhobar * rhobar + beta_norm * beta_norm)
        cosine = rhobar / rho_value
        sine_value = beta_norm / rho_value
        phi_value = cosine * phibar
        phibar = sine_value * phibar
        solution = solution + phi_value / rho_value * search_direction
        if last:
            break
        alpha_norm = jnp.sqrt(squares(residual_right) + EPSILON)
        right_raw = residual_right
        right_scale = alpha_norm
        right_vector = residual_right / alpha_norm
        theta_value = sine_value * alpha_norm
        rhobar = -cosine * alpha_norm
        search_direction = right_vector - theta_value / rho_value * search_direction
    return (solution, phibar * cosine * residual_right)


def solution(mesh):
    return jax.shard_map(
        body,
        mesh=mesh,
        in_specs=(
            P(("freq", "rcv"), None, None),
            P("freq", "rcv", None, None, None, None),
            P("freq", "rcv", None),
            P("freq", "rcv"),
        ),
        out_specs=(P(None, "freq", None, "rcv"), P(None, "freq", None, "rcv")),
        check_vma=False,
    )
```

```python
import math

import jax
import jax.numpy as jnp
from jax import lax
from jax.experimental import pallas as pl
from jax.experimental.pallas import tpu as pltpu
from jax.sharding import PartitionSpec as P

ITERS = 2


EPSILON = 1e-06


def with_halo(cells, sides, width):
    for axis, dim in sides:
        count = lax.axis_size(axis)
        ends = count - 1
        head = lax.slice_in_dim(cells, 0, width, axis=dim)
        tail = lax.slice_in_dim(cells, cells.shape[dim] - width, cells.shape[dim], axis=dim)
        cells = jnp.concatenate(
            [
                lax.ppermute(tail, axis, [(i, (i + 1) % count) for i in range(ends)]),
                cells,
                lax.ppermute(head, axis, [((i + 1) % count, i) for i in range(ends)]),
            ],
            axis=dim,
        )
    return cells


def from_behind(value, axis, steps):
    count = lax.axis_size(axis)
    first, last = (max(0, -steps), min(count, count - steps))
    return lax.ppermute(value, axis, [(source, source + steps) for source in range(first, last)])


def fourier_table(time_steps, freq_groups, local_freqs):
    shape = (time_steps, freq_groups, local_freqs)
    sample = lax.broadcasted_iota(jnp.int32, shape, 0)
    harmonic = (
        lax.broadcasted_iota(jnp.int32, shape, 1) * local_freqs
        + lax.broadcasted_iota(jnp.int32, shape, 2)
        + 1
    )
    phase_angle = 2.0 * math.pi / time_steps * (harmonic * sample % time_steps).astype(jnp.float32)
    scale_factor = 1.0 / math.sqrt(time_steps)
    return jnp.stack(
        [jnp.cos(phase_angle) * scale_factor, -jnp.sin(phase_angle) * scale_factor], axis=1
    ).astype(jnp.bfloat16)


def rcv_sum(partial):
    count = lax.axis_size("rcv")
    spread = jnp.broadcast_to(partial[None], (count,) + partial.shape)
    gathered = lax.all_to_all(spread, "rcv", 0, 0, tiled=False)
    return jnp.sum(gathered, axis=0)


def squares(field):
    return rcv_sum(jnp.sum(field * field, axis=(0, 2, 3)))[None, :, None, None]


def both_squares(first, second):
    partial = jnp.stack(
        [jnp.sum(first * first, axis=(0, 2, 3)), jnp.sum(second * second, axis=(0, 2, 3))]
    )
    total = rcv_sum(partial)
    return total[0][None, :, None, None], total[1][None, :, None, None]


def _stack_kernel(counts_ref, a_ref, m_ref):
    slots, _, block, _ = a_ref.shape
    count = counts_ref[pl.program_id(0) * pl.num_programs(1) + pl.program_id(1)]
    for slot in range(slots):
        live = slot < count
        real_part = jnp.where(live, a_ref[slot, 0], jnp.zeros_like(a_ref[slot, 0]))
        imaginary = jnp.where(live, a_ref[slot, 1], jnp.zeros_like(a_ref[slot, 1]))
        left = slice(2 * slot * block, (2 * slot + 1) * block)
        right = slice((2 * slot + 1) * block, (2 * slot + 2) * block)
        m_ref[:block, left] = real_part
        m_ref[:block, right] = -imaginary
        m_ref[block:, left] = imaginary
        m_ref[block:, right] = real_part


def stack_blocks(down_blocks, counts):
    local_freqs, local_blocks, slot_count, _, block_size, _ = down_blocks.shape
    width = 2 * slot_count * block_size
    grid_spec = pltpu.PrefetchScalarGridSpec(
        num_scalar_prefetch=1,
        grid=(local_freqs, local_blocks),
        in_specs=[
            pl.BlockSpec(
                (None, None, slot_count, 2, block_size, block_size),
                lambda f, r, n: (f, r, 0, 0, 0, 0),
            )
        ],
        out_specs=pl.BlockSpec(
            (None, None, 2 * block_size, width), lambda f, r, n: (f, r, 0, 0)
        ),
    )
    return pl.pallas_call(
        _stack_kernel,
        grid_spec=grid_spec,
        out_shape=jax.ShapeDtypeStruct(
            (local_freqs, local_blocks, 2 * block_size, width), jnp.bfloat16
        ),
    )(counts, down_blocks)


def _forward_kernel(cols_ref, counts_ref, x_ref, m_ref, o_ref, picked_ref):
    freq = pl.program_id(0)
    row = pl.program_id(1)
    rows = pl.num_programs(1)
    depth, width = m_ref.shape
    block = depth // 2
    slots = width // depth
    index = freq * rows + row
    count = counts_ref[index]
    for slot in range(slots):
        start = pl.multiple_of(cols_ref[index * slots + slot] * block, block)
        for part in range(2):
            taken = x_ref[part, :, pl.ds(start, block)]
            lanes = slice((2 * slot + part) * block, (2 * slot + part + 1) * block)
            picked_ref[:, lanes] = jnp.where(slot < count, taken, jnp.zeros_like(taken))
    contract = (((1,), (1,)), ((), ()))
    product = lax.dot_general(
        picked_ref[...], m_ref[...], contract, preferred_element_type=jnp.float32
    )
    o_ref[0] = product[:, :block]
    o_ref[1] = product[:, block:]


def _scatter(cols_ref, index, field, m_ref, acc_ref):
    depth, width = m_ref.shape
    block = depth // 2
    slots = width // depth
    spread = jnp.dot(field, m_ref[...], preferred_element_type=jnp.float32)
    for slot in range(slots):
        start = pl.multiple_of(cols_ref[index * slots + slot] * block, block)
        for part in range(2):
            lanes = slice((2 * slot + part) * block, (2 * slot + part + 1) * block)
            acc_ref[part, :, pl.ds(start, block)] += spread[:, lanes]


def _split(acc_ref, lower_ref, middle_ref, upper_ref):
    rim = lower_ref.shape[-1]
    own = middle_ref.shape[-1]
    lower_ref[...] = acc_ref[:, :, :rim]
    middle_ref[...] = acc_ref[:, :, rim : rim + own]
    upper_ref[...] = acc_ref[:, :, rim + own :]


def _adjoint_kernel(cols_ref, counts_ref, u_ref, m_ref, lower_ref, middle_ref, upper_ref, acc_ref):
    freq = pl.program_id(0)
    row = pl.program_id(1)
    rows = pl.num_programs(1)

    @pl.when(row == 0)
    def _():
        acc_ref[...] = jnp.zeros(acc_ref.shape, acc_ref.dtype)

    field = jnp.concatenate([u_ref[0], u_ref[1]], axis=1)
    _scatter(cols_ref, freq * rows + row, field, m_ref, acc_ref)

    @pl.when(row == rows - 1)
    def _():
        _split(acc_ref, lower_ref, middle_ref, upper_ref)


def _both_kernel(
    cols_ref,
    counts_ref,
    coef_ref,
    x_ref,
    q_ref,
    u_ref,
    m_ref,
    p_ref,
    lower_ref,
    middle_ref,
    upper_ref,
    picked_ref,
    acc_ref,
):
    freq = pl.program_id(0)
    row = pl.program_id(1)
    rows = pl.num_programs(1)
    depth, width = m_ref.shape
    block = depth // 2
    slots = width // depth
    index = freq * rows + row

    @pl.when(row == 0)
    def _():
        acc_ref[...] = jnp.zeros(acc_ref.shape, acc_ref.dtype)

    for slot in range(slots):
        start = pl.multiple_of(cols_ref[index * slots + slot] * block, block)
        for part in range(2):
            lanes = slice((2 * slot + part) * block, (2 * slot + part + 1) * block)
            picked_ref[:, lanes] = x_ref[part, :, pl.ds(start, block)]
    contract = (((1,), (1,)), ((), ()))
    product = lax.dot_general(
        picked_ref[...], m_ref[...], contract, preferred_element_type=jnp.float32
    )
    scale = coef_ref[2 * freq]
    shift = coef_ref[2 * freq + 1]
    for part in range(2):
        lanes = slice(part * block, (part + 1) * block)
        p_ref[part] = (q_ref[part] + product[:, lanes]) / scale - shift * u_ref[part]
    field = jnp.concatenate(
        [p_ref[0].astype(jnp.bfloat16), p_ref[1].astype(jnp.bfloat16)], axis=1
    )
    _scatter(cols_ref, index, field, m_ref, acc_ref)

    @pl.when(row == rows - 1)
    def _():
        _split(acc_ref, lower_ref, middle_ref, upper_ref)


def _part_specs(local_freqs, sources):
    def part_spec(lanes):
        return pl.BlockSpec((2, None, sources, lanes), lambda f, r, c, n: (0, f, 0, 0))

    def part_shape(lanes):
        return jax.ShapeDtypeStruct((2, local_freqs, sources, lanes), jnp.float32)

    return part_spec, part_shape


def apply_both(extended, raw, left, coefs, stacked, cols, counts):
    local_freqs, local_blocks, depth, width = stacked.shape
    block_size = depth // 2
    _, _, sources, span = extended.shape
    own_rows = local_blocks * block_size
    rim = (span - own_rows) // 2
    part_spec, part_shape = _part_specs(local_freqs, sources)
    own = pl.BlockSpec((2, None, sources, block_size), lambda f, r, c, n: (0, f, 0, r))
    grid_spec = pltpu.PrefetchScalarGridSpec(
        num_scalar_prefetch=2,
        grid=(local_freqs, local_blocks),
        in_specs=[
            pl.BlockSpec(memory_space=pltpu.SMEM),
            pl.BlockSpec((2, None, sources, span), lambda f, r, c, n: (0, f, 0, 0)),
            own,
            own,
            pl.BlockSpec((None, None, depth, width), lambda f, r, c, n: (f, r, 0, 0)),
        ],
        out_specs=[own, part_spec(rim), part_spec(own_rows), part_spec(rim)],
        scratch_shapes=[
            pltpu.VMEM((sources, width), jnp.bfloat16),
            pltpu.VMEM((2, sources, span), jnp.float32),
        ],
    )
    return pl.pallas_call(
        _both_kernel,
        grid_spec=grid_spec,
        out_shape=[
            jax.ShapeDtypeStruct(raw.shape, jnp.float32),
            part_shape(rim),
            part_shape(own_rows),
            part_shape(rim),
        ],
        compiler_params=pltpu.CompilerParams(dimension_semantics=("arbitrary", "arbitrary")),
        cost_estimate=pl.CostEstimate(
            flops=4 * local_freqs * local_blocks * sources * depth * width,
            transcendentals=0,
            bytes_accessed=stacked.size * 2 + extended.size * 2 + raw.size * 40,
        ),
    )(cols, counts, coefs, extended, raw, left, stacked)


def apply_forward(extended, stacked, cols, counts):
    local_freqs, local_blocks, depth, width = stacked.shape
    block_size = depth // 2
    _, _, sources, span = extended.shape
    grid_spec = pltpu.PrefetchScalarGridSpec(
        num_scalar_prefetch=2,
        grid=(local_freqs, local_blocks),
        in_specs=[
            pl.BlockSpec((2, None, sources, span), lambda f, r, c, n: (0, f, 0, 0)),
            pl.BlockSpec((None, None, depth, width), lambda f, r, c, n: (f, r, 0, 0)),
        ],
        out_specs=pl.BlockSpec((2, None, sources, block_size), lambda f, r, c, n: (0, f, 0, r)),
        scratch_shapes=[pltpu.VMEM((sources, width), jnp.bfloat16)],
    )
    return pl.pallas_call(
        _forward_kernel,
        grid_spec=grid_spec,
        out_shape=jax.ShapeDtypeStruct(
            (2, local_freqs, sources, local_blocks * block_size), jnp.float32
        ),
        compiler_params=pltpu.CompilerParams(dimension_semantics=("arbitrary", "arbitrary")),
        cost_estimate=pl.CostEstimate(
            flops=2 * local_freqs * local_blocks * sources * depth * width,
            transcendentals=0,
            bytes_accessed=stacked.size * 2 + extended.size * 2 + extended.size * 4,
        ),
    )(cols, counts, extended, stacked)


def apply_adjoint(rounded, stacked, cols, counts, span):
    local_freqs, local_blocks, depth, width = stacked.shape
    block_size = depth // 2
    sources = rounded.shape[2]
    own = local_blocks * block_size
    rim = (span - own) // 2
    part_spec, part_shape = _part_specs(local_freqs, sources)
    grid_spec = pltpu.PrefetchScalarGridSpec(
        num_scalar_prefetch=2,
        grid=(local_freqs, local_blocks),
        in_specs=[
            pl.BlockSpec((2, None, sources, block_size), lambda f, r, c, n: (0, f, 0, r)),
            pl.BlockSpec((None, None, depth, width), lambda f, r, c, n: (f, r, 0, 0)),
        ],
        out_specs=[part_spec(rim), part_spec(own), part_spec(rim)],
        scratch_shapes=[pltpu.VMEM((2, sources, span), jnp.float32)],
    )
    return pl.pallas_call(
        _adjoint_kernel,
        grid_spec=grid_spec,
        out_shape=[part_shape(rim), part_shape(own), part_shape(rim)],
        compiler_params=pltpu.CompilerParams(dimension_semantics=("arbitrary", "arbitrary")),
        cost_estimate=pl.CostEstimate(
            flops=2 * local_freqs * local_blocks * sources * depth * width,
            transcendentals=0,
            bytes_accessed=stacked.size * 2 + rounded.size * 2 + rounded.size * 12,
        ),
    )(cols, counts, rounded, stacked)


def body(up_time, down_blocks, block_cols, block_counts):
    freq_groups = lax.axis_size("freq")
    receiver_groups = lax.axis_size("rcv")
    shot_count, time_steps, receivers = up_time.shape
    local_freqs, local_blocks, slot_count, _, block_size, _ = down_blocks.shape
    local_rows = receivers // receiver_groups
    reach_blocks = (slot_count - 1) // 2
    rim_rows = reach_blocks * block_size
    span_blocks = local_blocks + 2 * reach_blocks
    fourier = fourier_table(time_steps, freq_groups, local_freqs)
    spectrum = jnp.einsum(
        "snr,ncgf->cfsgr", up_time, fourier, preferred_element_type=jnp.float32
    ).astype(jnp.bfloat16)
    spectrum = spectrum.reshape(
        2, local_freqs, shot_count, freq_groups * receiver_groups, local_rows
    )
    received = lax.all_to_all(spectrum, ("freq", "rcv"), split_axis=3, concat_axis=2, tiled=True)
    right_side = received.reshape(2, local_freqs, -1, local_rows).astype(jnp.float32)
    position = lax.axis_index("rcv")
    columns = jnp.clip(
        block_cols - position * local_blocks + reach_blocks, 0, span_blocks - 1
    ).reshape(-1)
    counts = jnp.clip(block_counts, 0, slot_count).reshape(-1)
    stacked = stack_blocks(down_blocks, counts)

    def exchange(lower_rim, middle, upper_rim):
        from_above = from_behind(lower_rim, "rcv", -1)
        from_below = from_behind(upper_rim, "rcv", 1)
        middle = middle.at[..., :rim_rows].add(from_below)
        middle = middle.at[..., local_rows - rim_rows :].add(from_above)
        return middle

    def adjoint(field):
        rounded = field.astype(jnp.bfloat16)
        parts = apply_adjoint(rounded, stacked, columns, counts, span_blocks * block_size)
        return field + exchange(*parts)

    def forward_adjoint(raw, scale, left, shift):
        extended = with_halo(raw.astype(jnp.bfloat16), (("rcv", 3),), rim_rows)
        coefs = jnp.stack(
            [jnp.broadcast_to(scale, shift.shape).reshape(-1), shift.reshape(-1)], axis=1
        ).reshape(-1)
        residual, *parts = apply_both(extended, raw, left, coefs, stacked, columns, counts)
        return residual, residual + exchange(*parts)

    def forward(field):
        extended = with_halo(field.astype(jnp.bfloat16), (("rcv", 3),), rim_rows)
        return field + apply_forward(extended, stacked, columns, counts)

    lifted = adjoint(right_side)
    right_squares, lifted_squares = both_squares(right_side, lifted)
    beta_norm = jnp.sqrt(right_squares + EPSILON)
    alpha_norm = jnp.sqrt(lifted_squares / (beta_norm * beta_norm) + EPSILON)
    left_vector = right_side / beta_norm
    right_raw = lifted
    right_scale = beta_norm * alpha_norm
    right_vector = right_raw / right_scale
    search_direction = right_vector
    solution = jnp.zeros_like(right_side)
    phibar = beta_norm
    rhobar = alpha_norm
    for iteration in range(ITERS):
        last = iteration == ITERS - 1
        residual_left, lifted = forward_adjoint(right_raw, right_scale, left_vector, alpha_norm)
        beta_norm = jnp.sqrt(squares(residual_left) + EPSILON)
        left_vector = residual_left / beta_norm
        residual_right = lifted / beta_norm - beta_norm * right_vector
        rho_value = jnp.sqrt(rhobar * rhobar + beta_norm * beta_norm)
        cosine = rhobar / rho_value
        sine_value = beta_norm / rho_value
        phi_value = cosine * phibar
        phibar = sine_value * phibar
        solution = solution + phi_value / rho_value * search_direction
        if last:
            break
        alpha_norm = jnp.sqrt(squares(residual_right) + EPSILON)
        right_raw = residual_right
        right_scale = alpha_norm
        right_vector = residual_right / alpha_norm
        theta_value = sine_value * alpha_norm
        rhobar = -cosine * alpha_norm
        search_direction = right_vector - theta_value / rho_value * search_direction
    return (solution, phibar * cosine * residual_right)


def solution(mesh):
    return jax.shard_map(
        body,
        mesh=mesh,
        in_specs=(
            P(("freq", "rcv"), None, None),
            P("freq", "rcv", None, None, None, None),
            P("freq", "rcv", None),
            P("freq", "rcv"),
        ),
        out_specs=(P(None, "freq", None, "rcv"), P(None, "freq", None, "rcv")),
        check_vma=False,
    )
```

```python
import math

import jax
import jax.numpy as jnp
from jax import lax
from jax.experimental import pallas as pl
from jax.experimental.pallas import tpu as pltpu
from jax.sharding import PartitionSpec as P

ITERS = 2


EPSILON = 1e-06


def with_halo(cells, sides, width):
    for axis, dim in sides:
        count = lax.axis_size(axis)
        ends = count - 1
        head = lax.slice_in_dim(cells, 0, width, axis=dim)
        tail = lax.slice_in_dim(cells, cells.shape[dim] - width, cells.shape[dim], axis=dim)
        cells = jnp.concatenate(
            [
                lax.ppermute(tail, axis, [(i, (i + 1) % count) for i in range(ends)]),
                cells,
                lax.ppermute(head, axis, [((i + 1) % count, i) for i in range(ends)]),
            ],
            axis=dim,
        )
    return cells


def from_behind(value, axis, steps):
    count = lax.axis_size(axis)
    first, last = (max(0, -steps), min(count, count - steps))
    return lax.ppermute(value, axis, [(source, source + steps) for source in range(first, last)])


def fourier_table(time_steps, freq_groups, local_freqs):
    shape = (time_steps, freq_groups, local_freqs)
    sample = lax.broadcasted_iota(jnp.int32, shape, 0)
    harmonic = (
        lax.broadcasted_iota(jnp.int32, shape, 1) * local_freqs
        + lax.broadcasted_iota(jnp.int32, shape, 2)
        + 1
    )
    phase_angle = 2.0 * math.pi / time_steps * (harmonic * sample % time_steps).astype(jnp.float32)
    scale_factor = 1.0 / math.sqrt(time_steps)
    return jnp.stack(
        [jnp.cos(phase_angle) * scale_factor, -jnp.sin(phase_angle) * scale_factor], axis=1
    ).astype(jnp.bfloat16)


def rcv_sum(partial):
    count = lax.axis_size("rcv")
    spread = jnp.broadcast_to(partial[None], (count,) + partial.shape)
    gathered = lax.all_to_all(spread, "rcv", 0, 0, tiled=False)
    return jnp.sum(gathered, axis=0)


def squares(field):
    return rcv_sum(jnp.sum(field * field, axis=(0, 2, 3)))[None, :, None, None]


def both_squares(first, second):
    partial = jnp.stack(
        [jnp.sum(first * first, axis=(0, 2, 3)), jnp.sum(second * second, axis=(0, 2, 3))]
    )
    total = rcv_sum(partial)
    return total[0][None, :, None, None], total[1][None, :, None, None]


def _stack_kernel(counts_ref, a_ref, m_ref):
    count = counts_ref[pl.program_id(0) * pl.num_programs(1) + pl.program_id(1)]
    _build(count, a_ref, m_ref)


def _build(count, a_ref, m_ref):
    slots, _, block, _ = a_ref.shape
    for slot in range(slots):
        live = slot < count
        real_part = jnp.where(live, a_ref[slot, 0], jnp.zeros_like(a_ref[slot, 0]))
        imaginary = jnp.where(live, a_ref[slot, 1], jnp.zeros_like(a_ref[slot, 1]))
        left = slice(2 * slot * block, (2 * slot + 1) * block)
        right = slice((2 * slot + 1) * block, (2 * slot + 2) * block)
        m_ref[:block, left] = real_part
        m_ref[:block, right] = -imaginary
        m_ref[block:, left] = imaginary
        m_ref[block:, right] = real_part


def stack_blocks(down_blocks, counts):
    local_freqs, local_blocks, slot_count, _, block_size, _ = down_blocks.shape
    width = 2 * slot_count * block_size
    grid_spec = pltpu.PrefetchScalarGridSpec(
        num_scalar_prefetch=1,
        grid=(local_freqs, local_blocks),
        in_specs=[
            pl.BlockSpec(
                (None, None, slot_count, 2, block_size, block_size),
                lambda f, r, n: (f, r, 0, 0, 0, 0),
            )
        ],
        out_specs=pl.BlockSpec(
            (None, None, 2 * block_size, width), lambda f, r, n: (f, r, 0, 0)
        ),
    )
    return pl.pallas_call(
        _stack_kernel,
        grid_spec=grid_spec,
        out_shape=jax.ShapeDtypeStruct(
            (local_freqs, local_blocks, 2 * block_size, width), jnp.bfloat16
        ),
    )(counts, down_blocks)


def _forward_kernel(cols_ref, counts_ref, x_ref, m_ref, o_ref, picked_ref):
    freq = pl.program_id(0)
    row = pl.program_id(1)
    rows = pl.num_programs(1)
    depth, width = m_ref.shape
    block = depth // 2
    slots = width // depth
    index = freq * rows + row
    count = counts_ref[index]
    for slot in range(slots):
        start = pl.multiple_of(cols_ref[index * slots + slot] * block, block)
        for part in range(2):
            taken = x_ref[part, :, pl.ds(start, block)]
            lanes = slice((2 * slot + part) * block, (2 * slot + part + 1) * block)
            picked_ref[:, lanes] = jnp.where(slot < count, taken, jnp.zeros_like(taken))
    contract = (((1,), (1,)), ((), ()))
    product = lax.dot_general(
        picked_ref[...], m_ref[...], contract, preferred_element_type=jnp.float32
    )
    o_ref[0] = product[:, :block]
    o_ref[1] = product[:, block:]


def _scatter(cols_ref, index, field, m_ref, acc_ref):
    depth, width = m_ref.shape
    block = depth // 2
    slots = width // depth
    spread = jnp.dot(field, m_ref[...], preferred_element_type=jnp.float32)
    for slot in range(slots):
        start = pl.multiple_of(cols_ref[index * slots + slot] * block, block)
        for part in range(2):
            lanes = slice((2 * slot + part) * block, (2 * slot + part + 1) * block)
            acc_ref[part, :, pl.ds(start, block)] += spread[:, lanes]


def _split(acc_ref, lower_ref, middle_ref, upper_ref):
    rim = lower_ref.shape[-1]
    own = middle_ref.shape[-1]
    lower_ref[...] = acc_ref[:, :, :rim]
    middle_ref[...] = acc_ref[:, :, rim : rim + own]
    upper_ref[...] = acc_ref[:, :, rim + own :]


def _adjoint_kernel(cols_ref, counts_ref, u_ref, m_ref, lower_ref, middle_ref, upper_ref, acc_ref):
    freq = pl.program_id(0)
    row = pl.program_id(1)
    rows = pl.num_programs(1)

    @pl.when(row == 0)
    def _():
        acc_ref[...] = jnp.zeros(acc_ref.shape, acc_ref.dtype)

    field = jnp.concatenate([u_ref[0], u_ref[1]], axis=1)
    _scatter(cols_ref, freq * rows + row, field, m_ref, acc_ref)

    @pl.when(row == rows - 1)
    def _():
        _split(acc_ref, lower_ref, middle_ref, upper_ref)


def _first_kernel(
    cols_ref, counts_ref, u_ref, a_ref, m_ref, lower_ref, middle_ref, upper_ref, acc_ref
):
    freq = pl.program_id(0)
    row = pl.program_id(1)
    rows = pl.num_programs(1)
    index = freq * rows + row

    @pl.when(row == 0)
    def _():
        acc_ref[...] = jnp.zeros(acc_ref.shape, acc_ref.dtype)

    _build(counts_ref[index], a_ref, m_ref)
    field = jnp.concatenate([u_ref[0], u_ref[1]], axis=1)
    _scatter(cols_ref, index, field, m_ref, acc_ref)

    @pl.when(row == rows - 1)
    def _():
        _split(acc_ref, lower_ref, middle_ref, upper_ref)


def apply_first(rounded, down_blocks, cols, counts, span):
    local_freqs, local_blocks, slot_count, _, block_size, _ = down_blocks.shape
    depth = 2 * block_size
    width = 2 * slot_count * block_size
    sources = rounded.shape[2]
    own = local_blocks * block_size
    rim = (span - own) // 2
    part_spec, part_shape = _part_specs(local_freqs, sources)
    grid_spec = pltpu.PrefetchScalarGridSpec(
        num_scalar_prefetch=2,
        grid=(local_freqs, local_blocks),
        in_specs=[
            pl.BlockSpec((2, None, sources, block_size), lambda f, r, c, n: (0, f, 0, r)),
            pl.BlockSpec(
                (None, None, slot_count, 2, block_size, block_size),
                lambda f, r, c, n: (f, r, 0, 0, 0, 0),
            ),
        ],
        out_specs=[
            pl.BlockSpec((None, None, depth, width), lambda f, r, c, n: (f, r, 0, 0)),
            part_spec(rim),
            part_spec(own),
            part_spec(rim),
        ],
        scratch_shapes=[pltpu.VMEM((2, sources, span), jnp.float32)],
    )
    return pl.pallas_call(
        _first_kernel,
        grid_spec=grid_spec,
        out_shape=[
            jax.ShapeDtypeStruct((local_freqs, local_blocks, depth, width), jnp.bfloat16),
            part_shape(rim),
            part_shape(own),
            part_shape(rim),
        ],
        compiler_params=pltpu.CompilerParams(dimension_semantics=("arbitrary", "arbitrary")),
    )(cols, counts, rounded, down_blocks)


def _both_kernel(
    cols_ref,
    counts_ref,
    coef_ref,
    x_ref,
    q_ref,
    u_ref,
    m_ref,
    p_ref,
    lower_ref,
    middle_ref,
    upper_ref,
    picked_ref,
    acc_ref,
):
    freq = pl.program_id(0)
    row = pl.program_id(1)
    rows = pl.num_programs(1)
    depth, width = m_ref.shape
    block = depth // 2
    slots = width // depth
    index = freq * rows + row

    @pl.when(row == 0)
    def _():
        acc_ref[...] = jnp.zeros(acc_ref.shape, acc_ref.dtype)

    for slot in range(slots):
        start = pl.multiple_of(cols_ref[index * slots + slot] * block, block)
        for part in range(2):
            lanes = slice((2 * slot + part) * block, (2 * slot + part + 1) * block)
            picked_ref[:, lanes] = x_ref[part, :, pl.ds(start, block)]
    contract = (((1,), (1,)), ((), ()))
    product = lax.dot_general(
        picked_ref[...], m_ref[...], contract, preferred_element_type=jnp.float32
    )
    scale = coef_ref[2 * freq]
    shift = coef_ref[2 * freq + 1]
    for part in range(2):
        lanes = slice(part * block, (part + 1) * block)
        p_ref[part] = (q_ref[part] + product[:, lanes]) / scale - shift * u_ref[part]
    field = jnp.concatenate(
        [p_ref[0].astype(jnp.bfloat16), p_ref[1].astype(jnp.bfloat16)], axis=1
    )
    _scatter(cols_ref, index, field, m_ref, acc_ref)

    @pl.when(row == rows - 1)
    def _():
        _split(acc_ref, lower_ref, middle_ref, upper_ref)


def _part_specs(local_freqs, sources):
    def part_spec(lanes):
        return pl.BlockSpec((2, None, sources, lanes), lambda f, r, c, n: (0, f, 0, 0))

    def part_shape(lanes):
        return jax.ShapeDtypeStruct((2, local_freqs, sources, lanes), jnp.float32)

    return part_spec, part_shape


def apply_both(extended, raw, left, coefs, stacked, cols, counts):
    local_freqs, local_blocks, depth, width = stacked.shape
    block_size = depth // 2
    _, _, sources, span = extended.shape
    own_rows = local_blocks * block_size
    rim = (span - own_rows) // 2
    part_spec, part_shape = _part_specs(local_freqs, sources)
    own = pl.BlockSpec((2, None, sources, block_size), lambda f, r, c, n: (0, f, 0, r))
    grid_spec = pltpu.PrefetchScalarGridSpec(
        num_scalar_prefetch=2,
        grid=(local_freqs, local_blocks),
        in_specs=[
            pl.BlockSpec(memory_space=pltpu.SMEM),
            pl.BlockSpec((2, None, sources, span), lambda f, r, c, n: (0, f, 0, 0)),
            own,
            own,
            pl.BlockSpec((None, None, depth, width), lambda f, r, c, n: (f, r, 0, 0)),
        ],
        out_specs=[own, part_spec(rim), part_spec(own_rows), part_spec(rim)],
        scratch_shapes=[
            pltpu.VMEM((sources, width), jnp.bfloat16),
            pltpu.VMEM((2, sources, span), jnp.float32),
        ],
    )
    return pl.pallas_call(
        _both_kernel,
        grid_spec=grid_spec,
        out_shape=[
            jax.ShapeDtypeStruct(raw.shape, jnp.float32),
            part_shape(rim),
            part_shape(own_rows),
            part_shape(rim),
        ],
        compiler_params=pltpu.CompilerParams(dimension_semantics=("arbitrary", "arbitrary")),
        cost_estimate=pl.CostEstimate(
            flops=4 * local_freqs * local_blocks * sources * depth * width,
            transcendentals=0,
            bytes_accessed=stacked.size * 2 + extended.size * 2 + raw.size * 40,
        ),
    )(cols, counts, coefs, extended, raw, left, stacked)


def apply_forward(extended, stacked, cols, counts):
    local_freqs, local_blocks, depth, width = stacked.shape
    block_size = depth // 2
    _, _, sources, span = extended.shape
    grid_spec = pltpu.PrefetchScalarGridSpec(
        num_scalar_prefetch=2,
        grid=(local_freqs, local_blocks),
        in_specs=[
            pl.BlockSpec((2, None, sources, span), lambda f, r, c, n: (0, f, 0, 0)),
            pl.BlockSpec((None, None, depth, width), lambda f, r, c, n: (f, r, 0, 0)),
        ],
        out_specs=pl.BlockSpec((2, None, sources, block_size), lambda f, r, c, n: (0, f, 0, r)),
        scratch_shapes=[pltpu.VMEM((sources, width), jnp.bfloat16)],
    )
    return pl.pallas_call(
        _forward_kernel,
        grid_spec=grid_spec,
        out_shape=jax.ShapeDtypeStruct(
            (2, local_freqs, sources, local_blocks * block_size), jnp.float32
        ),
        compiler_params=pltpu.CompilerParams(dimension_semantics=("arbitrary", "arbitrary")),
        cost_estimate=pl.CostEstimate(
            flops=2 * local_freqs * local_blocks * sources * depth * width,
            transcendentals=0,
            bytes_accessed=stacked.size * 2 + extended.size * 2 + extended.size * 4,
        ),
    )(cols, counts, extended, stacked)


def apply_adjoint(rounded, stacked, cols, counts, span):
    local_freqs, local_blocks, depth, width = stacked.shape
    block_size = depth // 2
    sources = rounded.shape[2]
    own = local_blocks * block_size
    rim = (span - own) // 2
    part_spec, part_shape = _part_specs(local_freqs, sources)
    grid_spec = pltpu.PrefetchScalarGridSpec(
        num_scalar_prefetch=2,
        grid=(local_freqs, local_blocks),
        in_specs=[
            pl.BlockSpec((2, None, sources, block_size), lambda f, r, c, n: (0, f, 0, r)),
            pl.BlockSpec((None, None, depth, width), lambda f, r, c, n: (f, r, 0, 0)),
        ],
        out_specs=[part_spec(rim), part_spec(own), part_spec(rim)],
        scratch_shapes=[pltpu.VMEM((2, sources, span), jnp.float32)],
    )
    return pl.pallas_call(
        _adjoint_kernel,
        grid_spec=grid_spec,
        out_shape=[part_shape(rim), part_shape(own), part_shape(rim)],
        compiler_params=pltpu.CompilerParams(dimension_semantics=("arbitrary", "arbitrary")),
        cost_estimate=pl.CostEstimate(
            flops=2 * local_freqs * local_blocks * sources * depth * width,
            transcendentals=0,
            bytes_accessed=stacked.size * 2 + rounded.size * 2 + rounded.size * 12,
        ),
    )(cols, counts, rounded, stacked)


def body(up_time, down_blocks, block_cols, block_counts):
    freq_groups = lax.axis_size("freq")
    receiver_groups = lax.axis_size("rcv")
    shot_count, time_steps, receivers = up_time.shape
    local_freqs, local_blocks, slot_count, _, block_size, _ = down_blocks.shape
    local_rows = receivers // receiver_groups
    reach_blocks = (slot_count - 1) // 2
    rim_rows = reach_blocks * block_size
    span_blocks = local_blocks + 2 * reach_blocks
    fourier = fourier_table(time_steps, freq_groups, local_freqs)
    spectrum = jnp.einsum(
        "snr,ncgf->cfsgr", up_time, fourier, preferred_element_type=jnp.float32
    ).astype(jnp.bfloat16)
    spectrum = spectrum.reshape(
        2, local_freqs, shot_count, freq_groups * receiver_groups, local_rows
    )
    received = lax.all_to_all(spectrum, ("freq", "rcv"), split_axis=3, concat_axis=2, tiled=True)
    right_side = received.reshape(2, local_freqs, -1, local_rows).astype(jnp.float32)
    position = lax.axis_index("rcv")
    columns = jnp.clip(
        block_cols - position * local_blocks + reach_blocks, 0, span_blocks - 1
    ).reshape(-1)
    counts = jnp.clip(block_counts, 0, slot_count).reshape(-1)

    def exchange(lower_rim, middle, upper_rim):
        from_above = from_behind(lower_rim, "rcv", -1)
        from_below = from_behind(upper_rim, "rcv", 1)
        middle = middle.at[..., :rim_rows].add(from_below)
        middle = middle.at[..., local_rows - rim_rows :].add(from_above)
        return middle

    def first_adjoint(field):
        rounded = field.astype(jnp.bfloat16)
        stacked, *parts = apply_first(
            rounded, down_blocks, columns, counts, span_blocks * block_size
        )
        return stacked, field + exchange(*parts)

    def forward_adjoint(raw, scale, left, shift):
        extended = with_halo(raw.astype(jnp.bfloat16), (("rcv", 3),), rim_rows)
        coefs = jnp.stack(
            [jnp.broadcast_to(scale, shift.shape).reshape(-1), shift.reshape(-1)], axis=1
        ).reshape(-1)
        residual, *parts = apply_both(extended, raw, left, coefs, stacked, columns, counts)
        return residual, residual + exchange(*parts)

    def forward(field):
        extended = with_halo(field.astype(jnp.bfloat16), (("rcv", 3),), rim_rows)
        return field + apply_forward(extended, stacked, columns, counts)

    stacked, lifted = first_adjoint(right_side)
    right_squares, lifted_squares = both_squares(right_side, lifted)
    beta_norm = jnp.sqrt(right_squares + EPSILON)
    alpha_norm = jnp.sqrt(lifted_squares / (beta_norm * beta_norm) + EPSILON)
    left_vector = right_side / beta_norm
    right_raw = lifted
    right_scale = beta_norm * alpha_norm
    right_vector = right_raw / right_scale
    search_direction = right_vector
    solution = jnp.zeros_like(right_side)
    phibar = beta_norm
    rhobar = alpha_norm
    for iteration in range(ITERS):
        last = iteration == ITERS - 1
        residual_left, lifted = forward_adjoint(right_raw, right_scale, left_vector, alpha_norm)
        beta_norm = jnp.sqrt(squares(residual_left) + EPSILON)
        left_vector = residual_left / beta_norm
        residual_right = lifted / beta_norm - beta_norm * right_vector
        rho_value = jnp.sqrt(rhobar * rhobar + beta_norm * beta_norm)
        cosine = rhobar / rho_value
        sine_value = beta_norm / rho_value
        phi_value = cosine * phibar
        phibar = sine_value * phibar
        solution = solution + phi_value / rho_value * search_direction
        if last:
            break
        alpha_norm = jnp.sqrt(squares(residual_right) + EPSILON)
        right_raw = residual_right
        right_scale = alpha_norm
        right_vector = residual_right / alpha_norm
        theta_value = sine_value * alpha_norm
        rhobar = -cosine * alpha_norm
        search_direction = right_vector - theta_value / rho_value * search_direction
    return (solution, phibar * cosine * residual_right)


def solution(mesh):
    return jax.shard_map(
        body,
        mesh=mesh,
        in_specs=(
            P(("freq", "rcv"), None, None),
            P("freq", "rcv", None, None, None, None),
            P("freq", "rcv", None),
            P("freq", "rcv"),
        ),
        out_specs=(P(None, "freq", None, "rcv"), P(None, "freq", None, "rcv")),
        check_vma=False,
    )
```

```python
import math

import jax
import jax.numpy as jnp
from jax import lax
from jax.experimental import pallas as pl
from jax.experimental.pallas import tpu as pltpu
from jax.sharding import PartitionSpec as P

ITERS = 2


EPSILON = 1e-06


def with_halo(cells, sides, width):
    for axis, dim in sides:
        count = lax.axis_size(axis)
        ends = count - 1
        head = lax.slice_in_dim(cells, 0, width, axis=dim)
        tail = lax.slice_in_dim(cells, cells.shape[dim] - width, cells.shape[dim], axis=dim)
        cells = jnp.concatenate(
            [
                lax.ppermute(tail, axis, [(i, (i + 1) % count) for i in range(ends)]),
                cells,
                lax.ppermute(head, axis, [((i + 1) % count, i) for i in range(ends)]),
            ],
            axis=dim,
        )
    return cells


def from_behind(value, axis, steps):
    count = lax.axis_size(axis)
    first, last = (max(0, -steps), min(count, count - steps))
    return lax.ppermute(value, axis, [(source, source + steps) for source in range(first, last)])


def fourier_table(time_steps, freq_groups, local_freqs):
    shape = (time_steps, freq_groups, local_freqs)
    sample = lax.broadcasted_iota(jnp.int32, shape, 0)
    harmonic = (
        lax.broadcasted_iota(jnp.int32, shape, 1) * local_freqs
        + lax.broadcasted_iota(jnp.int32, shape, 2)
        + 1
    )
    phase_angle = 2.0 * math.pi / time_steps * (harmonic * sample % time_steps).astype(jnp.float32)
    scale_factor = 1.0 / math.sqrt(time_steps)
    return jnp.stack(
        [jnp.cos(phase_angle) * scale_factor, -jnp.sin(phase_angle) * scale_factor], axis=1
    ).astype(jnp.bfloat16)


def rcv_sum(partial):
    count = lax.axis_size("rcv")
    spread = jnp.broadcast_to(partial[None], (count,) + partial.shape)
    gathered = lax.all_to_all(spread, "rcv", 0, 0, tiled=False)
    return jnp.sum(gathered, axis=0)


def squares(field):
    return rcv_sum(jnp.sum(field * field, axis=(0, 2, 3)))[None, :, None, None]


def both_squares(first, second):
    partial = jnp.stack(
        [jnp.sum(first * first, axis=(0, 2, 3)), jnp.sum(second * second, axis=(0, 2, 3))]
    )
    total = rcv_sum(partial)
    return total[0][None, :, None, None], total[1][None, :, None, None]


def _stack_kernel(counts_ref, a_ref, m_ref):
    slots, _, block, _ = a_ref.shape
    count = counts_ref[pl.program_id(0) * pl.num_programs(1) + pl.program_id(1)]
    for slot in range(slots):
        live = slot < count
        real_part = jnp.where(live, a_ref[slot, 0], jnp.zeros_like(a_ref[slot, 0]))
        imaginary = jnp.where(live, a_ref[slot, 1], jnp.zeros_like(a_ref[slot, 1]))
        left = slice(2 * slot * block, (2 * slot + 1) * block)
        right = slice((2 * slot + 1) * block, (2 * slot + 2) * block)
        m_ref[:block, left] = real_part
        m_ref[:block, right] = -imaginary
        m_ref[block:, left] = imaginary
        m_ref[block:, right] = real_part


def stack_blocks(down_blocks, counts):
    local_freqs, local_blocks, slot_count, _, block_size, _ = down_blocks.shape
    width = 2 * slot_count * block_size
    grid_spec = pltpu.PrefetchScalarGridSpec(
        num_scalar_prefetch=1,
        grid=(local_freqs, local_blocks),
        in_specs=[
            pl.BlockSpec(
                (None, None, slot_count, 2, block_size, block_size),
                lambda f, r, n: (f, r, 0, 0, 0, 0),
            )
        ],
        out_specs=pl.BlockSpec(
            (None, None, 2 * block_size, width), lambda f, r, n: (f, r, 0, 0)
        ),
    )
    return pl.pallas_call(
        _stack_kernel,
        grid_spec=grid_spec,
        out_shape=jax.ShapeDtypeStruct(
            (local_freqs, local_blocks, 2 * block_size, width), jnp.bfloat16
        ),
    )(counts, down_blocks)


def _forward_kernel(cols_ref, counts_ref, x_ref, m_ref, o_ref, picked_ref):
    freq = pl.program_id(0)
    row = pl.program_id(1)
    rows = pl.num_programs(1)
    depth, width = m_ref.shape
    block = depth // 2
    slots = width // depth
    index = freq * rows + row
    count = counts_ref[index]
    for slot in range(slots):
        start = pl.multiple_of(cols_ref[index * slots + slot] * block, block)
        for part in range(2):
            taken = x_ref[part, :, pl.ds(start, block)]
            lanes = slice((2 * slot + part) * block, (2 * slot + part + 1) * block)
            picked_ref[:, lanes] = jnp.where(slot < count, taken, jnp.zeros_like(taken))
    contract = (((1,), (1,)), ((), ()))
    product = lax.dot_general(
        picked_ref[...], m_ref[...], contract, preferred_element_type=jnp.float32
    )
    o_ref[0] = product[:, :block]
    o_ref[1] = product[:, block:]


def _scatter(cols_ref, index, field, m_ref, acc_ref):
    depth, width = m_ref.shape
    block = depth // 2
    slots = width // depth
    spread = jnp.dot(field, m_ref[...], preferred_element_type=jnp.float32)
    for slot in range(slots):
        start = pl.multiple_of(cols_ref[index * slots + slot] * block, block)
        for part in range(2):
            lanes = slice((2 * slot + part) * block, (2 * slot + part + 1) * block)
            acc_ref[part, :, pl.ds(start, block)] += spread[:, lanes]


def _split(acc_ref, lower_ref, middle_ref, upper_ref):
    rim = lower_ref.shape[-1]
    own = middle_ref.shape[-1]
    lower_ref[...] = acc_ref[:, :, :rim]
    middle_ref[...] = acc_ref[:, :, rim : rim + own]
    upper_ref[...] = acc_ref[:, :, rim + own :]


def _adjoint_kernel(cols_ref, counts_ref, u_ref, m_ref, lower_ref, middle_ref, upper_ref, acc_ref):
    freq = pl.program_id(0)
    row = pl.program_id(1)
    rows = pl.num_programs(1)

    @pl.when(row == 0)
    def _():
        acc_ref[...] = jnp.zeros(acc_ref.shape, acc_ref.dtype)

    field = jnp.concatenate([u_ref[0], u_ref[1]], axis=1)
    _scatter(cols_ref, freq * rows + row, field, m_ref, acc_ref)

    @pl.when(row == rows - 1)
    def _():
        _split(acc_ref, lower_ref, middle_ref, upper_ref)


def _both_kernel(
    cols_ref,
    counts_ref,
    coef_ref,
    below_ref,
    own_ref,
    above_ref,
    q_ref,
    u_ref,
    m_ref,
    p_ref,
    lower_ref,
    middle_ref,
    upper_ref,
    picked_ref,
    acc_ref,
):
    freq = pl.program_id(0)
    row = pl.program_id(1)
    rows = pl.num_programs(1)
    depth, width = m_ref.shape
    block = depth // 2
    slots = width // depth
    index = freq * rows + row

    @pl.when(row == 0)
    def _():
        acc_ref[...] = jnp.zeros(acc_ref.shape, acc_ref.dtype)

    rim_blocks = below_ref.shape[-1] // block
    own_blocks = own_ref.shape[-1] // block
    pieces = (
        (below_ref, 0, rim_blocks),
        (own_ref, rim_blocks, rim_blocks + own_blocks),
        (above_ref, rim_blocks + own_blocks, 2 * rim_blocks + own_blocks),
    )
    for slot in range(slots):
        column = cols_ref[index * slots + slot]
        for source, first, end in pieces:

            @pl.when((column >= first) & (column < end))
            def _():
                start = pl.multiple_of((column - first) * block, block)
                for part in range(2):
                    lanes = slice((2 * slot + part) * block, (2 * slot + part + 1) * block)
                    picked_ref[:, lanes] = source[part, :, pl.ds(start, block)]

    contract = (((1,), (1,)), ((), ()))
    product = lax.dot_general(
        picked_ref[...], m_ref[...], contract, preferred_element_type=jnp.float32
    )
    scale = coef_ref[2 * freq]
    shift = coef_ref[2 * freq + 1]
    for part in range(2):
        lanes = slice(part * block, (part + 1) * block)
        p_ref[part] = (q_ref[part] + product[:, lanes]) / scale - shift * u_ref[part]
    field = jnp.concatenate(
        [p_ref[0].astype(jnp.bfloat16), p_ref[1].astype(jnp.bfloat16)], axis=1
    )
    _scatter(cols_ref, index, field, m_ref, acc_ref)

    @pl.when(row == rows - 1)
    def _():
        _split(acc_ref, lower_ref, middle_ref, upper_ref)


def _part_specs(local_freqs, sources):
    def part_spec(lanes):
        return pl.BlockSpec((2, None, sources, lanes), lambda f, r, c, n: (0, f, 0, 0))

    def part_shape(lanes):
        return jax.ShapeDtypeStruct((2, local_freqs, sources, lanes), jnp.float32)

    return part_spec, part_shape


def apply_both(below, own_field, above, raw, left, coefs, stacked, cols, counts):
    local_freqs, local_blocks, depth, width = stacked.shape
    block_size = depth // 2
    sources = raw.shape[2]
    own_rows = local_blocks * block_size
    rim = below.shape[-1]
    span = 2 * rim + own_rows
    part_spec, part_shape = _part_specs(local_freqs, sources)
    own = pl.BlockSpec((2, None, sources, block_size), lambda f, r, c, n: (0, f, 0, r))
    grid_spec = pltpu.PrefetchScalarGridSpec(
        num_scalar_prefetch=2,
        grid=(local_freqs, local_blocks),
        in_specs=[
            pl.BlockSpec(memory_space=pltpu.SMEM),
            part_spec(rim),
            part_spec(own_rows),
            part_spec(rim),
            own,
            own,
            pl.BlockSpec((None, None, depth, width), lambda f, r, c, n: (f, r, 0, 0)),
        ],
        out_specs=[own, part_spec(rim), part_spec(own_rows), part_spec(rim)],
        scratch_shapes=[
            pltpu.VMEM((sources, width), jnp.bfloat16),
            pltpu.VMEM((2, sources, span), jnp.float32),
        ],
    )
    return pl.pallas_call(
        _both_kernel,
        grid_spec=grid_spec,
        out_shape=[
            jax.ShapeDtypeStruct(raw.shape, jnp.float32),
            part_shape(rim),
            part_shape(own_rows),
            part_shape(rim),
        ],
        compiler_params=pltpu.CompilerParams(dimension_semantics=("arbitrary", "arbitrary")),
        cost_estimate=pl.CostEstimate(
            flops=4 * local_freqs * local_blocks * sources * depth * width,
            transcendentals=0,
            bytes_accessed=stacked.size * 2 + raw.size * 46,
        ),
    )(cols, counts, coefs, below, own_field, above, raw, left, stacked)


def apply_forward(extended, stacked, cols, counts):
    local_freqs, local_blocks, depth, width = stacked.shape
    block_size = depth // 2
    _, _, sources, span = extended.shape
    grid_spec = pltpu.PrefetchScalarGridSpec(
        num_scalar_prefetch=2,
        grid=(local_freqs, local_blocks),
        in_specs=[
            pl.BlockSpec((2, None, sources, span), lambda f, r, c, n: (0, f, 0, 0)),
            pl.BlockSpec((None, None, depth, width), lambda f, r, c, n: (f, r, 0, 0)),
        ],
        out_specs=pl.BlockSpec((2, None, sources, block_size), lambda f, r, c, n: (0, f, 0, r)),
        scratch_shapes=[pltpu.VMEM((sources, width), jnp.bfloat16)],
    )
    return pl.pallas_call(
        _forward_kernel,
        grid_spec=grid_spec,
        out_shape=jax.ShapeDtypeStruct(
            (2, local_freqs, sources, local_blocks * block_size), jnp.float32
        ),
        compiler_params=pltpu.CompilerParams(dimension_semantics=("arbitrary", "arbitrary")),
        cost_estimate=pl.CostEstimate(
            flops=2 * local_freqs * local_blocks * sources * depth * width,
            transcendentals=0,
            bytes_accessed=stacked.size * 2 + extended.size * 2 + extended.size * 4,
        ),
    )(cols, counts, extended, stacked)


def apply_adjoint(rounded, stacked, cols, counts, span):
    local_freqs, local_blocks, depth, width = stacked.shape
    block_size = depth // 2
    sources = rounded.shape[2]
    own = local_blocks * block_size
    rim = (span - own) // 2
    part_spec, part_shape = _part_specs(local_freqs, sources)
    grid_spec = pltpu.PrefetchScalarGridSpec(
        num_scalar_prefetch=2,
        grid=(local_freqs, local_blocks),
        in_specs=[
            pl.BlockSpec((2, None, sources, block_size), lambda f, r, c, n: (0, f, 0, r)),
            pl.BlockSpec((None, None, depth, width), lambda f, r, c, n: (f, r, 0, 0)),
        ],
        out_specs=[part_spec(rim), part_spec(own), part_spec(rim)],
        scratch_shapes=[pltpu.VMEM((2, sources, span), jnp.float32)],
    )
    return pl.pallas_call(
        _adjoint_kernel,
        grid_spec=grid_spec,
        out_shape=[part_shape(rim), part_shape(own), part_shape(rim)],
        compiler_params=pltpu.CompilerParams(dimension_semantics=("arbitrary", "arbitrary")),
        cost_estimate=pl.CostEstimate(
            flops=2 * local_freqs * local_blocks * sources * depth * width,
            transcendentals=0,
            bytes_accessed=stacked.size * 2 + rounded.size * 2 + rounded.size * 12,
        ),
    )(cols, counts, rounded, stacked)


def body(up_time, down_blocks, block_cols, block_counts):
    freq_groups = lax.axis_size("freq")
    receiver_groups = lax.axis_size("rcv")
    shot_count, time_steps, receivers = up_time.shape
    local_freqs, local_blocks, slot_count, _, block_size, _ = down_blocks.shape
    local_rows = receivers // receiver_groups
    reach_blocks = (slot_count - 1) // 2
    rim_rows = reach_blocks * block_size
    span_blocks = local_blocks + 2 * reach_blocks
    fourier = fourier_table(time_steps, freq_groups, local_freqs)
    spectrum = jnp.einsum(
        "snr,ncgf->cfsgr", up_time, fourier, preferred_element_type=jnp.float32
    ).astype(jnp.bfloat16)
    spectrum = spectrum.reshape(
        2, local_freqs, shot_count, freq_groups * receiver_groups, local_rows
    )
    received = lax.all_to_all(spectrum, ("freq", "rcv"), split_axis=3, concat_axis=2, tiled=True)
    right_side = received.reshape(2, local_freqs, -1, local_rows).astype(jnp.float32)
    position = lax.axis_index("rcv")
    columns = jnp.clip(
        block_cols - position * local_blocks + reach_blocks, 0, span_blocks - 1
    ).reshape(-1)
    counts = jnp.clip(block_counts, 0, slot_count).reshape(-1)
    stacked = stack_blocks(down_blocks, counts)

    def exchange(lower_rim, middle, upper_rim):
        from_above = from_behind(lower_rim, "rcv", -1)
        from_below = from_behind(upper_rim, "rcv", 1)
        middle = middle.at[..., :rim_rows].add(from_below)
        middle = middle.at[..., local_rows - rim_rows :].add(from_above)
        return middle

    def adjoint(field):
        rounded = field.astype(jnp.bfloat16)
        parts = apply_adjoint(rounded, stacked, columns, counts, span_blocks * block_size)
        return field + exchange(*parts)

    def forward_adjoint(raw, scale, left, shift):
        rounded = raw.astype(jnp.bfloat16)
        below = from_behind(rounded[..., local_rows - rim_rows :], "rcv", 1)
        above = from_behind(rounded[..., :rim_rows], "rcv", -1)
        coefs = jnp.stack(
            [jnp.broadcast_to(scale, shift.shape).reshape(-1), shift.reshape(-1)], axis=1
        ).reshape(-1)
        residual, *parts = apply_both(
            below, rounded, above, raw, left, coefs, stacked, columns, counts
        )
        return residual, residual + exchange(*parts)

    def forward(field):
        extended = with_halo(field.astype(jnp.bfloat16), (("rcv", 3),), rim_rows)
        return field + apply_forward(extended, stacked, columns, counts)

    lifted = adjoint(right_side)
    right_squares, lifted_squares = both_squares(right_side, lifted)
    beta_norm = jnp.sqrt(right_squares + EPSILON)
    alpha_norm = jnp.sqrt(lifted_squares / (beta_norm * beta_norm) + EPSILON)
    left_vector = right_side / beta_norm
    right_raw = lifted
    right_scale = beta_norm * alpha_norm
    right_vector = right_raw / right_scale
    search_direction = right_vector
    solution = jnp.zeros_like(right_side)
    phibar = beta_norm
    rhobar = alpha_norm
    for iteration in range(ITERS):
        last = iteration == ITERS - 1
        residual_left, lifted = forward_adjoint(right_raw, right_scale, left_vector, alpha_norm)
        beta_norm = jnp.sqrt(squares(residual_left) + EPSILON)
        left_vector = residual_left / beta_norm
        residual_right = lifted / beta_norm - beta_norm * right_vector
        rho_value = jnp.sqrt(rhobar * rhobar + beta_norm * beta_norm)
        cosine = rhobar / rho_value
        sine_value = beta_norm / rho_value
        phi_value = cosine * phibar
        phibar = sine_value * phibar
        solution = solution + phi_value / rho_value * search_direction
        if last:
            break
        alpha_norm = jnp.sqrt(squares(residual_right) + EPSILON)
        right_raw = residual_right
        right_scale = alpha_norm
        right_vector = residual_right / alpha_norm
        theta_value = sine_value * alpha_norm
        rhobar = -cosine * alpha_norm
        search_direction = right_vector - theta_value / rho_value * search_direction
    return (solution, phibar * cosine * residual_right)


def solution(mesh):
    return jax.shard_map(
        body,
        mesh=mesh,
        in_specs=(
            P(("freq", "rcv"), None, None),
            P("freq", "rcv", None, None, None, None),
            P("freq", "rcv", None),
            P("freq", "rcv"),
        ),
        out_specs=(P(None, "freq", None, "rcv"), P(None, "freq", None, "rcv")),
        check_vma=False,
    )
```

```python
import math

import jax
import jax.numpy as jnp
from jax import lax
from jax.experimental import pallas as pl
from jax.experimental.pallas import tpu as pltpu
from jax.sharding import PartitionSpec as P

ITERS = 2


EPSILON = 1e-06


def with_halo(cells, sides, width):
    for axis, dim in sides:
        count = lax.axis_size(axis)
        ends = count - 1
        head = lax.slice_in_dim(cells, 0, width, axis=dim)
        tail = lax.slice_in_dim(cells, cells.shape[dim] - width, cells.shape[dim], axis=dim)
        cells = jnp.concatenate(
            [
                lax.ppermute(tail, axis, [(i, (i + 1) % count) for i in range(ends)]),
                cells,
                lax.ppermute(head, axis, [((i + 1) % count, i) for i in range(ends)]),
            ],
            axis=dim,
        )
    return cells


def from_behind(value, axis, steps):
    count = lax.axis_size(axis)
    first, last = (max(0, -steps), min(count, count - steps))
    return lax.ppermute(value, axis, [(source, source + steps) for source in range(first, last)])


def fourier_table(time_steps, freq_groups, local_freqs):
    shape = (time_steps, freq_groups, local_freqs)
    sample = lax.broadcasted_iota(jnp.int32, shape, 0)
    harmonic = (
        lax.broadcasted_iota(jnp.int32, shape, 1) * local_freqs
        + lax.broadcasted_iota(jnp.int32, shape, 2)
        + 1
    )
    phase_angle = 2.0 * math.pi / time_steps * (harmonic * sample % time_steps).astype(jnp.float32)
    scale_factor = 1.0 / math.sqrt(time_steps)
    return jnp.stack(
        [jnp.cos(phase_angle) * scale_factor, -jnp.sin(phase_angle) * scale_factor], axis=1
    ).astype(jnp.bfloat16)


def rcv_sum(partial):
    count = lax.axis_size("rcv")
    spread = jnp.broadcast_to(partial[None], (count,) + partial.shape)
    gathered = lax.all_to_all(spread, "rcv", 0, 0, tiled=False)
    return jnp.sum(gathered, axis=0)


def squares(field):
    return rcv_sum(jnp.sum(field * field, axis=(0, 2, 3)))[None, :, None, None]


def both_squares(first, second):
    partial = jnp.stack(
        [jnp.sum(first * first, axis=(0, 2, 3)), jnp.sum(second * second, axis=(0, 2, 3))]
    )
    total = rcv_sum(partial)
    return total[0][None, :, None, None], total[1][None, :, None, None]


def _stack_kernel(counts_ref, a_ref, m_ref):
    slots, _, block, _ = a_ref.shape
    count = counts_ref[pl.program_id(0) * pl.num_programs(1) + pl.program_id(1)]
    for slot in range(slots):
        live = slot < count
        real_part = jnp.where(live, a_ref[slot, 0], jnp.zeros_like(a_ref[slot, 0]))
        imaginary = jnp.where(live, a_ref[slot, 1], jnp.zeros_like(a_ref[slot, 1]))
        left = slice(2 * slot * block, (2 * slot + 1) * block)
        right = slice((2 * slot + 1) * block, (2 * slot + 2) * block)
        m_ref[:block, left] = real_part
        m_ref[:block, right] = -imaginary
        m_ref[block:, left] = imaginary
        m_ref[block:, right] = real_part


def stack_blocks(down_blocks, counts):
    local_freqs, local_blocks, slot_count, _, block_size, _ = down_blocks.shape
    width = 2 * slot_count * block_size
    grid_spec = pltpu.PrefetchScalarGridSpec(
        num_scalar_prefetch=1,
        grid=(local_freqs, local_blocks),
        in_specs=[
            pl.BlockSpec(
                (None, None, slot_count, 2, block_size, block_size),
                lambda f, r, n: (f, r, 0, 0, 0, 0),
            )
        ],
        out_specs=pl.BlockSpec(
            (None, None, 2 * block_size, width), lambda f, r, n: (f, r, 0, 0)
        ),
    )
    return pl.pallas_call(
        _stack_kernel,
        grid_spec=grid_spec,
        out_shape=jax.ShapeDtypeStruct(
            (local_freqs, local_blocks, 2 * block_size, width), jnp.bfloat16
        ),
    )(counts, down_blocks)


def _forward_kernel(cols_ref, counts_ref, x_ref, m_ref, o_ref, picked_ref):
    freq = pl.program_id(0)
    row = pl.program_id(1)
    rows = pl.num_programs(1)
    depth, width = m_ref.shape
    block = depth // 2
    slots = width // depth
    index = freq * rows + row
    count = counts_ref[index]
    for slot in range(slots):
        start = pl.multiple_of(cols_ref[index * slots + slot] * block, block)
        for part in range(2):
            taken = x_ref[part, :, pl.ds(start, block)]
            lanes = slice((2 * slot + part) * block, (2 * slot + part + 1) * block)
            picked_ref[:, lanes] = jnp.where(slot < count, taken, jnp.zeros_like(taken))
    contract = (((1,), (1,)), ((), ()))
    product = lax.dot_general(
        picked_ref[...], m_ref[...], contract, preferred_element_type=jnp.float32
    )
    o_ref[0] = product[:, :block]
    o_ref[1] = product[:, block:]


def _scatter(cols_ref, index, field, m_ref, acc_ref):
    depth, width = m_ref.shape
    block = depth // 2
    slots = width // depth
    spread = jnp.dot(field, m_ref[...], preferred_element_type=jnp.float32)
    for slot in range(slots):
        start = pl.multiple_of(cols_ref[index * slots + slot] * block, block)
        for part in range(2):
            lanes = slice((2 * slot + part) * block, (2 * slot + part + 1) * block)
            acc_ref[part, :, pl.ds(start, block)] += spread[:, lanes]


def _split(acc_ref, lower_ref, middle_ref, upper_ref):
    rim = lower_ref.shape[-1]
    own = middle_ref.shape[-1]
    lower_ref[...] = acc_ref[:, :, :rim]
    middle_ref[...] = acc_ref[:, :, rim : rim + own]
    upper_ref[...] = acc_ref[:, :, rim + own :]


def _adjoint_kernel(cols_ref, counts_ref, u_ref, m_ref, lower_ref, middle_ref, upper_ref, acc_ref):
    freq = pl.program_id(0)
    row = pl.program_id(1)
    rows = pl.num_programs(1)

    @pl.when(row == 0)
    def _():
        acc_ref[...] = jnp.zeros(acc_ref.shape, acc_ref.dtype)

    field = jnp.concatenate([u_ref[0], u_ref[1]], axis=1)
    _scatter(cols_ref, freq * rows + row, field, m_ref, acc_ref)

    @pl.when(row == rows - 1)
    def _():
        _split(acc_ref, lower_ref, middle_ref, upper_ref)


def _both_kernel(
    cols_ref,
    counts_ref,
    coef_ref,
    x_ref,
    q_ref,
    u_ref,
    m_ref,
    p_ref,
    lower_ref,
    middle_ref,
    upper_ref,
    squares_ref,
    picked_ref,
    acc_ref,
):
    freq = pl.program_id(0)
    row = pl.program_id(1)
    rows = pl.num_programs(1)
    depth, width = m_ref.shape
    block = depth // 2
    slots = width // depth
    index = freq * rows + row

    @pl.when(row == 0)
    def _():
        acc_ref[...] = jnp.zeros(acc_ref.shape, acc_ref.dtype)
        squares_ref[...] = jnp.zeros(squares_ref.shape, squares_ref.dtype)

    for slot in range(slots):
        start = pl.multiple_of(cols_ref[index * slots + slot] * block, block)
        for part in range(2):
            lanes = slice((2 * slot + part) * block, (2 * slot + part + 1) * block)
            picked_ref[:, lanes] = x_ref[part, :, pl.ds(start, block)]
    contract = (((1,), (1,)), ((), ()))
    product = lax.dot_general(
        picked_ref[...], m_ref[...], contract, preferred_element_type=jnp.float32
    )
    scale = coef_ref[2 * freq]
    shift = coef_ref[2 * freq + 1]
    for part in range(2):
        lanes = slice(part * block, (part + 1) * block)
        p_ref[part] = (q_ref[part] + product[:, lanes]) / scale - shift * u_ref[part]
    total = jnp.sum(p_ref[0] * p_ref[0] + p_ref[1] * p_ref[1], axis=(0, 1), keepdims=True)
    squares_ref[...] += jnp.broadcast_to(total, squares_ref.shape)
    field = jnp.concatenate(
        [p_ref[0].astype(jnp.bfloat16), p_ref[1].astype(jnp.bfloat16)], axis=1
    )
    _scatter(cols_ref, index, field, m_ref, acc_ref)

    @pl.when(row == rows - 1)
    def _():
        _split(acc_ref, lower_ref, middle_ref, upper_ref)


def _part_specs(local_freqs, sources):
    def part_spec(lanes):
        return pl.BlockSpec((2, None, sources, lanes), lambda f, r, c, n: (0, f, 0, 0))

    def part_shape(lanes):
        return jax.ShapeDtypeStruct((2, local_freqs, sources, lanes), jnp.float32)

    return part_spec, part_shape


def apply_both(extended, raw, left, coefs, stacked, cols, counts):
    local_freqs, local_blocks, depth, width = stacked.shape
    block_size = depth // 2
    _, _, sources, span = extended.shape
    own_rows = local_blocks * block_size
    rim = (span - own_rows) // 2
    part_spec, part_shape = _part_specs(local_freqs, sources)
    own = pl.BlockSpec((2, None, sources, block_size), lambda f, r, c, n: (0, f, 0, r))
    grid_spec = pltpu.PrefetchScalarGridSpec(
        num_scalar_prefetch=2,
        grid=(local_freqs, local_blocks),
        in_specs=[
            pl.BlockSpec(memory_space=pltpu.SMEM),
            pl.BlockSpec((2, None, sources, span), lambda f, r, c, n: (0, f, 0, 0)),
            own,
            own,
            pl.BlockSpec((None, None, depth, width), lambda f, r, c, n: (f, r, 0, 0)),
        ],
        out_specs=[
            own,
            part_spec(rim),
            part_spec(own_rows),
            part_spec(rim),
            pl.BlockSpec((None, 8, 128), lambda f, r, c, n: (f, 0, 0)),
        ],
        scratch_shapes=[
            pltpu.VMEM((sources, width), jnp.bfloat16),
            pltpu.VMEM((2, sources, span), jnp.float32),
        ],
    )
    return pl.pallas_call(
        _both_kernel,
        grid_spec=grid_spec,
        out_shape=[
            jax.ShapeDtypeStruct(raw.shape, jnp.float32),
            part_shape(rim),
            part_shape(own_rows),
            part_shape(rim),
            jax.ShapeDtypeStruct((local_freqs, 8, 128), jnp.float32),
        ],
        compiler_params=pltpu.CompilerParams(dimension_semantics=("arbitrary", "arbitrary")),
        cost_estimate=pl.CostEstimate(
            flops=4 * local_freqs * local_blocks * sources * depth * width,
            transcendentals=0,
            bytes_accessed=stacked.size * 2 + extended.size * 2 + raw.size * 40,
        ),
    )(cols, counts, coefs, extended, raw, left, stacked)


def apply_forward(extended, stacked, cols, counts):
    local_freqs, local_blocks, depth, width = stacked.shape
    block_size = depth // 2
    _, _, sources, span = extended.shape
    grid_spec = pltpu.PrefetchScalarGridSpec(
        num_scalar_prefetch=2,
        grid=(local_freqs, local_blocks),
        in_specs=[
            pl.BlockSpec((2, None, sources, span), lambda f, r, c, n: (0, f, 0, 0)),
            pl.BlockSpec((None, None, depth, width), lambda f, r, c, n: (f, r, 0, 0)),
        ],
        out_specs=pl.BlockSpec((2, None, sources, block_size), lambda f, r, c, n: (0, f, 0, r)),
        scratch_shapes=[pltpu.VMEM((sources, width), jnp.bfloat16)],
    )
    return pl.pallas_call(
        _forward_kernel,
        grid_spec=grid_spec,
        out_shape=jax.ShapeDtypeStruct(
            (2, local_freqs, sources, local_blocks * block_size), jnp.float32
        ),
        compiler_params=pltpu.CompilerParams(dimension_semantics=("arbitrary", "arbitrary")),
        cost_estimate=pl.CostEstimate(
            flops=2 * local_freqs * local_blocks * sources * depth * width,
            transcendentals=0,
            bytes_accessed=stacked.size * 2 + extended.size * 2 + extended.size * 4,
        ),
    )(cols, counts, extended, stacked)


def apply_adjoint(rounded, stacked, cols, counts, span):
    local_freqs, local_blocks, depth, width = stacked.shape
    block_size = depth // 2
    sources = rounded.shape[2]
    own = local_blocks * block_size
    rim = (span - own) // 2
    part_spec, part_shape = _part_specs(local_freqs, sources)
    grid_spec = pltpu.PrefetchScalarGridSpec(
        num_scalar_prefetch=2,
        grid=(local_freqs, local_blocks),
        in_specs=[
            pl.BlockSpec((2, None, sources, block_size), lambda f, r, c, n: (0, f, 0, r)),
            pl.BlockSpec((None, None, depth, width), lambda f, r, c, n: (f, r, 0, 0)),
        ],
        out_specs=[part_spec(rim), part_spec(own), part_spec(rim)],
        scratch_shapes=[pltpu.VMEM((2, sources, span), jnp.float32)],
    )
    return pl.pallas_call(
        _adjoint_kernel,
        grid_spec=grid_spec,
        out_shape=[part_shape(rim), part_shape(own), part_shape(rim)],
        compiler_params=pltpu.CompilerParams(dimension_semantics=("arbitrary", "arbitrary")),
        cost_estimate=pl.CostEstimate(
            flops=2 * local_freqs * local_blocks * sources * depth * width,
            transcendentals=0,
            bytes_accessed=stacked.size * 2 + rounded.size * 2 + rounded.size * 12,
        ),
    )(cols, counts, rounded, stacked)


def body(up_time, down_blocks, block_cols, block_counts):
    freq_groups = lax.axis_size("freq")
    receiver_groups = lax.axis_size("rcv")
    shot_count, time_steps, receivers = up_time.shape
    local_freqs, local_blocks, slot_count, _, block_size, _ = down_blocks.shape
    local_rows = receivers // receiver_groups
    reach_blocks = (slot_count - 1) // 2
    rim_rows = reach_blocks * block_size
    span_blocks = local_blocks + 2 * reach_blocks
    fourier = fourier_table(time_steps, freq_groups, local_freqs)
    spectrum = jnp.einsum(
        "snr,ncgf->cfsgr", up_time, fourier, preferred_element_type=jnp.float32
    ).astype(jnp.bfloat16)
    spectrum = spectrum.reshape(
        2, local_freqs, shot_count, freq_groups * receiver_groups, local_rows
    )
    received = lax.all_to_all(spectrum, ("freq", "rcv"), split_axis=3, concat_axis=2, tiled=True)
    right_side = received.reshape(2, local_freqs, -1, local_rows).astype(jnp.float32)
    position = lax.axis_index("rcv")
    columns = jnp.clip(
        block_cols - position * local_blocks + reach_blocks, 0, span_blocks - 1
    ).reshape(-1)
    counts = jnp.clip(block_counts, 0, slot_count).reshape(-1)
    stacked = stack_blocks(down_blocks, counts)

    def exchange(lower_rim, middle, upper_rim):
        from_above = from_behind(lower_rim, "rcv", -1)
        from_below = from_behind(upper_rim, "rcv", 1)
        middle = middle.at[..., :rim_rows].add(from_below)
        middle = middle.at[..., local_rows - rim_rows :].add(from_above)
        return middle

    def adjoint(field):
        rounded = field.astype(jnp.bfloat16)
        parts = apply_adjoint(rounded, stacked, columns, counts, span_blocks * block_size)
        return field + exchange(*parts)

    def forward_adjoint(raw, scale, left, shift):
        extended = with_halo(raw.astype(jnp.bfloat16), (("rcv", 3),), rim_rows)
        coefs = jnp.stack(
            [jnp.broadcast_to(scale, shift.shape).reshape(-1), shift.reshape(-1)], axis=1
        ).reshape(-1)
        residual, lower, middle, upper, partial = apply_both(
            extended, raw, left, coefs, stacked, columns, counts
        )
        total = rcv_sum(partial[:, 0, 0])[None, :, None, None]
        return residual, residual + exchange(lower, middle, upper), total

    def forward(field):
        extended = with_halo(field.astype(jnp.bfloat16), (("rcv", 3),), rim_rows)
        return field + apply_forward(extended, stacked, columns, counts)

    lifted = adjoint(right_side)
    right_squares, lifted_squares = both_squares(right_side, lifted)
    beta_norm = jnp.sqrt(right_squares + EPSILON)
    alpha_norm = jnp.sqrt(lifted_squares / (beta_norm * beta_norm) + EPSILON)
    left_vector = right_side / beta_norm
    right_raw = lifted
    right_scale = beta_norm * alpha_norm
    right_vector = right_raw / right_scale
    search_direction = right_vector
    solution = jnp.zeros_like(right_side)
    phibar = beta_norm
    rhobar = alpha_norm
    for iteration in range(ITERS):
        last = iteration == ITERS - 1
        residual_left, lifted, left_squares = forward_adjoint(
            right_raw, right_scale, left_vector, alpha_norm
        )
        beta_norm = jnp.sqrt(left_squares + EPSILON)
        left_vector = residual_left / beta_norm
        residual_right = lifted / beta_norm - beta_norm * right_vector
        rho_value = jnp.sqrt(rhobar * rhobar + beta_norm * beta_norm)
        cosine = rhobar / rho_value
        sine_value = beta_norm / rho_value
        phi_value = cosine * phibar
        phibar = sine_value * phibar
        solution = solution + phi_value / rho_value * search_direction
        if last:
            break
        alpha_norm = jnp.sqrt(squares(residual_right) + EPSILON)
        right_raw = residual_right
        right_scale = alpha_norm
        right_vector = residual_right / alpha_norm
        theta_value = sine_value * alpha_norm
        rhobar = -cosine * alpha_norm
        search_direction = right_vector - theta_value / rho_value * search_direction
    return (solution, phibar * cosine * residual_right)


def solution(mesh):
    return jax.shard_map(
        body,
        mesh=mesh,
        in_specs=(
            P(("freq", "rcv"), None, None),
            P("freq", "rcv", None, None, None, None),
            P("freq", "rcv", None),
            P("freq", "rcv"),
        ),
        out_specs=(P(None, "freq", None, "rcv"), P(None, "freq", None, "rcv")),
        check_vma=False,
    )
```

```python
import math

import jax
import jax.numpy as jnp
from jax import lax
from jax.experimental import pallas as pl
from jax.experimental.pallas import tpu as pltpu
from jax.sharding import PartitionSpec as P

ITERS = 2


EPSILON = 1e-06


def with_halo(cells, sides, width):
    for axis, dim in sides:
        count = lax.axis_size(axis)
        ends = count - 1
        head = lax.slice_in_dim(cells, 0, width, axis=dim)
        tail = lax.slice_in_dim(cells, cells.shape[dim] - width, cells.shape[dim], axis=dim)
        cells = jnp.concatenate(
            [
                lax.ppermute(tail, axis, [(i, (i + 1) % count) for i in range(ends)]),
                cells,
                lax.ppermute(head, axis, [((i + 1) % count, i) for i in range(ends)]),
            ],
            axis=dim,
        )
    return cells


def from_behind(value, axis, steps):
    count = lax.axis_size(axis)
    first, last = (max(0, -steps), min(count, count - steps))
    return lax.ppermute(value, axis, [(source, source + steps) for source in range(first, last)])


def fourier_table(time_steps, freq_groups, local_freqs):
    shape = (time_steps, freq_groups, local_freqs)
    sample = lax.broadcasted_iota(jnp.int32, shape, 0)
    harmonic = (
        lax.broadcasted_iota(jnp.int32, shape, 1) * local_freqs
        + lax.broadcasted_iota(jnp.int32, shape, 2)
        + 1
    )
    phase_angle = 2.0 * math.pi / time_steps * (harmonic * sample % time_steps).astype(jnp.float32)
    scale_factor = 1.0 / math.sqrt(time_steps)
    return jnp.stack(
        [jnp.cos(phase_angle) * scale_factor, -jnp.sin(phase_angle) * scale_factor], axis=1
    ).astype(jnp.bfloat16)


def rcv_sum(partial):
    count = lax.axis_size("rcv")
    spread = jnp.broadcast_to(partial[None], (count,) + partial.shape)
    gathered = lax.all_to_all(spread, "rcv", 0, 0, tiled=False)
    return jnp.sum(gathered, axis=0)


def squares(field):
    return rcv_sum(jnp.sum(field * field, axis=(0, 2, 3)))[None, :, None, None]


def both_squares(first, second):
    partial = jnp.stack(
        [jnp.sum(first * first, axis=(0, 2, 3)), jnp.sum(second * second, axis=(0, 2, 3))]
    )
    total = rcv_sum(partial)
    return total[0][None, :, None, None], total[1][None, :, None, None]


def _stack_kernel(counts_ref, a_ref, m_ref):
    slots, _, block, _ = a_ref.shape
    count = counts_ref[pl.program_id(0) * pl.num_programs(1) + pl.program_id(1)]
    for slot in range(slots):
        live = slot < count
        real_part = jnp.where(live, a_ref[slot, 0], jnp.zeros_like(a_ref[slot, 0]))
        imaginary = jnp.where(live, a_ref[slot, 1], jnp.zeros_like(a_ref[slot, 1]))
        left = slice(2 * slot * block, (2 * slot + 1) * block)
        right = slice((2 * slot + 1) * block, (2 * slot + 2) * block)
        m_ref[:block, left] = real_part
        m_ref[:block, right] = -imaginary
        m_ref[block:, left] = imaginary
        m_ref[block:, right] = real_part


def stack_blocks(down_blocks, counts):
    local_freqs, local_blocks, slot_count, _, block_size, _ = down_blocks.shape
    width = 2 * slot_count * block_size
    grid_spec = pltpu.PrefetchScalarGridSpec(
        num_scalar_prefetch=1,
        grid=(local_freqs, local_blocks),
        in_specs=[
            pl.BlockSpec(
                (None, None, slot_count, 2, block_size, block_size),
                lambda f, r, n: (f, r, 0, 0, 0, 0),
            )
        ],
        out_specs=pl.BlockSpec(
            (None, None, 2 * block_size, width), lambda f, r, n: (f, r, 0, 0)
        ),
    )
    return pl.pallas_call(
        _stack_kernel,
        grid_spec=grid_spec,
        out_shape=jax.ShapeDtypeStruct(
            (local_freqs, local_blocks, 2 * block_size, width), jnp.bfloat16
        ),
    )(counts, down_blocks)


def _forward_kernel(cols_ref, counts_ref, x_ref, m_ref, o_ref, picked_ref):
    freq = pl.program_id(0)
    row = pl.program_id(1)
    rows = pl.num_programs(1)
    depth, width = m_ref.shape
    block = depth // 2
    slots = width // depth
    index = freq * rows + row
    count = counts_ref[index]
    for slot in range(slots):
        start = pl.multiple_of(cols_ref[index * slots + slot] * block, block)
        for part in range(2):
            taken = x_ref[part, :, pl.ds(start, block)]
            lanes = slice((2 * slot + part) * block, (2 * slot + part + 1) * block)
            picked_ref[:, lanes] = jnp.where(slot < count, taken, jnp.zeros_like(taken))
    contract = (((1,), (1,)), ((), ()))
    product = lax.dot_general(
        picked_ref[...], m_ref[...], contract, preferred_element_type=jnp.float32
    )
    o_ref[0] = product[:, :block]
    o_ref[1] = product[:, block:]


def _scatter(cols_ref, index, field, m_ref, acc_ref):
    depth, width = m_ref.shape
    block = depth // 2
    slots = width // depth
    spread = jnp.dot(field, m_ref[...], preferred_element_type=jnp.float32)
    for slot in range(slots):
        start = pl.multiple_of(cols_ref[index * slots + slot] * block, block)
        for part in range(2):
            lanes = slice((2 * slot + part) * block, (2 * slot + part + 1) * block)
            acc_ref[part, :, pl.ds(start, block)] += spread[:, lanes]


def _split(acc_ref, lower_ref, middle_ref, upper_ref):
    rim = lower_ref.shape[-1]
    own = middle_ref.shape[-1]
    lower_ref[...] = acc_ref[:, :, :rim]
    middle_ref[...] = acc_ref[:, :, rim : rim + own]
    upper_ref[...] = acc_ref[:, :, rim + own :]


def _adjoint_kernel(cols_ref, counts_ref, u_ref, m_ref, lower_ref, middle_ref, upper_ref, acc_ref):
    freq = pl.program_id(0)
    row = pl.program_id(1)
    rows = pl.num_programs(1)

    @pl.when(row == 0)
    def _():
        acc_ref[...] = jnp.zeros(acc_ref.shape, acc_ref.dtype)

    field = jnp.concatenate([u_ref[0], u_ref[1]], axis=1)
    _scatter(cols_ref, freq * rows + row, field, m_ref, acc_ref)

    @pl.when(row == rows - 1)
    def _():
        _split(acc_ref, lower_ref, middle_ref, upper_ref)


def _both_kernel(
    cols_ref,
    counts_ref,
    coef_ref,
    x_ref,
    q_ref,
    u_ref,
    m_ref,
    p_ref,
    lower_ref,
    middle_ref,
    upper_ref,
    squares_ref,
    picked_ref,
    acc_ref,
):
    freq = pl.program_id(0)
    row = pl.program_id(1)
    rows = pl.num_programs(1)
    depth, width = m_ref.shape
    block = depth // 2
    slots = width // depth
    index = freq * rows + row

    @pl.when(row == 0)
    def _():
        acc_ref[...] = jnp.zeros(acc_ref.shape, acc_ref.dtype)
        squares_ref[...] = jnp.zeros(squares_ref.shape, squares_ref.dtype)

    for slot in range(slots):
        start = pl.multiple_of(cols_ref[index * slots + slot] * block, block)
        for part in range(2):
            lanes = slice((2 * slot + part) * block, (2 * slot + part + 1) * block)
            picked_ref[:, lanes] = x_ref[part, :, pl.ds(start, block)]
    contract = (((1,), (1,)), ((), ()))
    product = lax.dot_general(
        picked_ref[...], m_ref[...], contract, preferred_element_type=jnp.float32
    )
    scale = coef_ref[2 * freq]
    shift = coef_ref[2 * freq + 1]
    for part in range(2):
        lanes = slice(part * block, (part + 1) * block)
        p_ref[part] = (q_ref[part] + product[:, lanes]) / scale - shift * u_ref[part]
    total = jnp.sum(p_ref[0] * p_ref[0] + p_ref[1] * p_ref[1], axis=(0, 1), keepdims=True)
    squares_ref[...] += jnp.broadcast_to(total, squares_ref.shape)
    field = jnp.concatenate(
        [p_ref[0].astype(jnp.bfloat16), p_ref[1].astype(jnp.bfloat16)], axis=1
    )
    _scatter(cols_ref, index, field, m_ref, acc_ref)

    @pl.when(row == rows - 1)
    def _():
        _split(acc_ref, lower_ref, middle_ref, upper_ref)


def _part_specs(local_freqs, sources):
    def part_spec(lanes):
        return pl.BlockSpec((2, None, sources, lanes), lambda f, r, c, n: (0, f, 0, 0))

    def part_shape(lanes):
        return jax.ShapeDtypeStruct((2, local_freqs, sources, lanes), jnp.float32)

    return part_spec, part_shape


def apply_both(extended, raw, left, coefs, stacked, cols, counts):
    local_freqs, local_blocks, depth, width = stacked.shape
    block_size = depth // 2
    _, _, sources, span = extended.shape
    own_rows = local_blocks * block_size
    rim = (span - own_rows) // 2
    part_spec, part_shape = _part_specs(local_freqs, sources)
    own = pl.BlockSpec((2, None, sources, block_size), lambda f, r, c, n: (0, f, 0, r))
    grid_spec = pltpu.PrefetchScalarGridSpec(
        num_scalar_prefetch=2,
        grid=(local_freqs, local_blocks),
        in_specs=[
            pl.BlockSpec(memory_space=pltpu.SMEM),
            pl.BlockSpec((2, None, sources, span), lambda f, r, c, n: (0, f, 0, 0)),
            own,
            own,
            pl.BlockSpec((None, None, depth, width), lambda f, r, c, n: (f, r, 0, 0)),
        ],
        out_specs=[
            own,
            part_spec(rim),
            part_spec(own_rows),
            part_spec(rim),
            pl.BlockSpec((None, 8, 128), lambda f, r, c, n: (f, 0, 0)),
        ],
        scratch_shapes=[
            pltpu.VMEM((sources, width), jnp.bfloat16),
            pltpu.VMEM((2, sources, span), jnp.float32),
        ],
    )
    return pl.pallas_call(
        _both_kernel,
        grid_spec=grid_spec,
        out_shape=[
            jax.ShapeDtypeStruct(raw.shape, jnp.float32),
            part_shape(rim),
            part_shape(own_rows),
            part_shape(rim),
            jax.ShapeDtypeStruct((local_freqs, 8, 128), jnp.float32),
        ],
        compiler_params=pltpu.CompilerParams(dimension_semantics=("arbitrary", "arbitrary")),
        cost_estimate=pl.CostEstimate(
            flops=4 * local_freqs * local_blocks * sources * depth * width,
            transcendentals=0,
            bytes_accessed=stacked.size * 2 + extended.size * 2 + raw.size * 40,
        ),
    )(cols, counts, coefs, extended, raw, left, stacked)


def apply_forward(extended, stacked, cols, counts):
    local_freqs, local_blocks, depth, width = stacked.shape
    block_size = depth // 2
    _, _, sources, span = extended.shape
    grid_spec = pltpu.PrefetchScalarGridSpec(
        num_scalar_prefetch=2,
        grid=(local_freqs, local_blocks),
        in_specs=[
            pl.BlockSpec((2, None, sources, span), lambda f, r, c, n: (0, f, 0, 0)),
            pl.BlockSpec((None, None, depth, width), lambda f, r, c, n: (f, r, 0, 0)),
        ],
        out_specs=pl.BlockSpec((2, None, sources, block_size), lambda f, r, c, n: (0, f, 0, r)),
        scratch_shapes=[pltpu.VMEM((sources, width), jnp.bfloat16)],
    )
    return pl.pallas_call(
        _forward_kernel,
        grid_spec=grid_spec,
        out_shape=jax.ShapeDtypeStruct(
            (2, local_freqs, sources, local_blocks * block_size), jnp.float32
        ),
        compiler_params=pltpu.CompilerParams(dimension_semantics=("arbitrary", "arbitrary")),
        cost_estimate=pl.CostEstimate(
            flops=2 * local_freqs * local_blocks * sources * depth * width,
            transcendentals=0,
            bytes_accessed=stacked.size * 2 + extended.size * 2 + extended.size * 4,
        ),
    )(cols, counts, extended, stacked)


def apply_adjoint(rounded, stacked, cols, counts, span):
    local_freqs, local_blocks, depth, width = stacked.shape
    block_size = depth // 2
    sources = rounded.shape[2]
    own = local_blocks * block_size
    rim = (span - own) // 2
    part_spec, part_shape = _part_specs(local_freqs, sources)
    grid_spec = pltpu.PrefetchScalarGridSpec(
        num_scalar_prefetch=2,
        grid=(local_freqs, local_blocks),
        in_specs=[
            pl.BlockSpec((2, None, sources, block_size), lambda f, r, c, n: (0, f, 0, r)),
            pl.BlockSpec((None, None, depth, width), lambda f, r, c, n: (f, r, 0, 0)),
        ],
        out_specs=[part_spec(rim), part_spec(own), part_spec(rim)],
        scratch_shapes=[pltpu.VMEM((2, sources, span), jnp.float32)],
    )
    return pl.pallas_call(
        _adjoint_kernel,
        grid_spec=grid_spec,
        out_shape=[part_shape(rim), part_shape(own), part_shape(rim)],
        compiler_params=pltpu.CompilerParams(dimension_semantics=("arbitrary", "arbitrary")),
        cost_estimate=pl.CostEstimate(
            flops=2 * local_freqs * local_blocks * sources * depth * width,
            transcendentals=0,
            bytes_accessed=stacked.size * 2 + rounded.size * 2 + rounded.size * 12,
        ),
    )(cols, counts, rounded, stacked)


def body(up_time, down_blocks, block_cols, block_counts):
    freq_groups = lax.axis_size("freq")
    receiver_groups = lax.axis_size("rcv")
    shot_count, time_steps, receivers = up_time.shape
    local_freqs, local_blocks, slot_count, _, block_size, _ = down_blocks.shape
    local_rows = receivers // receiver_groups
    reach_blocks = (slot_count - 1) // 2
    rim_rows = reach_blocks * block_size
    span_blocks = local_blocks + 2 * reach_blocks
    fourier = fourier_table(time_steps, freq_groups, local_freqs)
    spectrum = jnp.einsum(
        "snr,ncgf->cfsgr", up_time, fourier, preferred_element_type=jnp.float32
    ).astype(jnp.bfloat16)
    spectrum = spectrum.reshape(
        2, local_freqs, shot_count, freq_groups, receiver_groups, local_rows
    )
    by_freq = lax.all_to_all(spectrum, "freq", split_axis=3, concat_axis=2, tiled=True)
    received = lax.all_to_all(by_freq, "rcv", split_axis=4, concat_axis=3, tiled=True)
    right_side = received.reshape(2, local_freqs, -1, local_rows).astype(jnp.float32)
    position = lax.axis_index("rcv")
    columns = jnp.clip(
        block_cols - position * local_blocks + reach_blocks, 0, span_blocks - 1
    ).reshape(-1)
    counts = jnp.clip(block_counts, 0, slot_count).reshape(-1)
    stacked = stack_blocks(down_blocks, counts)

    def exchange(lower_rim, middle, upper_rim):
        from_above = from_behind(lower_rim, "rcv", -1)
        from_below = from_behind(upper_rim, "rcv", 1)
        middle = middle.at[..., :rim_rows].add(from_below)
        middle = middle.at[..., local_rows - rim_rows :].add(from_above)
        return middle

    def adjoint(field):
        rounded = field.astype(jnp.bfloat16)
        parts = apply_adjoint(rounded, stacked, columns, counts, span_blocks * block_size)
        return field + exchange(*parts)

    def forward_adjoint(raw, scale, left, shift):
        extended = with_halo(raw.astype(jnp.bfloat16), (("rcv", 3),), rim_rows)
        coefs = jnp.stack(
            [jnp.broadcast_to(scale, shift.shape).reshape(-1), shift.reshape(-1)], axis=1
        ).reshape(-1)
        residual, lower, middle, upper, partial = apply_both(
            extended, raw, left, coefs, stacked, columns, counts
        )
        total = rcv_sum(partial[:, 0, 0])[None, :, None, None]
        return residual, residual + exchange(lower, middle, upper), total

    def forward(field):
        extended = with_halo(field.astype(jnp.bfloat16), (("rcv", 3),), rim_rows)
        return field + apply_forward(extended, stacked, columns, counts)

    lifted = adjoint(right_side)
    right_squares, lifted_squares = both_squares(right_side, lifted)
    beta_norm = jnp.sqrt(right_squares + EPSILON)
    alpha_norm = jnp.sqrt(lifted_squares / (beta_norm * beta_norm) + EPSILON)
    left_vector = right_side / beta_norm
    right_raw = lifted
    right_scale = beta_norm * alpha_norm
    right_vector = right_raw / right_scale
    search_direction = right_vector
    solution = jnp.zeros_like(right_side)
    phibar = beta_norm
    rhobar = alpha_norm
    for iteration in range(ITERS):
        last = iteration == ITERS - 1
        residual_left, lifted, left_squares = forward_adjoint(
            right_raw, right_scale, left_vector, alpha_norm
        )
        beta_norm = jnp.sqrt(left_squares + EPSILON)
        left_vector = residual_left / beta_norm
        residual_right = lifted / beta_norm - beta_norm * right_vector
        rho_value = jnp.sqrt(rhobar * rhobar + beta_norm * beta_norm)
        cosine = rhobar / rho_value
        sine_value = beta_norm / rho_value
        phi_value = cosine * phibar
        phibar = sine_value * phibar
        solution = solution + phi_value / rho_value * search_direction
        if last:
            break
        alpha_norm = jnp.sqrt(squares(residual_right) + EPSILON)
        right_raw = residual_right
        right_scale = alpha_norm
        right_vector = residual_right / alpha_norm
        theta_value = sine_value * alpha_norm
        rhobar = -cosine * alpha_norm
        search_direction = right_vector - theta_value / rho_value * search_direction
    return (solution, phibar * cosine * residual_right)


def solution(mesh):
    return jax.shard_map(
        body,
        mesh=mesh,
        in_specs=(
            P(("freq", "rcv"), None, None),
            P("freq", "rcv", None, None, None, None),
            P("freq", "rcv", None),
            P("freq", "rcv"),
        ),
        out_specs=(P(None, "freq", None, "rcv"), P(None, "freq", None, "rcv")),
        check_vma=False,
    )
```

```python
import functools
import math

import jax
import jax.numpy as jnp
from jax import lax
from jax.experimental import pallas as pl
from jax.experimental.pallas import tpu as pltpu
from jax.sharding import PartitionSpec as P

ITERS = 2


EPSILON = 1e-06


def with_halo(cells, sides, width):
    for axis, dim in sides:
        count = lax.axis_size(axis)
        ends = count - 1
        head = lax.slice_in_dim(cells, 0, width, axis=dim)
        tail = lax.slice_in_dim(cells, cells.shape[dim] - width, cells.shape[dim], axis=dim)
        cells = jnp.concatenate(
            [
                lax.ppermute(tail, axis, [(i, (i + 1) % count) for i in range(ends)]),
                cells,
                lax.ppermute(head, axis, [((i + 1) % count, i) for i in range(ends)]),
            ],
            axis=dim,
        )
    return cells


def from_behind(value, axis, steps):
    count = lax.axis_size(axis)
    first, last = (max(0, -steps), min(count, count - steps))
    return lax.ppermute(value, axis, [(source, source + steps) for source in range(first, last)])


def fourier_table(time_steps, freq_groups, local_freqs):
    shape = (time_steps, freq_groups, local_freqs)
    sample = lax.broadcasted_iota(jnp.int32, shape, 0)
    harmonic = (
        lax.broadcasted_iota(jnp.int32, shape, 1) * local_freqs
        + lax.broadcasted_iota(jnp.int32, shape, 2)
        + 1
    )
    phase_angle = 2.0 * math.pi / time_steps * (harmonic * sample % time_steps).astype(jnp.float32)
    scale_factor = 1.0 / math.sqrt(time_steps)
    return jnp.stack(
        [jnp.cos(phase_angle) * scale_factor, -jnp.sin(phase_angle) * scale_factor], axis=1
    ).astype(jnp.bfloat16)


def rcv_sum(partial):
    count = lax.axis_size("rcv")
    spread = jnp.broadcast_to(partial[None], (count,) + partial.shape)
    gathered = lax.all_to_all(spread, "rcv", 0, 0, tiled=False)
    return jnp.sum(gathered, axis=0)


def squares(field):
    return rcv_sum(jnp.sum(field * field, axis=(0, 2, 3)))[None, :, None, None]


def both_squares(first, second):
    partial = jnp.stack(
        [jnp.sum(first * first, axis=(0, 2, 3)), jnp.sum(second * second, axis=(0, 2, 3))]
    )
    total = rcv_sum(partial)
    return total[0][None, :, None, None], total[1][None, :, None, None]


def _stack_kernel(counts_ref, a_ref, m_ref):
    slots, _, block, _ = a_ref.shape
    count = counts_ref[pl.program_id(0) * pl.num_programs(1) + pl.program_id(1)]
    for slot in range(slots):
        live = slot < count
        real_part = jnp.where(live, a_ref[slot, 0], jnp.zeros_like(a_ref[slot, 0]))
        imaginary = jnp.where(live, a_ref[slot, 1], jnp.zeros_like(a_ref[slot, 1]))
        left = slice(2 * slot * block, (2 * slot + 1) * block)
        right = slice((2 * slot + 1) * block, (2 * slot + 2) * block)
        m_ref[:block, left] = real_part
        m_ref[:block, right] = -imaginary
        m_ref[block:, left] = imaginary
        m_ref[block:, right] = real_part


def stack_blocks(down_blocks, counts):
    local_freqs, local_blocks, slot_count, _, block_size, _ = down_blocks.shape
    width = 2 * slot_count * block_size
    grid_spec = pltpu.PrefetchScalarGridSpec(
        num_scalar_prefetch=1,
        grid=(local_freqs, local_blocks),
        in_specs=[
            pl.BlockSpec(
                (None, None, slot_count, 2, block_size, block_size),
                lambda f, r, n: (f, r, 0, 0, 0, 0),
            )
        ],
        out_specs=pl.BlockSpec(
            (None, None, 2 * block_size, width), lambda f, r, n: (f, r, 0, 0)
        ),
    )
    return pl.pallas_call(
        _stack_kernel,
        grid_spec=grid_spec,
        out_shape=jax.ShapeDtypeStruct(
            (local_freqs, local_blocks, 2 * block_size, width), jnp.bfloat16
        ),
    )(counts, down_blocks)


def _forward_kernel(cols_ref, counts_ref, x_ref, m_ref, o_ref, picked_ref):
    freq = pl.program_id(0)
    row = pl.program_id(1)
    rows = pl.num_programs(1)
    depth, width = m_ref.shape
    block = depth // 2
    slots = width // depth
    index = freq * rows + row
    count = counts_ref[index]
    for slot in range(slots):
        start = pl.multiple_of(cols_ref[index * slots + slot] * block, block)
        for part in range(2):
            taken = x_ref[part, :, pl.ds(start, block)]
            lanes = slice((2 * slot + part) * block, (2 * slot + part + 1) * block)
            picked_ref[:, lanes] = jnp.where(slot < count, taken, jnp.zeros_like(taken))
    contract = (((1,), (1,)), ((), ()))
    product = lax.dot_general(
        picked_ref[...], m_ref[...], contract, preferred_element_type=jnp.float32
    )
    o_ref[0] = product[:, :block]
    o_ref[1] = product[:, block:]


def _scatter(cols_ref, index, field, m_ref, acc_ref):
    depth, width = m_ref.shape
    block = depth // 2
    slots = width // depth
    spread = jnp.dot(field, m_ref[...], preferred_element_type=jnp.float32)
    for slot in range(slots):
        start = pl.multiple_of(cols_ref[index * slots + slot] * block, block)
        for part in range(2):
            lanes = slice((2 * slot + part) * block, (2 * slot + part + 1) * block)
            acc_ref[part, :, pl.ds(start, block)] += spread[:, lanes]


def _split(acc_ref, lower_ref, middle_ref, upper_ref):
    rim = lower_ref.shape[-1]
    own = middle_ref.shape[-1]
    lower_ref[...] = acc_ref[:, :, :rim]
    middle_ref[...] = acc_ref[:, :, rim : rim + own]
    upper_ref[...] = acc_ref[:, :, rim + own :]


def _adjoint_kernel(
    cols_ref, counts_ref, u_ref, m_ref, lower_ref, middle_ref, upper_ref, acc_ref, *, first
):
    freq = pl.program_id(0) + first
    row = pl.program_id(1)
    rows = pl.num_programs(1)

    @pl.when(row == 0)
    def _():
        acc_ref[...] = jnp.zeros(acc_ref.shape, acc_ref.dtype)

    field = jnp.concatenate([u_ref[0], u_ref[1]], axis=1)
    _scatter(cols_ref, freq * rows + row, field, m_ref, acc_ref)

    @pl.when(row == rows - 1)
    def _():
        _split(acc_ref, lower_ref, middle_ref, upper_ref)


def _both_kernel(
    cols_ref,
    counts_ref,
    coef_ref,
    x_ref,
    q_ref,
    u_ref,
    m_ref,
    p_ref,
    lower_ref,
    middle_ref,
    upper_ref,
    squares_ref,
    picked_ref,
    acc_ref,
    *,
    first,
):
    freq = pl.program_id(0) + first
    row = pl.program_id(1)
    rows = pl.num_programs(1)
    depth, width = m_ref.shape
    block = depth // 2
    slots = width // depth
    index = freq * rows + row

    @pl.when(row == 0)
    def _():
        acc_ref[...] = jnp.zeros(acc_ref.shape, acc_ref.dtype)
        squares_ref[...] = jnp.zeros(squares_ref.shape, squares_ref.dtype)

    for slot in range(slots):
        start = pl.multiple_of(cols_ref[index * slots + slot] * block, block)
        for part in range(2):
            lanes = slice((2 * slot + part) * block, (2 * slot + part + 1) * block)
            picked_ref[:, lanes] = x_ref[part, :, pl.ds(start, block)]
    contract = (((1,), (1,)), ((), ()))
    product = lax.dot_general(
        picked_ref[...], m_ref[...], contract, preferred_element_type=jnp.float32
    )
    scale = coef_ref[2 * freq]
    shift = coef_ref[2 * freq + 1]
    for part in range(2):
        lanes = slice(part * block, (part + 1) * block)
        p_ref[part] = (q_ref[part] + product[:, lanes]) / scale - shift * u_ref[part]
    total = jnp.sum(p_ref[0] * p_ref[0] + p_ref[1] * p_ref[1], axis=(0, 1), keepdims=True)
    squares_ref[...] += jnp.broadcast_to(total, squares_ref.shape)
    field = jnp.concatenate(
        [p_ref[0].astype(jnp.bfloat16), p_ref[1].astype(jnp.bfloat16)], axis=1
    )
    _scatter(cols_ref, index, field, m_ref, acc_ref)

    @pl.when(row == rows - 1)
    def _():
        _split(acc_ref, lower_ref, middle_ref, upper_ref)


def _part_specs(local_freqs, sources):
    def part_spec(lanes):
        return pl.BlockSpec((2, None, sources, lanes), lambda f, r, c, n: (0, f, 0, 0))

    def part_shape(lanes):
        return jax.ShapeDtypeStruct((2, local_freqs, sources, lanes), jnp.float32)

    return part_spec, part_shape


def apply_both(extended, raw, left, coefs, stacked, cols, counts, first):
    _, local_blocks, depth, width = stacked.shape
    local_freqs = 1
    block_size = depth // 2
    _, _, sources, span = extended.shape
    own_rows = local_blocks * block_size
    rim = (span - own_rows) // 2
    part_spec, part_shape = _part_specs(local_freqs, sources)
    own = pl.BlockSpec((2, None, sources, block_size), lambda f, r, c, n: (0, f, 0, r))
    taken = pl.BlockSpec((2, None, sources, block_size), lambda f, r, c, n: (0, f + first, 0, r))
    grid_spec = pltpu.PrefetchScalarGridSpec(
        num_scalar_prefetch=2,
        grid=(local_freqs, local_blocks),
        in_specs=[
            pl.BlockSpec(memory_space=pltpu.SMEM),
            pl.BlockSpec((2, None, sources, span), lambda f, r, c, n: (0, f + first, 0, 0)),
            taken,
            taken,
            pl.BlockSpec((None, None, depth, width), lambda f, r, c, n: (f + first, r, 0, 0)),
        ],
        out_specs=[
            own,
            part_spec(rim),
            part_spec(own_rows),
            part_spec(rim),
            pl.BlockSpec((None, 8, 128), lambda f, r, c, n: (f, 0, 0)),
        ],
        scratch_shapes=[
            pltpu.VMEM((sources, width), jnp.bfloat16),
            pltpu.VMEM((2, sources, span), jnp.float32),
        ],
    )
    return pl.pallas_call(
        functools.partial(_both_kernel, first=first),
        grid_spec=grid_spec,
        out_shape=[
            jax.ShapeDtypeStruct((2, local_freqs) + raw.shape[2:], jnp.float32),
            part_shape(rim),
            part_shape(own_rows),
            part_shape(rim),
            jax.ShapeDtypeStruct((local_freqs, 8, 128), jnp.float32),
        ],
        compiler_params=pltpu.CompilerParams(dimension_semantics=("arbitrary", "arbitrary")),
        cost_estimate=pl.CostEstimate(
            flops=4 * local_blocks * sources * depth * width,
            transcendentals=0,
            bytes_accessed=(stacked.size + extended.size + raw.size * 20) // stacked.shape[0] * 2,
        ),
    )(cols, counts, coefs, extended, raw, left, stacked)


def apply_forward(extended, stacked, cols, counts):
    local_freqs, local_blocks, depth, width = stacked.shape
    block_size = depth // 2
    _, _, sources, span = extended.shape
    grid_spec = pltpu.PrefetchScalarGridSpec(
        num_scalar_prefetch=2,
        grid=(local_freqs, local_blocks),
        in_specs=[
            pl.BlockSpec((2, None, sources, span), lambda f, r, c, n: (0, f, 0, 0)),
            pl.BlockSpec((None, None, depth, width), lambda f, r, c, n: (f, r, 0, 0)),
        ],
        out_specs=pl.BlockSpec((2, None, sources, block_size), lambda f, r, c, n: (0, f, 0, r)),
        scratch_shapes=[pltpu.VMEM((sources, width), jnp.bfloat16)],
    )
    return pl.pallas_call(
        _forward_kernel,
        grid_spec=grid_spec,
        out_shape=jax.ShapeDtypeStruct(
            (2, local_freqs, sources, local_blocks * block_size), jnp.float32
        ),
        compiler_params=pltpu.CompilerParams(dimension_semantics=("arbitrary", "arbitrary")),
        cost_estimate=pl.CostEstimate(
            flops=2 * local_freqs * local_blocks * sources * depth * width,
            transcendentals=0,
            bytes_accessed=stacked.size * 2 + extended.size * 2 + extended.size * 4,
        ),
    )(cols, counts, extended, stacked)


def apply_adjoint(rounded, stacked, cols, counts, span, first):
    _, local_blocks, depth, width = stacked.shape
    local_freqs = 1
    block_size = depth // 2
    sources = rounded.shape[2]
    own = local_blocks * block_size
    rim = (span - own) // 2
    part_spec, part_shape = _part_specs(local_freqs, sources)
    grid_spec = pltpu.PrefetchScalarGridSpec(
        num_scalar_prefetch=2,
        grid=(local_freqs, local_blocks),
        in_specs=[
            pl.BlockSpec(
                (2, None, sources, block_size), lambda f, r, c, n: (0, f + first, 0, r)
            ),
            pl.BlockSpec((None, None, depth, width), lambda f, r, c, n: (f + first, r, 0, 0)),
        ],
        out_specs=[part_spec(rim), part_spec(own), part_spec(rim)],
        scratch_shapes=[pltpu.VMEM((2, sources, span), jnp.float32)],
    )
    return pl.pallas_call(
        functools.partial(_adjoint_kernel, first=first),
        grid_spec=grid_spec,
        out_shape=[part_shape(rim), part_shape(own), part_shape(rim)],
        compiler_params=pltpu.CompilerParams(dimension_semantics=("arbitrary", "arbitrary")),
        cost_estimate=pl.CostEstimate(
            flops=2 * local_freqs * local_blocks * sources * depth * width,
            transcendentals=0,
            bytes_accessed=stacked.size * 2 + rounded.size * 2 + rounded.size * 12,
        ),
    )(cols, counts, rounded, stacked)


def body(up_time, down_blocks, block_cols, block_counts):
    freq_groups = lax.axis_size("freq")
    receiver_groups = lax.axis_size("rcv")
    shot_count, time_steps, receivers = up_time.shape
    local_freqs, local_blocks, slot_count, _, block_size, _ = down_blocks.shape
    local_rows = receivers // receiver_groups
    reach_blocks = (slot_count - 1) // 2
    rim_rows = reach_blocks * block_size
    span_blocks = local_blocks + 2 * reach_blocks
    fourier = fourier_table(time_steps, freq_groups, local_freqs)
    spectrum = jnp.einsum(
        "snr,ncgf->cfsgr", up_time, fourier, preferred_element_type=jnp.float32
    ).astype(jnp.bfloat16)
    spectrum = spectrum.reshape(
        2, local_freqs, shot_count, freq_groups * receiver_groups, local_rows
    )
    received = lax.all_to_all(spectrum, ("freq", "rcv"), split_axis=3, concat_axis=2, tiled=True)
    right_side = received.reshape(2, local_freqs, -1, local_rows).astype(jnp.float32)
    position = lax.axis_index("rcv")
    columns = jnp.clip(
        block_cols - position * local_blocks + reach_blocks, 0, span_blocks - 1
    ).reshape(-1)
    counts = jnp.clip(block_counts, 0, slot_count).reshape(-1)
    stacked = stack_blocks(down_blocks, counts)

    def exchange(lower_rim, middle, upper_rim):
        from_above = from_behind(lower_rim, "rcv", -1)
        from_below = from_behind(upper_rim, "rcv", 1)
        middle = middle.at[..., :rim_rows].add(from_below)
        middle = middle.at[..., local_rows - rim_rows :].add(from_above)
        return middle

    def adjoint(field):
        rounded = field.astype(jnp.bfloat16)
        pieces = [
            exchange(*apply_adjoint(rounded, stacked, columns, counts, span_blocks * block_size, f))
            for f in range(local_freqs)
        ]
        return field + jnp.concatenate(pieces, axis=1)

    def forward_adjoint(raw, scale, left, shift):
        extended = with_halo(raw.astype(jnp.bfloat16), (("rcv", 3),), rim_rows)
        coefs = jnp.stack(
            [jnp.broadcast_to(scale, shift.shape).reshape(-1), shift.reshape(-1)], axis=1
        ).reshape(-1)
        results = [
            apply_both(extended, raw, left, coefs, stacked, columns, counts, f)
            for f in range(local_freqs)
        ]
        residual = jnp.concatenate([piece[0] for piece in results], axis=1)
        spread = jnp.concatenate([exchange(*piece[1:4]) for piece in results], axis=1)
        partial = jnp.concatenate([piece[4][:, 0, 0] for piece in results])
        total = rcv_sum(partial)[None, :, None, None]
        return residual, residual + spread, total

    def forward(field):
        extended = with_halo(field.astype(jnp.bfloat16), (("rcv", 3),), rim_rows)
        return field + apply_forward(extended, stacked, columns, counts)

    lifted = adjoint(right_side)
    right_squares, lifted_squares = both_squares(right_side, lifted)
    beta_norm = jnp.sqrt(right_squares + EPSILON)
    alpha_norm = jnp.sqrt(lifted_squares / (beta_norm * beta_norm) + EPSILON)
    left_vector = right_side / beta_norm
    right_raw = lifted
    right_scale = beta_norm * alpha_norm
    right_vector = right_raw / right_scale
    search_direction = right_vector
    solution = jnp.zeros_like(right_side)
    phibar = beta_norm
    rhobar = alpha_norm
    for iteration in range(ITERS):
        last = iteration == ITERS - 1
        residual_left, lifted, left_squares = forward_adjoint(
            right_raw, right_scale, left_vector, alpha_norm
        )
        beta_norm = jnp.sqrt(left_squares + EPSILON)
        left_vector = residual_left / beta_norm
        residual_right = lifted / beta_norm - beta_norm * right_vector
        rho_value = jnp.sqrt(rhobar * rhobar + beta_norm * beta_norm)
        cosine = rhobar / rho_value
        sine_value = beta_norm / rho_value
        phi_value = cosine * phibar
        phibar = sine_value * phibar
        solution = solution + phi_value / rho_value * search_direction
        if last:
            break
        alpha_norm = jnp.sqrt(squares(residual_right) + EPSILON)
        right_raw = residual_right
        right_scale = alpha_norm
        right_vector = residual_right / alpha_norm
        theta_value = sine_value * alpha_norm
        rhobar = -cosine * alpha_norm
        search_direction = right_vector - theta_value / rho_value * search_direction
    return (solution, phibar * cosine * residual_right)


def solution(mesh):
    return jax.shard_map(
        body,
        mesh=mesh,
        in_specs=(
            P(("freq", "rcv"), None, None),
            P("freq", "rcv", None, None, None, None),
            P("freq", "rcv", None),
            P("freq", "rcv"),
        ),
        out_specs=(P(None, "freq", None, "rcv"), P(None, "freq", None, "rcv")),
        check_vma=False,
    )
```

```python
import math

import jax
import jax.numpy as jnp
from jax import lax
from jax.experimental import pallas as pl
from jax.experimental.pallas import tpu as pltpu
from jax.sharding import PartitionSpec as P

ITERS = 2


EPSILON = 1e-06


def with_halo(cells, sides, width):
    for axis, dim in sides:
        count = lax.axis_size(axis)
        ends = count - 1
        head = lax.slice_in_dim(cells, 0, width, axis=dim)
        tail = lax.slice_in_dim(cells, cells.shape[dim] - width, cells.shape[dim], axis=dim)
        cells = jnp.concatenate(
            [
                lax.ppermute(tail, axis, [(i, (i + 1) % count) for i in range(ends)]),
                cells,
                lax.ppermute(head, axis, [((i + 1) % count, i) for i in range(ends)]),
            ],
            axis=dim,
        )
    return cells


def from_behind(value, axis, steps):
    count = lax.axis_size(axis)
    first, last = (max(0, -steps), min(count, count - steps))
    return lax.ppermute(value, axis, [(source, source + steps) for source in range(first, last)])


def fourier_table(time_steps, freq_groups, local_freqs):
    shape = (time_steps, freq_groups, local_freqs)
    sample = lax.broadcasted_iota(jnp.int32, shape, 0)
    harmonic = (
        lax.broadcasted_iota(jnp.int32, shape, 1) * local_freqs
        + lax.broadcasted_iota(jnp.int32, shape, 2)
        + 1
    )
    phase_angle = 2.0 * math.pi / time_steps * (harmonic * sample % time_steps).astype(jnp.float32)
    scale_factor = 1.0 / math.sqrt(time_steps)
    return jnp.stack(
        [jnp.cos(phase_angle) * scale_factor, -jnp.sin(phase_angle) * scale_factor], axis=1
    ).astype(jnp.bfloat16)


def rcv_sum(partial):
    count = lax.axis_size("rcv")
    spread = jnp.broadcast_to(partial[None], (count,) + partial.shape)
    gathered = lax.all_to_all(spread, "rcv", 0, 0, tiled=False)
    return jnp.sum(gathered, axis=0)


def squares(field):
    return rcv_sum(jnp.sum(field * field, axis=(0, 2, 3)))[None, :, None, None]


def both_squares(first, second):
    partial = jnp.stack(
        [jnp.sum(first * first, axis=(0, 2, 3)), jnp.sum(second * second, axis=(0, 2, 3))]
    )
    total = rcv_sum(partial)
    return total[0][None, :, None, None], total[1][None, :, None, None]


def _stack_kernel(counts_ref, a_ref, m_ref):
    slots, _, block, _ = a_ref.shape
    count = counts_ref[pl.program_id(0) * pl.num_programs(1) + pl.program_id(1)]
    for slot in range(slots):
        live = slot < count
        real_part = jnp.where(live, a_ref[slot, 0], jnp.zeros_like(a_ref[slot, 0]))
        imaginary = jnp.where(live, a_ref[slot, 1], jnp.zeros_like(a_ref[slot, 1]))
        left = slice(2 * slot * block, (2 * slot + 1) * block)
        right = slice((2 * slot + 1) * block, (2 * slot + 2) * block)
        m_ref[:block, left] = real_part
        m_ref[:block, right] = -imaginary
        m_ref[block:, left] = imaginary
        m_ref[block:, right] = real_part


def stack_blocks(down_blocks, counts):
    local_freqs, local_blocks, slot_count, _, block_size, _ = down_blocks.shape
    width = 2 * slot_count * block_size
    grid_spec = pltpu.PrefetchScalarGridSpec(
        num_scalar_prefetch=1,
        grid=(local_freqs, local_blocks),
        in_specs=[
            pl.BlockSpec(
                (None, None, slot_count, 2, block_size, block_size),
                lambda f, r, n: (f, r, 0, 0, 0, 0),
            )
        ],
        out_specs=pl.BlockSpec(
            (None, None, 2 * block_size, width), lambda f, r, n: (f, r, 0, 0)
        ),
    )
    return pl.pallas_call(
        _stack_kernel,
        grid_spec=grid_spec,
        out_shape=jax.ShapeDtypeStruct(
            (local_freqs, local_blocks, 2 * block_size, width), jnp.bfloat16
        ),
    )(counts, down_blocks)


def _forward_kernel(cols_ref, counts_ref, x_ref, m_ref, o_ref, picked_ref):
    freq = pl.program_id(0)
    row = pl.program_id(1)
    rows = pl.num_programs(1)
    depth, width = m_ref.shape
    block = depth // 2
    slots = width // depth
    index = freq * rows + row
    count = counts_ref[index]
    for slot in range(slots):
        start = pl.multiple_of(cols_ref[index * slots + slot] * block, block)
        for part in range(2):
            taken = x_ref[part, :, pl.ds(start, block)]
            lanes = slice((2 * slot + part) * block, (2 * slot + part + 1) * block)
            picked_ref[:, lanes] = jnp.where(slot < count, taken, jnp.zeros_like(taken))
    contract = (((1,), (1,)), ((), ()))
    product = lax.dot_general(
        picked_ref[...], m_ref[...], contract, preferred_element_type=jnp.float32
    )
    o_ref[0] = product[:, :block]
    o_ref[1] = product[:, block:]


def _scatter(cols_ref, index, field, m_ref, acc_ref):
    depth, width = m_ref.shape
    block = depth // 2
    slots = width // depth
    spread = jnp.dot(field, m_ref[...], preferred_element_type=jnp.float32)
    for slot in range(slots):
        start = pl.multiple_of(cols_ref[index * slots + slot] * block, block)
        for part in range(2):
            lanes = slice((2 * slot + part) * block, (2 * slot + part + 1) * block)
            acc_ref[part, :, pl.ds(start, block)] += spread[:, lanes]


def _split(acc_ref, lower_ref, middle_ref, upper_ref):
    rim = lower_ref.shape[-1]
    own = middle_ref.shape[-1]
    lower_ref[...] = acc_ref[:, :, :rim]
    middle_ref[...] = acc_ref[:, :, rim : rim + own]
    upper_ref[...] = acc_ref[:, :, rim + own :]


def _adjoint_kernel(cols_ref, counts_ref, u_ref, m_ref, lower_ref, middle_ref, upper_ref, acc_ref):
    freq = pl.program_id(0)
    row = pl.program_id(1)
    rows = pl.num_programs(1)

    @pl.when(row == 0)
    def _():
        acc_ref[...] = jnp.zeros(acc_ref.shape, acc_ref.dtype)

    field = jnp.concatenate([u_ref[0], u_ref[1]], axis=1)
    _scatter(cols_ref, freq * rows + row, field, m_ref, acc_ref)

    @pl.when(row == rows - 1)
    def _():
        _split(acc_ref, lower_ref, middle_ref, upper_ref)


def _both_kernel(
    cols_ref,
    counts_ref,
    coef_ref,
    below_ref,
    own_ref,
    above_ref,
    q_ref,
    u_ref,
    m_ref,
    p_ref,
    lower_ref,
    middle_ref,
    upper_ref,
    squares_ref,
    picked_ref,
    acc_ref,
):
    freq = pl.program_id(0)
    row = pl.program_id(1)
    rows = pl.num_programs(1)
    depth, width = m_ref.shape
    block = depth // 2
    slots = width // depth
    index = freq * rows + row

    @pl.when(row == 0)
    def _():
        acc_ref[...] = jnp.zeros(acc_ref.shape, acc_ref.dtype)
        squares_ref[...] = jnp.zeros(squares_ref.shape, squares_ref.dtype)

    rim_blocks = below_ref.shape[-1] // block
    own_blocks = own_ref.shape[-1] // block
    pieces = (
        (below_ref, 0, rim_blocks),
        (own_ref, rim_blocks, rim_blocks + own_blocks),
        (above_ref, rim_blocks + own_blocks, 2 * rim_blocks + own_blocks),
    )
    for slot in range(slots):
        column = cols_ref[index * slots + slot]
        for source, first, end in pieces:

            @pl.when((column >= first) & (column < end))
            def _():
                start = pl.multiple_of((column - first) * block, block)
                for part in range(2):
                    lanes = slice((2 * slot + part) * block, (2 * slot + part + 1) * block)
                    picked_ref[:, lanes] = source[part, :, pl.ds(start, block)]

    contract = (((1,), (1,)), ((), ()))
    product = lax.dot_general(
        picked_ref[...], m_ref[...], contract, preferred_element_type=jnp.float32
    )
    scale = coef_ref[2 * freq]
    shift = coef_ref[2 * freq + 1]
    for part in range(2):
        lanes = slice(part * block, (part + 1) * block)
        p_ref[part] = (q_ref[part] + product[:, lanes]) / scale - shift * u_ref[part]
    total = jnp.sum(p_ref[0] * p_ref[0] + p_ref[1] * p_ref[1], axis=(0, 1), keepdims=True)
    squares_ref[...] += jnp.broadcast_to(total, squares_ref.shape)
    field = jnp.concatenate(
        [p_ref[0].astype(jnp.bfloat16), p_ref[1].astype(jnp.bfloat16)], axis=1
    )
    _scatter(cols_ref, index, field, m_ref, acc_ref)

    @pl.when(row == rows - 1)
    def _():
        _split(acc_ref, lower_ref, middle_ref, upper_ref)


def _part_specs(local_freqs, sources):
    def part_spec(lanes):
        return pl.BlockSpec((2, None, sources, lanes), lambda f, r, c, n: (0, f, 0, 0))

    def part_shape(lanes):
        return jax.ShapeDtypeStruct((2, local_freqs, sources, lanes), jnp.float32)

    return part_spec, part_shape


def apply_both(below, own_field, above, raw, left, coefs, stacked, cols, counts):
    local_freqs, local_blocks, depth, width = stacked.shape
    block_size = depth // 2
    sources = raw.shape[2]
    own_rows = local_blocks * block_size
    rim = below.shape[-1]
    span = 2 * rim + own_rows
    part_spec, part_shape = _part_specs(local_freqs, sources)
    own = pl.BlockSpec((2, None, sources, block_size), lambda f, r, c, n: (0, f, 0, r))
    grid_spec = pltpu.PrefetchScalarGridSpec(
        num_scalar_prefetch=2,
        grid=(local_freqs, local_blocks),
        in_specs=[
            pl.BlockSpec(memory_space=pltpu.SMEM),
            part_spec(rim),
            part_spec(own_rows),
            part_spec(rim),
            own,
            own,
            pl.BlockSpec((None, None, depth, width), lambda f, r, c, n: (f, r, 0, 0)),
        ],
        out_specs=[
            own,
            part_spec(rim),
            part_spec(own_rows),
            part_spec(rim),
            pl.BlockSpec((None, 8, 128), lambda f, r, c, n: (f, 0, 0)),
        ],
        scratch_shapes=[
            pltpu.VMEM((sources, width), jnp.bfloat16),
            pltpu.VMEM((2, sources, span), jnp.float32),
        ],
    )
    return pl.pallas_call(
        _both_kernel,
        grid_spec=grid_spec,
        out_shape=[
            jax.ShapeDtypeStruct(raw.shape, jnp.float32),
            part_shape(rim),
            part_shape(own_rows),
            part_shape(rim),
            jax.ShapeDtypeStruct((local_freqs, 8, 128), jnp.float32),
        ],
        compiler_params=pltpu.CompilerParams(dimension_semantics=("arbitrary", "arbitrary")),
        cost_estimate=pl.CostEstimate(
            flops=4 * local_freqs * local_blocks * sources * depth * width,
            transcendentals=0,
            bytes_accessed=stacked.size * 2 + raw.size * 46,
        ),
    )(cols, counts, coefs, below, own_field, above, raw, left, stacked)


def apply_forward(extended, stacked, cols, counts):
    local_freqs, local_blocks, depth, width = stacked.shape
    block_size = depth // 2
    _, _, sources, span = extended.shape
    grid_spec = pltpu.PrefetchScalarGridSpec(
        num_scalar_prefetch=2,
        grid=(local_freqs, local_blocks),
        in_specs=[
            pl.BlockSpec((2, None, sources, span), lambda f, r, c, n: (0, f, 0, 0)),
            pl.BlockSpec((None, None, depth, width), lambda f, r, c, n: (f, r, 0, 0)),
        ],
        out_specs=pl.BlockSpec((2, None, sources, block_size), lambda f, r, c, n: (0, f, 0, r)),
        scratch_shapes=[pltpu.VMEM((sources, width), jnp.bfloat16)],
    )
    return pl.pallas_call(
        _forward_kernel,
        grid_spec=grid_spec,
        out_shape=jax.ShapeDtypeStruct(
            (2, local_freqs, sources, local_blocks * block_size), jnp.float32
        ),
        compiler_params=pltpu.CompilerParams(dimension_semantics=("arbitrary", "arbitrary")),
        cost_estimate=pl.CostEstimate(
            flops=2 * local_freqs * local_blocks * sources * depth * width,
            transcendentals=0,
            bytes_accessed=stacked.size * 2 + extended.size * 2 + extended.size * 4,
        ),
    )(cols, counts, extended, stacked)


def apply_adjoint(rounded, stacked, cols, counts, span):
    local_freqs, local_blocks, depth, width = stacked.shape
    block_size = depth // 2
    sources = rounded.shape[2]
    own = local_blocks * block_size
    rim = (span - own) // 2
    part_spec, part_shape = _part_specs(local_freqs, sources)
    grid_spec = pltpu.PrefetchScalarGridSpec(
        num_scalar_prefetch=2,
        grid=(local_freqs, local_blocks),
        in_specs=[
            pl.BlockSpec((2, None, sources, block_size), lambda f, r, c, n: (0, f, 0, r)),
            pl.BlockSpec((None, None, depth, width), lambda f, r, c, n: (f, r, 0, 0)),
        ],
        out_specs=[part_spec(rim), part_spec(own), part_spec(rim)],
        scratch_shapes=[pltpu.VMEM((2, sources, span), jnp.float32)],
    )
    return pl.pallas_call(
        _adjoint_kernel,
        grid_spec=grid_spec,
        out_shape=[part_shape(rim), part_shape(own), part_shape(rim)],
        compiler_params=pltpu.CompilerParams(dimension_semantics=("arbitrary", "arbitrary")),
        cost_estimate=pl.CostEstimate(
            flops=2 * local_freqs * local_blocks * sources * depth * width,
            transcendentals=0,
            bytes_accessed=stacked.size * 2 + rounded.size * 2 + rounded.size * 12,
        ),
    )(cols, counts, rounded, stacked)


def body(up_time, down_blocks, block_cols, block_counts):
    freq_groups = lax.axis_size("freq")
    receiver_groups = lax.axis_size("rcv")
    shot_count, time_steps, receivers = up_time.shape
    local_freqs, local_blocks, slot_count, _, block_size, _ = down_blocks.shape
    local_rows = receivers // receiver_groups
    reach_blocks = (slot_count - 1) // 2
    rim_rows = reach_blocks * block_size
    span_blocks = local_blocks + 2 * reach_blocks
    fourier = fourier_table(time_steps, freq_groups, local_freqs)
    spectrum = jnp.einsum(
        "snr,ncgf->cfsgr", up_time, fourier, preferred_element_type=jnp.float32
    ).astype(jnp.bfloat16)
    spectrum = spectrum.reshape(
        2, local_freqs, shot_count, freq_groups * receiver_groups, local_rows
    )
    received = lax.all_to_all(spectrum, ("freq", "rcv"), split_axis=3, concat_axis=2, tiled=True)
    right_side = received.reshape(2, local_freqs, -1, local_rows).astype(jnp.float32)
    position = lax.axis_index("rcv")
    columns = jnp.clip(
        block_cols - position * local_blocks + reach_blocks, 0, span_blocks - 1
    ).reshape(-1)
    counts = jnp.clip(block_counts, 0, slot_count).reshape(-1)
    stacked = stack_blocks(down_blocks, counts)

    def exchange(lower_rim, middle, upper_rim):
        from_above = from_behind(lower_rim, "rcv", -1)
        from_below = from_behind(upper_rim, "rcv", 1)
        middle = middle.at[..., :rim_rows].add(from_below)
        middle = middle.at[..., local_rows - rim_rows :].add(from_above)
        return middle

    def adjoint(field):
        rounded = field.astype(jnp.bfloat16)
        parts = apply_adjoint(rounded, stacked, columns, counts, span_blocks * block_size)
        return field + exchange(*parts)

    def forward_adjoint(raw, scale, left, shift):
        rounded = raw.astype(jnp.bfloat16)
        below = from_behind(rounded[..., local_rows - rim_rows :], "rcv", 1)
        above = from_behind(rounded[..., :rim_rows], "rcv", -1)
        coefs = jnp.stack(
            [jnp.broadcast_to(scale, shift.shape).reshape(-1), shift.reshape(-1)], axis=1
        ).reshape(-1)
        residual, lower, middle, upper, partial = apply_both(
            below, rounded, above, raw, left, coefs, stacked, columns, counts
        )
        total = rcv_sum(partial[:, 0, 0])[None, :, None, None]
        return residual, residual + exchange(lower, middle, upper), total

    def forward(field):
        extended = with_halo(field.astype(jnp.bfloat16), (("rcv", 3),), rim_rows)
        return field + apply_forward(extended, stacked, columns, counts)

    lifted = adjoint(right_side)
    right_squares, lifted_squares = both_squares(right_side, lifted)
    beta_norm = jnp.sqrt(right_squares + EPSILON)
    alpha_norm = jnp.sqrt(lifted_squares / (beta_norm * beta_norm) + EPSILON)
    left_vector = right_side / beta_norm
    right_raw = lifted
    right_scale = beta_norm * alpha_norm
    right_vector = right_raw / right_scale
    search_direction = right_vector
    solution = jnp.zeros_like(right_side)
    phibar = beta_norm
    rhobar = alpha_norm
    for iteration in range(ITERS):
        last = iteration == ITERS - 1
        residual_left, lifted, left_squares = forward_adjoint(
            right_raw, right_scale, left_vector, alpha_norm
        )
        beta_norm = jnp.sqrt(left_squares + EPSILON)
        left_vector = residual_left / beta_norm
        residual_right = lifted / beta_norm - beta_norm * right_vector
        rho_value = jnp.sqrt(rhobar * rhobar + beta_norm * beta_norm)
        cosine = rhobar / rho_value
        sine_value = beta_norm / rho_value
        phi_value = cosine * phibar
        phibar = sine_value * phibar
        solution = solution + phi_value / rho_value * search_direction
        if last:
            break
        alpha_norm = jnp.sqrt(squares(residual_right) + EPSILON)
        right_raw = residual_right
        right_scale = alpha_norm
        right_vector = residual_right / alpha_norm
        theta_value = sine_value * alpha_norm
        rhobar = -cosine * alpha_norm
        search_direction = right_vector - theta_value / rho_value * search_direction
    return (solution, phibar * cosine * residual_right)


def solution(mesh):
    return jax.shard_map(
        body,
        mesh=mesh,
        in_specs=(
            P(("freq", "rcv"), None, None),
            P("freq", "rcv", None, None, None, None),
            P("freq", "rcv", None),
            P("freq", "rcv"),
        ),
        out_specs=(P(None, "freq", None, "rcv"), P(None, "freq", None, "rcv")),
        check_vma=False,
    )
```
